128 devices in a mesh: req: 8 (over y, core), ep: 16 (over x, z).
Axes of the slice: x: 4, y: 4, z: 4, core: 2. Of those that a mesh axis runs over, the one named last changes fastest.
Arguments:
- residual_in: bfloat16 [8, 2048, 2048], P('req', 'ep'), may hold values from -6 to 6
- queries: bfloat16 [8, 2048, 1024], P('req', 'ep'), may hold values from -44 to 44
- new_keys: bfloat16 [8, 2048, 1024], P('req', 'ep'), may hold values from -11 to 11
- new_values: bfloat16 [8, 2048, 1024], P('req', 'ep'), may hold values from -6 to 6
- cache_keys: bfloat16 [8, 4096, 1024], P('req', 'ep'), may hold values from -6 to 6
- cache_values: bfloat16 [8, 4096, 1024], P('req', 'ep'), may hold values from -6 to 6
- cached_len: int32 [8], P('req'), may hold values from 1024 to 4096, as said below
- rope_offset: int32 [8], P('req'), may hold values from 0 to 8191
- out_weight: bfloat16 [1024, 2048], replicated, may hold values from -1.5 to 1.5
- gate_weight: bfloat16 [128, 2048, 704], P(('req', 'ep')), may hold values from -0.125 to 0.125
- up_weight: bfloat16 [128, 2048, 704], P(('req', 'ep')), may hold values from -0.125 to 0.125
- down_weight: bfloat16 [128, 704, 2048], P(('req', 'ep')), may hold values from -0.15625 to 0.15625
- expert_ids: int32 [8, 2048, 6], P('req', 'ep'), may hold values from 0 to 63, all different within a row; in each aligned block of 128 rows (0 to 127, 128 to 255, ..., all dimensions but the last counted through in order) at most 13 rows name the same one
- gate_share: float32 [8, 2048, 6], P('req', 'ep'), may hold values from 0.1 to 0.5
Outputs:
- layer_out: bfloat16 [8, 2048, 2048], P('req', 'ep')
The draws below stay inside these ranges and needn't reach their ends.
Inputs may be any that keep to these rules, and one draw needn't show every extreme that they name: `cached_len`: some request uses all 4096 cached positions in every draw. `expert_ids`: each row names 6 different experts. In each aligned block of 128 rows (one request's new tokens on one index of ep) no expert is named by more than 13 rows, a bound that some block reaches.
All inputs are finite; a program needn't handle non-finite values.
Results may differ from the reference program's by a relative error of at most 0.0085.
Values may be sent and summed in bfloat16 or wider, within the bound.
No kernel may reach another device: no remote copies, remote signals or barrier semaphores. Data moves between devices by JAX's collectives and lax.ppermute only.
A program may use at most 128 MiB of HBM per device.

```python
import math
import jax
import jax.numpy as jnp
import numpy as np
from jax import lax

D = 2048
HEADS = 8
HD = 128
FF = 1408
TOPK = 6
PIECE = 128
CACHE_DEV = 256
FF_HALF = 704
EXPERTS = 64
NEWTOK = 2048
CACHE = 4096
REQS = 8
CAP = 13
N_EP = 16


def paired_rows(key):
    shape = (REQS, NEWTOK, HEADS * HD)
    base = jax.random.fold_in(key, 11)
    keys_raw = jnp.clip(jax.random.normal(jax.random.fold_in(base, 1), shape, jnp.float32), -5.0, 5.0)
    query_raw = jnp.clip(jax.random.normal(jax.random.fold_in(base, 2), shape, jnp.float32), -5.0, 5.0)
    return (query_raw, keys_raw)


def draw_queries(key, part):
    return paired_rows(key)[0].astype(jnp.bfloat16)


def draw_new_keys(key, part):
    return paired_rows(key)[1].astype(jnp.bfloat16)


def draw_cached_len(key, part):
    lengths = jax.random.randint(jax.random.fold_in(key, 21), (REQS,), CACHE // 4, CACHE + 1, jnp.int32)
    fullest = jax.random.randint(jax.random.fold_in(key, 22), (), 0, REQS, jnp.int32)
    return jnp.where(jnp.arange(REQS, dtype=jnp.int32) == fullest, CACHE, lengths).astype(jnp.int32)


def plant(values, key, low, top_value):
    place = [jax.random.randint(jax.random.fold_in(key, axis), (), 0, length) for axis, length in enumerate(values.shape)]
    longest = values.shape.index(max(values.shape))
    neighbour = place[:longest] + [(place[longest] + 1) % values.shape[longest]] + place[longest + 1:]
    return values.at[tuple(place)].set(low).at[tuple(neighbour)].set(top_value)


def level_of(stream_key, shape, cuts, smallest, high):
    factor_of, own = 1.0, jax.random.fold_in(stream_key, 6)
    for dim, shards_of in cuts:
        steps = jnp.exp(jax.random.uniform(jax.random.fold_in(own, dim), (shards_of,), jnp.float32, smallest / len(cuts), high / len(cuts)))
        factor_of = factor_of * jnp.repeat(steps, shape[dim] // shards_of).reshape([-1 if axis == dim else 1 for axis in range(len(shape))])
    return factor_of


def shared_out(own_key, own, number, rows, number_of, top, bound, slope):
    sequence = jax.random.permutation(own_key, number_of)
    packed, usual = shares(number_of, rows * top, bound, slope, True), shares(number_of, rows * top, bound, slope, False)
    places = jnp.arange(number_of)

    def named(tallies, offset_by):
        used = int((tallies > 0).sum())
        fixed = max(1, used // 4)
        moved = fixed + (places - fixed + offset_by * (used - fixed)) % max(1, number_of - fixed)
        return jnp.zeros((number_of,), jnp.int32).at[sequence[jnp.where(places < fixed, places, moved)]].set(jnp.asarray(tallies, jnp.int32))

    tallies = jnp.where(number % 4 == 0, named(packed, number // 4), named(usual, number - number // 4 - 1))
    mixed = jax.random.permutation(jax.random.fold_in(own, 3), number_of)
    donor, sink = mixed[0:number_of // 2 * 2:2], mixed[1:number_of // 2 * 2:2]
    margin = jnp.minimum(tallies[donor] - 1, bound - tallies[sink]) // 2
    margin = jnp.where((donor == sequence[0]) | (sink == sequence[0]) | (tallies[sink] == 0), 0, jnp.maximum(margin, 0))
    moved = jax.random.randint(jax.random.fold_in(own, 4), (number_of // 2,), 0, 1 << 20) % (margin + 1)
    tallies = tallies.at[donor].add(-moved).at[sink].add(moved)
    items = jnp.searchsorted(jnp.cumsum(tallies), jnp.arange(rows * top), side="right").astype(jnp.int32)
    listing = items.reshape(top, rows).T
    listing = listing[jax.random.permutation(jax.random.fold_in(own, 1), rows)]
    offset_by = jax.random.randint(jax.random.fold_in(own, 2), (rows, 1), 0, top)
    return jnp.take_along_axis(listing, (jnp.arange(top)[None, :] + offset_by) % top, axis=1)


def shares(number_of, total, bound, lean, full):
    loads = [(1 << 20) // math.isqrt(standing ** lean) + 1 for standing in range(1, number_of + 1)]
    largest = bound if full else min(bound, max(-(-total // number_of), total * loads[0] // sum(loads)))
    least = 1 if total - largest >= number_of - 1 else 0
    counts, spare = [largest] + [least] * (number_of - 1), total - largest - least * (number_of - 1)
    while spare > 0:
        movable = [i for i in range(1, number_of) if counts[i] < largest] or [i for i in range(1, number_of) if counts[i] < bound]
        pool, budget = sum([loads[i] for i in movable]), spare
        for i in movable:
            addition = min(bound - counts[i], max(1, budget * loads[i] // pool), spare)
            counts[i] = counts[i] + addition
            spare = spare - addition
    return np.array(counts)


def centred(key, shape, scale, reach, cuts=(), kind=jnp.bfloat16):
    result = scale * jax.random.normal(key, shape, jnp.float32)
    if cuts:
        result = result * level_of(key, shape, cuts, -0.22, 0.18)
    return jnp.clip(result, -reach, reach).astype(kind)


def setup_inputs(seed: int = 0) -> dict:
    keys = jax.random.split(jax.random.key(seed), 15)
    residual_in = centred(keys[0], (REQS, NEWTOK, D), 1.0, 6.0, ((0, 8), (1, 16)))
    queries = draw_queries(jax.random.fold_in(keys[14], 71), 0)
    new_keys = draw_new_keys(jax.random.fold_in(keys[14], 71), 0)
    new_values = centred(keys[3], (REQS, NEWTOK, HEADS * HD), 1.0, 6.0, ((0, 8), (1, 16)))
    cache_keys = centred(keys[4], (REQS, CACHE, HEADS * HD), 1.0, 6.0, ((0, 8), (1, 16)))
    cache_values = centred(keys[5], (REQS, CACHE, HEADS * HD), 1.0, 6.0, ((0, 8), (1, 16)))
    cached_len = draw_cached_len(jax.random.fold_in(keys[14], 71), 0)
    rope_offset = plant(jax.random.randint(keys[7], (REQS,), 0, 8192), jax.random.fold_in(keys[7], 1), 0, 8191).astype(jnp.int32)
    out_weight = centred(keys[8], (HEADS * HD, D), 16 ** -0.5, 1.5)
    gate_weight = centred(keys[9], (2 * EXPERTS, D, FF_HALF), D ** -0.5, 0.125, ((0, 128),))
    up_weight = centred(keys[10], (2 * EXPERTS, D, FF_HALF), D ** -0.5, 0.125, ((0, 128),))
    down_weight = centred(keys[11], (2 * EXPERTS, FF_HALF, D), FF ** -0.5, 0.15625, ((0, 128),))
    expert_ids_keys = jax.random.split(jax.random.fold_in(keys[12], 1), REQS * NEWTOK // PIECE)
    expert_ids_turns = jax.random.permutation(jax.random.fold_in(keys[12], 3), REQS * NEWTOK // PIECE)
    expert_ids = jax.vmap(lambda own, number: shared_out(jax.random.fold_in(keys[12], 2), own, number, PIECE, EXPERTS, TOPK, CAP, 2))(expert_ids_keys, expert_ids_turns).reshape((REQS, NEWTOK, TOPK))
    gate_share = jnp.clip(0.1 + 0.4 * jax.random.uniform(keys[13], (REQS, NEWTOK, TOPK), jnp.float32) ** level_of(keys[13], (REQS, NEWTOK, TOPK), ((0, 8), (1, 16)), -0.2, 0.2), 0.1, 0.5)
    return dict(residual_in=residual_in, queries=queries, new_keys=new_keys, new_values=new_values, cache_keys=cache_keys, cache_values=cache_values, cached_len=cached_len, rope_offset=rope_offset, out_weight=out_weight, gate_weight=gate_weight, up_weight=up_weight, down_weight=down_weight, expert_ids=expert_ids, gate_share=gate_share)


NEG_FILL = -1e+30
EPS = 1e-06
ROPE_BASE = 10000.0

def rotate_rows(values, positions, head_count):
    width_each = values.shape[-1] // head_count
    half_size = width_each // 2
    frequency = ROPE_BASE ** (-jnp.arange(half_size, dtype=jnp.int32).astype(jnp.float32) / half_size)
    angles = positions.astype(jnp.float32)[..., None] * frequency
    cosine = jnp.cos(angles)[..., None, :]
    sine = jnp.sin(angles)[..., None, :]
    shaped = values.astype(jnp.float32).reshape(values.shape[:-1] + (head_count, width_each))
    lower = shaped[..., :half_size]
    upper = shaped[..., half_size:]
    turned = jnp.concatenate([lower * cosine - upper * sine, lower * sine + upper * cosine], axis=-1)
    return turned.reshape(values.shape).astype(jnp.bfloat16)

def block_terms(query_all, cache_k, cache_v, keys_new, values_new, length, cache_start, new_start):
    query_count = query_all.shape[0]
    cache_rows = cache_k.shape[0]
    piece_rows = keys_new.shape[0]
    query_heads = query_all.astype(jnp.float32).reshape(query_count, HEADS, HD)
    key_heads = jnp.concatenate([cache_k, keys_new], 0).astype(jnp.float32).reshape(-1, HEADS, HD)
    value_heads = jnp.concatenate([cache_v, values_new], 0).astype(jnp.float32).reshape(-1, HEADS, HD)
    scores = jnp.einsum('qhd,khd->hqk', query_heads, key_heads, precision=lax.Precision.HIGHEST) * HD ** (-0.5)
    cache_valid = cache_start + jnp.arange(cache_rows, dtype=jnp.int32) < length
    new_valid = (new_start + jnp.arange(piece_rows, dtype=jnp.int32))[None, :] <= jnp.arange(query_count, dtype=jnp.int32)[:, None]
    valid = jnp.concatenate([jnp.broadcast_to(cache_valid[None, :], (query_count, cache_rows)), new_valid], 1)[None]
    masked = jnp.where(valid, scores, NEG_FILL)
    score_peak = lax.optimization_barrier(jnp.max(masked, -1))
    weights = jnp.where(valid, jnp.exp(masked - score_peak[..., None]), 0.0)
    weight_sum = lax.optimization_barrier(jnp.sum(weights, -1))
    rounded = lax.optimization_barrier(weights.astype(jnp.bfloat16)).astype(jnp.float32)
    mixed = jnp.einsum('hqk,khd->qhd', rounded, value_heads, precision=lax.Precision.HIGHEST)
    return (mixed, score_peak.T, weight_sum.T)

def expert_half(rows, gate_part, up_part, down_part):
    gate_val = jnp.dot(rows, gate_part, preferred_element_type=jnp.float32)
    up_val = jnp.dot(rows, up_part, preferred_element_type=jnp.float32)
    activation = (jax.nn.silu(gate_val) * up_val).astype(jnp.bfloat16)
    return jnp.dot(activation, down_part, preferred_element_type=jnp.float32).astype(jnp.bfloat16)

def reference(residual_in, queries, new_keys, new_values, cache_keys, cache_values, cached_len, rope_offset, out_weight, gate_weight, up_weight, down_weight, expert_ids, gate_share):

    def one_request(inputs):
        query_raw, key_raw, value_new, cache_k, cache_v, length, offset = inputs
        positions = offset + length + jnp.arange(NEWTOK, dtype=jnp.int32)
        query_turned = rotate_rows(query_raw, positions, HEADS)
        key_turned = rotate_rows(key_raw, positions, HEADS)

        def block(block_id):
            cache_start = (block_id * CACHE_DEV).astype(jnp.int32)
            new_start = (block_id * PIECE).astype(jnp.int32)
            cache_kb = lax.dynamic_slice_in_dim(cache_k, cache_start, CACHE_DEV, 0)
            cache_vb = lax.dynamic_slice_in_dim(cache_v, cache_start, CACHE_DEV, 0)
            key_b = lax.dynamic_slice_in_dim(key_turned, new_start, PIECE, 0)
            value_b = lax.dynamic_slice_in_dim(value_new, new_start, PIECE, 0)
            return block_terms(query_turned, cache_kb, cache_vb, key_b, value_b, length, cache_start, new_start)
        mixed, score_peak, weight_sum = lax.map(block, jnp.arange(N_EP, dtype=jnp.int32))
        peak = lax.optimization_barrier(jnp.max(score_peak, 0))
        factor = jnp.exp(score_peak - peak)
        summed = lax.optimization_barrier(jnp.sum(factor[..., None] * mixed, 0))
        denominator = lax.optimization_barrier(jnp.sum(factor * weight_sum, 0))
        return (summed / denominator[..., None]).reshape(NEWTOK, HEADS * HD).astype(jnp.bfloat16)
    attended = lax.map(one_request, (queries, new_keys, new_values, cache_keys, cache_values, cached_len, rope_offset))
    hidden = residual_in.astype(jnp.float32) + jnp.einsum('rtc,cd->rtd', attended.astype(jnp.float32), out_weight.astype(jnp.float32), precision=lax.Precision.HIGHEST)
    inv_root = lax.rsqrt(lax.optimization_barrier(jnp.mean(hidden * hidden, -1, keepdims=True)) + EPS)
    normed = (hidden * inv_root).astype(jnp.bfloat16).reshape(REQS * NEWTOK, D)
    flat_ids = expert_ids.reshape(REQS * NEWTOK, TOPK)
    flat_share = gate_share.reshape(REQS * NEWTOK, TOPK)
    limit = REQS * N_EP * CAP

    def step(running, expert):
        chosen = flat_ids == expert
        used = jnp.any(chosen, -1)
        weight = lax.optimization_barrier(jnp.sum(jnp.where(chosen, flat_share, 0.0), -1))
        count = jnp.sum(used.astype(jnp.int32))
        index = jnp.nonzero(used, size=limit, fill_value=0)[0].astype(jnp.int32)
        live = jnp.arange(limit, dtype=jnp.int32) < count
        rows = normed[index]
        first = expert_half(rows, gate_weight[2 * expert], up_weight[2 * expert], down_weight[2 * expert])
        second = expert_half(rows, gate_weight[2 * expert + 1], up_weight[2 * expert + 1], down_weight[2 * expert + 1])
        joined = lax.optimization_barrier((first.astype(jnp.float32) + second.astype(jnp.float32)).astype(jnp.bfloat16)).astype(jnp.float32)
        share = jnp.where(live, weight[index], 0.0)[:, None] * joined
        return (running.at[index].add(share), None)
    routed, _ = lax.scan(step, jnp.zeros((REQS * NEWTOK, D), jnp.float32), jnp.arange(EXPERTS, dtype=jnp.int32))
    return (hidden + routed.reshape(REQS, NEWTOK, D)).astype(jnp.bfloat16)
```

```python
import jax
import jax.numpy as jnp
from jax import lax
from jax.sharding import PartitionSpec as P

HEADS = 8
HD = 128


NEG_FILL = -1e30
EPS = 1e-06
ROPE_BASE = 10000.0


def rotate_rows(values, positions, head_count):
    width_each = values.shape[-1] // head_count
    half_size = width_each // 2
    frequency = ROPE_BASE ** (
        -jnp.arange(half_size, dtype=jnp.int32).astype(jnp.float32) / half_size
    )
    angles = positions.astype(jnp.float32)[..., None] * frequency
    cosine = jnp.cos(angles)[..., None, :]
    sine = jnp.sin(angles)[..., None, :]
    shaped = values.astype(jnp.float32).reshape(values.shape[:-1] + (head_count, width_each))
    lower = shaped[..., :half_size]
    upper = shaped[..., half_size:]
    turned = jnp.concatenate(
        [lower * cosine - upper * sine, lower * sine + upper * cosine], axis=-1
    )
    return turned.reshape(values.shape).astype(jnp.bfloat16)


def block_terms(query_all, cache_k, cache_v, keys_new, values_new, length, cache_start, new_start):
    query_count = query_all.shape[0]
    cache_rows = cache_k.shape[0]
    piece_rows = keys_new.shape[0]
    query_heads = query_all.reshape(query_count, HEADS, HD)
    key_heads = jnp.concatenate([cache_k, keys_new], 0).reshape(-1, HEADS, HD)
    value_heads = jnp.concatenate([cache_v, values_new], 0).reshape(-1, HEADS, HD)
    scores = jnp.einsum(
        "qhd,khd->hqk", query_heads, key_heads, preferred_element_type=jnp.float32
    ) * HD ** (-0.5)
    cache_valid = cache_start + jnp.arange(cache_rows, dtype=jnp.int32) < length
    new_valid = (new_start + jnp.arange(piece_rows, dtype=jnp.int32))[None, :] <= jnp.arange(
        query_count, dtype=jnp.int32
    )[:, None]
    valid = jnp.concatenate(
        [jnp.broadcast_to(cache_valid[None, :], (query_count, cache_rows)), new_valid], 1
    )[None]
    masked = jnp.where(valid, scores, NEG_FILL)
    score_peak = jnp.max(masked, -1)
    weights = jnp.where(valid, jnp.exp(masked - score_peak[..., None]), 0.0)
    weight_sum = jnp.sum(weights, -1)
    mixed = jnp.einsum(
        "hqk,khd->qhd",
        weights.astype(jnp.bfloat16),
        value_heads,
        preferred_element_type=jnp.float32,
    )
    return (mixed, score_peak.T, weight_sum.T)


def expert_half(rows, gate_part, up_part, down_part):
    gate_val = jnp.dot(rows, gate_part, preferred_element_type=jnp.float32)
    up_val = jnp.dot(rows, up_part, preferred_element_type=jnp.float32)
    activation = (jax.nn.silu(gate_val) * up_val).astype(jnp.bfloat16)
    return jnp.dot(activation, down_part, preferred_element_type=jnp.float32).astype(jnp.bfloat16)


def deliver(rows):
    return lax.all_to_all(rows, ("req", "ep"), split_axis=0, concat_axis=0, tiled=True)


def collect(rows):
    return lax.all_to_all(rows, ("req", "ep"), split_axis=0, concat_axis=0, tiled=True)


def head_attention(recv, length, half_index, piece_rows, cache_rows):
    pieces = recv.shape[0]
    block_rows = cache_rows + piece_rows
    query_rows = recv.shape[1] - 2 * block_rows
    keys = recv[:, :block_rows]
    values = recv[:, block_rows : 2 * block_rows]
    query = recv[:, 2 * block_rows :].reshape(pieces * query_rows, HD)
    scores = jnp.einsum(
        "qd,bkd->bqk", query, keys, preferred_element_type=jnp.float32
    ) * HD ** (-0.5)
    block = jnp.arange(pieces, dtype=jnp.int32)[:, None, None]
    key_pos = jnp.arange(block_rows, dtype=jnp.int32)[None, None, :]
    query_row = jnp.arange(pieces * query_rows, dtype=jnp.int32)
    query_index = (
        (query_row // query_rows) * piece_rows + half_index * query_rows + query_row % query_rows
    )[None, :, None]
    cache_valid = block * cache_rows + key_pos < length
    new_valid = block * piece_rows + (key_pos - cache_rows) <= query_index
    valid = jnp.where(key_pos < cache_rows, cache_valid, new_valid)
    masked = jnp.where(valid, scores, NEG_FILL)
    score_peak = jnp.max(masked, -1)
    weights = jnp.where(valid, jnp.exp(masked - score_peak[..., None]), 0.0)
    weight_sum = jnp.sum(weights, -1)
    mixed = jnp.einsum(
        "bqk,bkd->bqd",
        weights.astype(jnp.bfloat16),
        values,
        preferred_element_type=jnp.float32,
    )
    peak = jnp.max(score_peak, 0, keepdims=True)
    factor = jnp.exp(score_peak - peak)
    summed = jnp.sum(factor[..., None] * mixed, 0)
    denominator = jnp.sum(factor * weight_sum, 0)
    return (summed / denominator[:, None]).astype(jnp.bfloat16)


def shards(
    residual_in,
    queries,
    new_keys,
    new_values,
    cache_keys,
    cache_values,
    cached_len,
    rope_offset,
    out_weight,
    gate_weight,
    up_weight,
    down_weight,
    expert_ids,
    gate_share,
):
    req_count = lax.axis_size("req")
    piece_count = lax.axis_size("ep")
    devices = req_count * piece_count
    experts = devices // 2
    groups, piece_rows, _ = queries.shape
    cache_rows = cache_keys.shape[1]
    top_count = expert_ids.shape[2]
    capacity = (piece_rows * top_count + experts - 1) // experts + 1
    piece_index = lax.axis_index("ep")
    new_index = piece_index * piece_rows + jnp.arange(piece_rows, dtype=jnp.int32)
    positions = rope_offset[:, None] + cached_len[:, None] + new_index[None, :]
    query_turned = rotate_rows(queries, positions, HEADS)[0]
    key_turned = rotate_rows(new_keys, positions, HEADS)[0]
    splits = piece_count // HEADS
    query_rows = piece_rows // splits

    def by_head(rows):
        return jnp.transpose(rows.reshape(rows.shape[0], HEADS, HD), (1, 0, 2))

    kv = jnp.concatenate(
        [
            by_head(cache_keys[0]),
            by_head(key_turned),
            by_head(cache_values[0]),
            by_head(new_values[0]),
        ],
        1,
    )
    kv = jnp.broadcast_to(kv[:, None], (HEADS, splits) + kv.shape[1:]).reshape(
        (piece_count,) + kv.shape[1:]
    )
    q_parts = jnp.transpose(
        query_turned.reshape(splits, query_rows, HEADS, HD), (2, 0, 1, 3)
    ).reshape(piece_count, query_rows, HD)
    sending = jnp.concatenate([kv, q_parts], 1)
    arrived = lax.all_to_all(sending, "ep", split_axis=0, concat_axis=0, tiled=True)
    head_out = head_attention(
        arrived, cached_len[0], piece_index % splits, piece_rows, cache_rows
    ).reshape(piece_count, query_rows, HD)
    returned = lax.all_to_all(head_out, "ep", split_axis=0, concat_axis=0, tiled=True)
    attended = jnp.transpose(
        returned.reshape(HEADS, splits, query_rows, HD), (1, 2, 0, 3)
    ).reshape(groups, piece_rows, HEADS * HD)
    hidden = residual_in.astype(jnp.float32) + jnp.einsum(
        "gtc,cd->gtd", attended, out_weight, preferred_element_type=jnp.float32
    )
    inv_root = lax.rsqrt(jnp.mean(hidden * hidden, -1, keepdims=True) + EPS)
    normed = (hidden * inv_root).astype(jnp.bfloat16)
    width = normed.shape[-1]
    matches = (expert_ids[..., None] == jnp.arange(experts, dtype=jnp.int32)).astype(jnp.int32)
    flat_matches = matches.reshape(groups, piece_rows * top_count, experts)
    earlier = jnp.cumsum(flat_matches, 1) - flat_matches
    slot_index = jnp.sum(earlier * flat_matches, -1).reshape(groups, piece_rows, top_count)
    group_index = jnp.arange(groups, dtype=jnp.int32)[:, None, None]
    target_row = ((expert_ids * groups + group_index) * capacity + slot_index).reshape(-1)
    row_copies = jnp.broadcast_to(
        normed[:, :, None, :], (groups, piece_rows, top_count, width)
    ).reshape(-1, width)
    outgoing = (
        jnp.zeros((experts * groups * capacity, width), jnp.bfloat16).at[target_row].set(row_copies)
    )
    sending = jnp.broadcast_to(
        outgoing.reshape(experts, 1, groups * capacity, width),
        (experts, 2, groups * capacity, width),
    ).reshape(devices, groups, capacity, width)
    arrived = deliver(sending)
    produced = expert_half(
        arrived.reshape(-1, width), gate_weight[0], up_weight[0], down_weight[0]
    ).reshape(devices, groups, capacity, width)
    came_back = collect(produced).reshape(experts, 2, groups * capacity, width)
    joined = (came_back[:, 0].astype(jnp.float32) + came_back[:, 1].astype(jnp.float32)).astype(
        jnp.bfloat16
    )
    results = lax.optimization_barrier(joined).reshape(experts * groups * capacity, width)
    picked = results[target_row].reshape(groups, piece_rows, top_count, width).astype(jnp.float32)
    routed = jnp.sum(gate_share[..., None] * picked, 2)
    return (hidden + routed).astype(jnp.bfloat16)


def solution(mesh):
    in_specs = (
        P("req", "ep", None),
        P("req", "ep", None),
        P("req", "ep", None),
        P("req", "ep", None),
        P("req", "ep", None),
        P("req", "ep", None),
        P("req"),
        P("req"),
        P(),
        P(("req", "ep"), None, None),
        P(("req", "ep"), None, None),
        P(("req", "ep"), None, None),
        P("req", "ep", None),
        P("req", "ep", None),
    )
    out_specs = P("req", "ep", None)
    return jax.shard_map(shards, mesh=mesh, in_specs=in_specs, out_specs=out_specs, check_vma=False)
```

```python
import jax
import jax.numpy as jnp
from jax import lax
from jax.sharding import PartitionSpec as P

HEADS = 8
HD = 128


NEG_FILL = -1e30
EPS = 1e-06
ROPE_BASE = 10000.0


def rotate_rows(values, positions, head_count):
    width_each = values.shape[-1] // head_count
    half_size = width_each // 2
    frequency = ROPE_BASE ** (
        -jnp.arange(half_size, dtype=jnp.int32).astype(jnp.float32) / half_size
    )
    angles = positions.astype(jnp.float32)[..., None] * frequency
    cosine = jnp.cos(angles)[..., None, :]
    sine = jnp.sin(angles)[..., None, :]
    shaped = values.astype(jnp.float32).reshape(values.shape[:-1] + (head_count, width_each))
    lower = shaped[..., :half_size]
    upper = shaped[..., half_size:]
    turned = jnp.concatenate(
        [lower * cosine - upper * sine, lower * sine + upper * cosine], axis=-1
    )
    return turned.reshape(values.shape).astype(jnp.bfloat16)


def block_terms(query_all, cache_k, cache_v, keys_new, values_new, length, cache_start, new_start):
    query_count = query_all.shape[0]
    cache_rows = cache_k.shape[0]
    piece_rows = keys_new.shape[0]
    query_heads = query_all.reshape(query_count, HEADS, HD)
    key_heads = jnp.concatenate([cache_k, keys_new], 0).reshape(-1, HEADS, HD)
    value_heads = jnp.concatenate([cache_v, values_new], 0).reshape(-1, HEADS, HD)
    scores = jnp.einsum(
        "qhd,khd->hqk", query_heads, key_heads, preferred_element_type=jnp.float32
    ) * HD ** (-0.5)
    cache_valid = cache_start + jnp.arange(cache_rows, dtype=jnp.int32) < length
    new_valid = (new_start + jnp.arange(piece_rows, dtype=jnp.int32))[None, :] <= jnp.arange(
        query_count, dtype=jnp.int32
    )[:, None]
    valid = jnp.concatenate(
        [jnp.broadcast_to(cache_valid[None, :], (query_count, cache_rows)), new_valid], 1
    )[None]
    masked = jnp.where(valid, scores, NEG_FILL)
    score_peak = jnp.max(masked, -1)
    weights = jnp.where(valid, jnp.exp(masked - score_peak[..., None]), 0.0)
    weight_sum = jnp.sum(weights, -1)
    mixed = jnp.einsum(
        "hqk,khd->qhd",
        weights.astype(jnp.bfloat16),
        value_heads,
        preferred_element_type=jnp.float32,
    )
    return (mixed, score_peak.T, weight_sum.T)


def expert_half(rows, gate_part, up_part, down_part):
    gate_val = jnp.dot(rows, gate_part, preferred_element_type=jnp.float32)
    up_val = jnp.dot(rows, up_part, preferred_element_type=jnp.float32)
    activation = (jax.nn.silu(gate_val) * up_val).astype(jnp.bfloat16)
    return jnp.dot(activation, down_part, preferred_element_type=jnp.float32).astype(jnp.bfloat16)


def deliver(rows):
    return lax.all_to_all(rows, ("req", "ep"), split_axis=0, concat_axis=0, tiled=True)


def collect(rows):
    return lax.all_to_all(rows, ("req", "ep"), split_axis=0, concat_axis=0, tiled=True)


def head_attention(recv, length, half_index, piece_rows, cache_rows):
    pieces = recv.shape[0]
    block_rows = cache_rows + piece_rows
    query_rows = recv.shape[1] - 2 * block_rows
    keys = recv[:, :block_rows]
    values = recv[:, block_rows : 2 * block_rows]
    query = recv[:, 2 * block_rows :].reshape(pieces * query_rows, HD)
    scores = jnp.einsum(
        "qd,bkd->bqk", query, keys, preferred_element_type=jnp.float32
    ) * HD ** (-0.5)
    block = jnp.arange(pieces, dtype=jnp.int32)[:, None, None]
    key_pos = jnp.arange(block_rows, dtype=jnp.int32)[None, None, :]
    query_row = jnp.arange(pieces * query_rows, dtype=jnp.int32)
    query_index = (
        (query_row // query_rows) * piece_rows + half_index * query_rows + query_row % query_rows
    )[None, :, None]
    cache_valid = block * cache_rows + key_pos < length
    new_valid = block * piece_rows + (key_pos - cache_rows) <= query_index
    valid = jnp.where(key_pos < cache_rows, cache_valid, new_valid)
    masked = jnp.where(valid, scores, NEG_FILL)
    score_peak = jnp.max(masked, -1)
    weights = jnp.where(valid, jnp.exp(masked - score_peak[..., None]), 0.0)
    weight_sum = jnp.sum(weights, -1)
    mixed = jnp.einsum(
        "bqk,bkd->bqd",
        weights.astype(jnp.bfloat16),
        values,
        preferred_element_type=jnp.float32,
    )
    peak = jnp.max(score_peak, 0, keepdims=True)
    factor = jnp.exp(score_peak - peak)
    summed = jnp.sum(factor[..., None] * mixed, 0)
    denominator = jnp.sum(factor * weight_sum, 0)
    return (summed / denominator[:, None]).astype(jnp.bfloat16)


def shards(
    residual_in,
    queries,
    new_keys,
    new_values,
    cache_keys,
    cache_values,
    cached_len,
    rope_offset,
    out_weight,
    gate_weight,
    up_weight,
    down_weight,
    expert_ids,
    gate_share,
):
    req_count = lax.axis_size("req")
    piece_count = lax.axis_size("ep")
    devices = req_count * piece_count
    experts = devices // 2
    groups, piece_rows, _ = queries.shape
    cache_rows = cache_keys.shape[1]
    top_count = expert_ids.shape[2]
    capacity = (piece_rows * top_count + experts - 1) // experts + 1
    piece_index = lax.axis_index("ep")
    new_index = piece_index * piece_rows + jnp.arange(piece_rows, dtype=jnp.int32)
    positions = rope_offset[:, None] + cached_len[:, None] + new_index[None, :]
    query_turned = rotate_rows(queries, positions, HEADS)[0]
    key_turned = rotate_rows(new_keys, positions, HEADS)[0]
    splits = piece_count // HEADS
    query_rows = piece_rows // splits

    def by_head(rows):
        return jnp.transpose(rows.reshape(rows.shape[0], HEADS, HD), (1, 0, 2))

    kv = jnp.concatenate(
        [
            by_head(cache_keys[0]),
            by_head(key_turned),
            by_head(cache_values[0]),
            by_head(new_values[0]),
        ],
        1,
    )
    kv = jnp.broadcast_to(kv[:, None], (HEADS, splits) + kv.shape[1:]).reshape(
        (piece_count,) + kv.shape[1:]
    )
    q_parts = jnp.transpose(
        query_turned.reshape(splits, query_rows, HEADS, HD), (2, 0, 1, 3)
    ).reshape(piece_count, query_rows, HD)
    sending = jnp.concatenate([kv, q_parts], 1)
    arrived = lax.all_to_all(sending, "ep", split_axis=0, concat_axis=0, tiled=True)
    head_out = head_attention(
        arrived, cached_len[0], piece_index % splits, piece_rows, cache_rows
    ).reshape(piece_count, query_rows, HD)
    returned = lax.all_to_all(head_out, "ep", split_axis=0, concat_axis=0, tiled=True)
    attended = jnp.transpose(
        returned.reshape(HEADS, splits, query_rows, HD), (1, 2, 0, 3)
    ).reshape(groups, piece_rows, HEADS * HD)
    hidden = residual_in.astype(jnp.float32) + jnp.einsum(
        "gtc,cd->gtd", attended, out_weight, preferred_element_type=jnp.float32
    )
    inv_root = lax.rsqrt(jnp.mean(hidden * hidden, -1, keepdims=True) + EPS)
    normed = (hidden * inv_root).astype(jnp.bfloat16)
    width = normed.shape[-1]
    rows = normed[0]
    slots = -(-capacity // 16) * 16
    ids = expert_ids[0]
    matches = (ids[..., None] == jnp.arange(experts, dtype=jnp.int32)).astype(jnp.int32)
    flat_matches = matches.reshape(piece_rows * top_count, experts)
    earlier = jnp.cumsum(flat_matches, 0) - flat_matches
    slot_index = jnp.sum(earlier * flat_matches, -1).reshape(piece_rows, top_count)
    target = ids * slots + slot_index
    chosen = target[..., None] == jnp.arange(experts * slots, dtype=jnp.int32)
    picked = jnp.any(chosen, 1).reshape(piece_rows, experts, 1, slots)
    weight = jnp.sum(jnp.where(chosen, gate_share[0][..., None], 0.0), 1)
    select = jnp.broadcast_to(picked, (piece_rows, experts, 2, slots)).astype(jnp.bfloat16)
    sending = jnp.einsum(
        "teks,tw->eksw", select, rows, preferred_element_type=jnp.float32
    ).astype(jnp.bfloat16).reshape(devices, slots, width)
    arrived = deliver(sending)
    produced = expert_half(
        arrived.reshape(-1, width), gate_weight[0], up_weight[0], down_weight[0]
    ).reshape(devices, slots, width)
    came_back = collect(produced).reshape(experts, 2, slots, width)
    joined = (came_back[:, 0].astype(jnp.float32) + came_back[:, 1].astype(jnp.float32)).astype(
        jnp.bfloat16
    )
    routed = jnp.dot(
        weight,
        joined.reshape(experts * slots, width).astype(jnp.float32),
        precision=lax.Precision.HIGHEST,
    )
    return (hidden + routed[None]).astype(jnp.bfloat16)


def solution(mesh):
    in_specs = (
        P("req", "ep", None),
        P("req", "ep", None),
        P("req", "ep", None),
        P("req", "ep", None),
        P("req", "ep", None),
        P("req", "ep", None),
        P("req"),
        P("req"),
        P(),
        P(("req", "ep"), None, None),
        P(("req", "ep"), None, None),
        P(("req", "ep"), None, None),
        P("req", "ep", None),
        P("req", "ep", None),
    )
    out_specs = P("req", "ep", None)
    return jax.shard_map(shards, mesh=mesh, in_specs=in_specs, out_specs=out_specs, check_vma=False)
```

```python
import jax
import jax.numpy as jnp
from jax import lax
from jax.sharding import PartitionSpec as P

HEADS = 8
HD = 128


NEG_FILL = -1e30
EPS = 1e-06
ROPE_BASE = 10000.0


def rotate_rows(values, positions, head_count):
    width_each = values.shape[-1] // head_count
    half_size = width_each // 2
    frequency = ROPE_BASE ** (
        -jnp.arange(half_size, dtype=jnp.int32).astype(jnp.float32) / half_size
    )
    angles = positions.astype(jnp.float32)[..., None] * frequency
    cosine = jnp.cos(angles)[..., None, :]
    sine = jnp.sin(angles)[..., None, :]
    shaped = values.astype(jnp.float32).reshape(values.shape[:-1] + (head_count, width_each))
    lower = shaped[..., :half_size]
    upper = shaped[..., half_size:]
    turned = jnp.concatenate(
        [lower * cosine - upper * sine, lower * sine + upper * cosine], axis=-1
    )
    return turned.reshape(values.shape).astype(jnp.bfloat16)


def block_terms(query_all, cache_k, cache_v, keys_new, values_new, length, cache_start, new_start):
    query_count = query_all.shape[0]
    cache_rows = cache_k.shape[0]
    piece_rows = keys_new.shape[0]
    query_heads = query_all.reshape(query_count, HEADS, HD)
    key_heads = jnp.concatenate([cache_k, keys_new], 0).reshape(-1, HEADS, HD)
    value_heads = jnp.concatenate([cache_v, values_new], 0).reshape(-1, HEADS, HD)
    scores = jnp.einsum(
        "qhd,khd->hqk", query_heads, key_heads, preferred_element_type=jnp.float32
    ) * HD ** (-0.5)
    cache_valid = cache_start + jnp.arange(cache_rows, dtype=jnp.int32) < length
    new_valid = (new_start + jnp.arange(piece_rows, dtype=jnp.int32))[None, :] <= jnp.arange(
        query_count, dtype=jnp.int32
    )[:, None]
    valid = jnp.concatenate(
        [jnp.broadcast_to(cache_valid[None, :], (query_count, cache_rows)), new_valid], 1
    )[None]
    masked = jnp.where(valid, scores, NEG_FILL)
    score_peak = jnp.max(masked, -1)
    weights = jnp.where(valid, jnp.exp(masked - score_peak[..., None]), 0.0)
    weight_sum = jnp.sum(weights, -1)
    mixed = jnp.einsum(
        "hqk,khd->qhd",
        weights.astype(jnp.bfloat16),
        value_heads,
        preferred_element_type=jnp.float32,
    )
    return (mixed, score_peak.T, weight_sum.T)


def expert_half(rows, gate_part, up_part, down_part):
    gate_val = jnp.dot(rows, gate_part, preferred_element_type=jnp.float32)
    up_val = jnp.dot(rows, up_part, preferred_element_type=jnp.float32)
    activation = (jax.nn.silu(gate_val) * up_val).astype(jnp.bfloat16)
    return jnp.dot(activation, down_part, preferred_element_type=jnp.float32).astype(jnp.bfloat16)


def deliver(rows):
    return lax.all_to_all(rows, ("req", "ep"), split_axis=0, concat_axis=0, tiled=True)


def collect(rows):
    return lax.all_to_all(rows, ("req", "ep"), split_axis=0, concat_axis=0, tiled=True)


def head_attention(keys, values, query, length, half_index, piece_rows, cache_rows):
    pieces, query_rows = query.shape[0], query.shape[1]
    block_rows = cache_rows + piece_rows
    query = query.reshape(pieces * query_rows, HD)
    scores = jnp.einsum(
        "qd,bkd->bqk", query, keys, preferred_element_type=jnp.float32
    ) * HD ** (-0.5)
    block = jnp.arange(pieces, dtype=jnp.int32)[:, None, None]
    key_pos = jnp.arange(block_rows, dtype=jnp.int32)[None, None, :]
    query_row = jnp.arange(pieces * query_rows, dtype=jnp.int32)
    query_index = (
        (query_row // query_rows) * piece_rows + half_index * query_rows + query_row % query_rows
    )[None, :, None]
    cache_valid = block * cache_rows + key_pos < length
    new_valid = block * piece_rows + (key_pos - cache_rows) <= query_index
    valid = jnp.where(key_pos < cache_rows, cache_valid, new_valid)
    masked = jnp.where(valid, scores, NEG_FILL)
    score_peak = jnp.max(masked, -1)
    weights = jnp.where(valid, jnp.exp(masked - score_peak[..., None]), 0.0)
    weight_sum = jnp.sum(weights, -1)
    mixed = jnp.einsum(
        "bqk,bkd->bqd",
        weights.astype(jnp.bfloat16),
        values,
        preferred_element_type=jnp.float32,
    )
    peak = jnp.max(score_peak, 0, keepdims=True)
    factor = jnp.exp(score_peak - peak)
    summed = jnp.sum(factor[..., None] * mixed, 0)
    denominator = jnp.sum(factor * weight_sum, 0)
    return (summed / denominator[:, None]).astype(jnp.bfloat16)


def shards(
    residual_in,
    queries,
    new_keys,
    new_values,
    cache_keys,
    cache_values,
    cached_len,
    rope_offset,
    out_weight,
    gate_weight,
    up_weight,
    down_weight,
    expert_ids,
    gate_share,
):
    req_count = lax.axis_size("req")
    piece_count = lax.axis_size("ep")
    devices = req_count * piece_count
    experts = devices // 2
    groups, piece_rows, _ = queries.shape
    cache_rows = cache_keys.shape[1]
    top_count = expert_ids.shape[2]
    capacity = (piece_rows * top_count + experts - 1) // experts + 1
    piece_index = lax.axis_index("ep")
    new_index = piece_index * piece_rows + jnp.arange(piece_rows, dtype=jnp.int32)
    positions = rope_offset[:, None] + cached_len[:, None] + new_index[None, :]
    query_turned = rotate_rows(queries, positions, HEADS)[0]
    key_turned = rotate_rows(new_keys, positions, HEADS)[0]
    splits = piece_count // HEADS
    query_rows = piece_rows // splits

    def by_head(rows):
        return jnp.transpose(rows.reshape(rows.shape[0], HEADS, HD), (1, 0, 2))

    def both_halves(parts):
        joined = jnp.concatenate(parts, 1)
        return jnp.broadcast_to(joined[:, None], (HEADS, splits) + joined.shape[1:]).reshape(
            (piece_count,) + joined.shape[1:]
        )

    cache_sent = both_halves([by_head(cache_keys[0]), by_head(cache_values[0])])
    cache_got = lax.all_to_all(cache_sent, "ep", split_axis=0, concat_axis=0, tiled=True)
    q_parts = jnp.transpose(
        query_turned.reshape(splits, query_rows, HEADS, HD), (2, 0, 1, 3)
    ).reshape(piece_count, query_rows, HD)
    new_sent = jnp.concatenate(
        [both_halves([by_head(key_turned), by_head(new_values[0])]), q_parts], 1
    )
    new_sent, cache_got = lax.optimization_barrier((new_sent, cache_got))
    new_got = lax.all_to_all(new_sent, "ep", split_axis=0, concat_axis=0, tiled=True)
    keys = jnp.concatenate([cache_got[:, :cache_rows], new_got[:, :piece_rows]], 1)
    values = jnp.concatenate(
        [cache_got[:, cache_rows:], new_got[:, piece_rows : 2 * piece_rows]], 1
    )
    head_out = head_attention(
        keys,
        values,
        new_got[:, 2 * piece_rows :],
        cached_len[0],
        piece_index % splits,
        piece_rows,
        cache_rows,
    ).reshape(piece_count, query_rows, HD)
    returned = lax.all_to_all(head_out, "ep", split_axis=0, concat_axis=0, tiled=True)
    attended = jnp.transpose(
        returned.reshape(HEADS, splits, query_rows, HD), (1, 2, 0, 3)
    ).reshape(groups, piece_rows, HEADS * HD)
    hidden = residual_in.astype(jnp.float32) + jnp.einsum(
        "gtc,cd->gtd", attended, out_weight, preferred_element_type=jnp.float32
    )
    inv_root = lax.rsqrt(jnp.mean(hidden * hidden, -1, keepdims=True) + EPS)
    normed = (hidden * inv_root).astype(jnp.bfloat16)
    width = normed.shape[-1]
    rows = normed[0]
    slots = -(-capacity // 16) * 16
    ids = expert_ids[0]
    matches = (ids[..., None] == jnp.arange(experts, dtype=jnp.int32)).astype(jnp.int32)
    flat_matches = matches.reshape(piece_rows * top_count, experts)
    earlier = jnp.cumsum(flat_matches, 0) - flat_matches
    slot_index = jnp.sum(earlier * flat_matches, -1).reshape(piece_rows, top_count)
    target = ids * slots + slot_index
    chosen = target[..., None] == jnp.arange(experts * slots, dtype=jnp.int32)
    picked = jnp.any(chosen, 1).reshape(piece_rows, experts, 1, slots)
    weight = jnp.sum(jnp.where(chosen, gate_share[0][..., None], 0.0), 1)
    select = jnp.broadcast_to(picked, (piece_rows, experts, 2, slots)).astype(jnp.bfloat16)
    weight = weight.reshape(piece_rows, experts, slots)
    routed = jnp.zeros((piece_rows, width), jnp.float32)
    chunk = 8
    for low in range(0, slots, chunk):
        sending = jnp.einsum(
            "teks,tw->eksw",
            select[..., low : low + chunk],
            rows,
            preferred_element_type=jnp.float32,
        ).astype(jnp.bfloat16).reshape(devices, chunk, width)
        arrived = deliver(sending)
        produced = expert_half(
            arrived.reshape(-1, width), gate_weight[0], up_weight[0], down_weight[0]
        ).reshape(devices, chunk, width)
        came_back = collect(produced).reshape(experts, 2, chunk, width)
        joined = (
            came_back[:, 0].astype(jnp.float32) + came_back[:, 1].astype(jnp.float32)
        ).astype(jnp.bfloat16)
        routed = routed + jnp.dot(
            weight[..., low : low + chunk].reshape(piece_rows, experts * chunk),
            joined.reshape(experts * chunk, width).astype(jnp.float32),
            precision=lax.Precision.HIGHEST,
        )
    return (hidden + routed[None]).astype(jnp.bfloat16)


def solution(mesh):
    in_specs = (
        P("req", "ep", None),
        P("req", "ep", None),
        P("req", "ep", None),
        P("req", "ep", None),
        P("req", "ep", None),
        P("req", "ep", None),
        P("req"),
        P("req"),
        P(),
        P(("req", "ep"), None, None),
        P(("req", "ep"), None, None),
        P(("req", "ep"), None, None),
        P("req", "ep", None),
        P("req", "ep", None),
    )
    out_specs = P("req", "ep", None)
    return jax.shard_map(shards, mesh=mesh, in_specs=in_specs, out_specs=out_specs, check_vma=False)
```

```python
import jax
import jax.numpy as jnp
from jax import lax
from jax.sharding import PartitionSpec as P

HEADS = 8
HD = 128


NEG_FILL = -1e30
EPS = 1e-06
ROPE_BASE = 10000.0


def rotate_rows(values, positions, head_count):
    width_each = values.shape[-1] // head_count
    half_size = width_each // 2
    frequency = ROPE_BASE ** (
        -jnp.arange(half_size, dtype=jnp.int32).astype(jnp.float32) / half_size
    )
    angles = positions.astype(jnp.float32)[..., None] * frequency
    cosine = jnp.cos(angles)[..., None, :]
    sine = jnp.sin(angles)[..., None, :]
    shaped = values.astype(jnp.float32).reshape(values.shape[:-1] + (head_count, width_each))
    lower = shaped[..., :half_size]
    upper = shaped[..., half_size:]
    turned = jnp.concatenate(
        [lower * cosine - upper * sine, lower * sine + upper * cosine], axis=-1
    )
    return turned.reshape(values.shape).astype(jnp.bfloat16)


def block_terms(query_all, cache_k, cache_v, keys_new, values_new, length, cache_start, new_start):
    query_count = query_all.shape[0]
    cache_rows = cache_k.shape[0]
    piece_rows = keys_new.shape[0]
    query_heads = query_all.reshape(query_count, HEADS, HD)
    key_heads = jnp.concatenate([cache_k, keys_new], 0).reshape(-1, HEADS, HD)
    value_heads = jnp.concatenate([cache_v, values_new], 0).reshape(-1, HEADS, HD)
    scores = jnp.einsum(
        "qhd,khd->hqk", query_heads, key_heads, preferred_element_type=jnp.float32
    ) * HD ** (-0.5)
    cache_valid = cache_start + jnp.arange(cache_rows, dtype=jnp.int32) < length
    new_valid = (new_start + jnp.arange(piece_rows, dtype=jnp.int32))[None, :] <= jnp.arange(
        query_count, dtype=jnp.int32
    )[:, None]
    valid = jnp.concatenate(
        [jnp.broadcast_to(cache_valid[None, :], (query_count, cache_rows)), new_valid], 1
    )[None]
    masked = jnp.where(valid, scores, NEG_FILL)
    score_peak = jnp.max(masked, -1)
    weights = jnp.where(valid, jnp.exp(masked - score_peak[..., None]), 0.0)
    weight_sum = jnp.sum(weights, -1)
    mixed = jnp.einsum(
        "hqk,khd->qhd",
        weights.astype(jnp.bfloat16),
        value_heads,
        preferred_element_type=jnp.float32,
    )
    return (mixed, score_peak.T, weight_sum.T)


def expert_half(rows, gate_part, up_part, down_part):
    gate_val = jnp.dot(rows, gate_part, preferred_element_type=jnp.float32)
    up_val = jnp.dot(rows, up_part, preferred_element_type=jnp.float32)
    activation = (jax.nn.silu(gate_val) * up_val).astype(jnp.bfloat16)
    return jnp.dot(activation, down_part, preferred_element_type=jnp.float32).astype(jnp.bfloat16)


def deliver(rows):
    return lax.all_to_all(rows, ("req", "ep"), split_axis=0, concat_axis=0, tiled=True)


def collect(rows):
    return lax.all_to_all(rows, ("req", "ep"), split_axis=0, concat_axis=0, tiled=True)


def head_attention(keys, values, query, length, half_index, piece_rows, cache_rows):
    pieces, query_rows = query.shape[0], query.shape[1]
    block_rows = cache_rows + piece_rows
    query = query.reshape(pieces * query_rows, HD)
    scores = jnp.einsum(
        "qd,bkd->bqk", query, keys, preferred_element_type=jnp.float32
    ) * HD ** (-0.5)
    block = jnp.arange(pieces, dtype=jnp.int32)[:, None, None]
    key_pos = jnp.arange(block_rows, dtype=jnp.int32)[None, None, :]
    query_row = jnp.arange(pieces * query_rows, dtype=jnp.int32)
    query_index = (
        (query_row // query_rows) * piece_rows + half_index * query_rows + query_row % query_rows
    )[None, :, None]
    cache_valid = block * cache_rows + key_pos < length
    new_valid = block * piece_rows + (key_pos - cache_rows) <= query_index
    valid = jnp.where(key_pos < cache_rows, cache_valid, new_valid)
    masked = jnp.where(valid, scores, NEG_FILL)
    score_peak = jnp.max(masked, -1)
    weights = jnp.where(valid, jnp.exp(masked - score_peak[..., None]), 0.0)
    weight_sum = jnp.sum(weights, -1)
    mixed = jnp.einsum(
        "bqk,bkd->bqd",
        weights.astype(jnp.bfloat16),
        values,
        preferred_element_type=jnp.float32,
    )
    peak = jnp.max(score_peak, 0, keepdims=True)
    factor = jnp.exp(score_peak - peak)
    summed = jnp.sum(factor[..., None] * mixed, 0)
    denominator = jnp.sum(factor * weight_sum, 0)
    return (summed / denominator[:, None]).astype(jnp.bfloat16)


def shards(
    residual_in,
    queries,
    new_keys,
    new_values,
    cache_keys,
    cache_values,
    cached_len,
    rope_offset,
    out_weight,
    gate_weight,
    up_weight,
    down_weight,
    expert_ids,
    gate_share,
):
    req_count = lax.axis_size("req")
    piece_count = lax.axis_size("ep")
    devices = req_count * piece_count
    experts = devices // 2
    groups, piece_rows, _ = queries.shape
    cache_rows = cache_keys.shape[1]
    top_count = expert_ids.shape[2]
    capacity = (piece_rows * top_count + experts - 1) // experts + 1
    piece_index = lax.axis_index("ep")
    new_index = piece_index * piece_rows + jnp.arange(piece_rows, dtype=jnp.int32)
    positions = rope_offset[:, None] + cached_len[:, None] + new_index[None, :]
    query_turned = rotate_rows(queries, positions, HEADS)[0]
    key_turned = rotate_rows(new_keys, positions, HEADS)[0]
    splits = piece_count // HEADS
    query_rows = piece_rows // splits

    def by_head(rows):
        return jnp.transpose(rows.reshape(rows.shape[0], HEADS, HD), (1, 0, 2))

    def both_halves(parts):
        joined = jnp.concatenate(parts, 1)
        return jnp.broadcast_to(joined[:, None], (HEADS, splits) + joined.shape[1:]).reshape(
            (piece_count,) + joined.shape[1:]
        )

    cache_sent = both_halves([by_head(cache_keys[0]), by_head(cache_values[0])])
    cache_got = lax.all_to_all(cache_sent, "ep", split_axis=0, concat_axis=0, tiled=True)
    q_parts = jnp.transpose(
        query_turned.reshape(splits, query_rows, HEADS, HD), (2, 0, 1, 3)
    ).reshape(piece_count, query_rows, HD)
    new_sent = jnp.concatenate(
        [both_halves([by_head(key_turned), by_head(new_values[0])]), q_parts], 1
    )
    new_sent, cache_got = lax.optimization_barrier((new_sent, cache_got))
    new_got = lax.all_to_all(new_sent, "ep", split_axis=0, concat_axis=0, tiled=True)
    keys = jnp.concatenate([cache_got[:, :cache_rows], new_got[:, :piece_rows]], 1)
    values = jnp.concatenate(
        [cache_got[:, cache_rows:], new_got[:, piece_rows : 2 * piece_rows]], 1
    )
    head_out = head_attention(
        keys,
        values,
        new_got[:, 2 * piece_rows :],
        cached_len[0],
        piece_index % splits,
        piece_rows,
        cache_rows,
    ).reshape(piece_count, query_rows, HD)
    returned = lax.all_to_all(head_out, "ep", split_axis=0, concat_axis=0, tiled=True)
    attended = jnp.transpose(
        returned.reshape(HEADS, splits, query_rows, HD), (1, 2, 0, 3)
    ).reshape(groups, piece_rows, HEADS * HD)
    hidden = residual_in.astype(jnp.float32) + jnp.einsum(
        "gtc,cd->gtd", attended, out_weight, preferred_element_type=jnp.float32
    )
    inv_root = lax.rsqrt(jnp.mean(hidden * hidden, -1, keepdims=True) + EPS)
    normed = (hidden * inv_root).astype(jnp.bfloat16)
    width = normed.shape[-1]
    rows = normed[0]
    slots = capacity
    ids = expert_ids[0]
    matches = (ids[..., None] == jnp.arange(experts, dtype=jnp.int32)).astype(jnp.int32)
    flat_matches = matches.reshape(piece_rows * top_count, experts)
    earlier = jnp.cumsum(flat_matches, 0) - flat_matches
    slot_index = jnp.sum(earlier * flat_matches, -1).reshape(piece_rows, top_count)
    target = ids * slots + slot_index
    chosen = target[..., None] == jnp.arange(experts * slots, dtype=jnp.int32)
    picked = jnp.any(chosen, 1).reshape(piece_rows, experts, 1, slots)
    weight = jnp.sum(jnp.where(chosen, gate_share[0][..., None], 0.0), 1)
    select = jnp.broadcast_to(picked, (piece_rows, experts, 2, slots)).astype(jnp.bfloat16)
    weight = weight.reshape(piece_rows, experts, slots)
    routed = jnp.zeros((piece_rows, width), jnp.float32)
    lane = 128
    for low, high in ((0, 8), (8, slots)):
        chunk = high - low
        travel = (chunk, width) if chunk % 8 == 0 else (chunk * width // lane, lane)
        sending = jnp.einsum(
            "teks,tw->eksw",
            select[..., low:high],
            rows,
            preferred_element_type=jnp.float32,
        ).astype(jnp.bfloat16).reshape((devices,) + travel)
        arrived = deliver(sending)
        produced = expert_half(
            arrived.reshape(-1, width), gate_weight[0], up_weight[0], down_weight[0]
        ).reshape((devices,) + travel)
        came_back = collect(produced).reshape(experts, 2, chunk, width)
        joined = (
            came_back[:, 0].astype(jnp.float32) + came_back[:, 1].astype(jnp.float32)
        ).astype(jnp.bfloat16)
        routed = routed + jnp.dot(
            weight[..., low:high].reshape(piece_rows, experts * chunk),
            joined.reshape(experts * chunk, width).astype(jnp.float32),
            precision=lax.Precision.HIGHEST,
        )
    return (hidden + routed[None]).astype(jnp.bfloat16)


def solution(mesh):
    in_specs = (
        P("req", "ep", None),
        P("req", "ep", None),
        P("req", "ep", None),
        P("req", "ep", None),
        P("req", "ep", None),
        P("req", "ep", None),
        P("req"),
        P("req"),
        P(),
        P(("req", "ep"), None, None),
        P(("req", "ep"), None, None),
        P(("req", "ep"), None, None),
        P("req", "ep", None),
        P("req", "ep", None),
    )
    out_specs = P("req", "ep", None)
    return jax.shard_map(shards, mesh=mesh, in_specs=in_specs, out_specs=out_specs, check_vma=False)
```

```python
import functools

import jax
import jax.numpy as jnp
from jax import lax
from jax.experimental import pallas as pl
from jax.experimental.pallas import tpu as pltpu
from jax.sharding import PartitionSpec as P

HEADS = 8
HD = 128


NEG_FILL = -1e30
EPS = 1e-06
ROPE_BASE = 10000.0


def rotate_rows(values, positions, head_count):
    width_each = values.shape[-1] // head_count
    half_size = width_each // 2
    frequency = ROPE_BASE ** (
        -jnp.arange(half_size, dtype=jnp.int32).astype(jnp.float32) / half_size
    )
    angles = positions.astype(jnp.float32)[..., None] * frequency
    cosine = jnp.cos(angles)[..., None, :]
    sine = jnp.sin(angles)[..., None, :]
    shaped = values.astype(jnp.float32).reshape(values.shape[:-1] + (head_count, width_each))
    lower = shaped[..., :half_size]
    upper = shaped[..., half_size:]
    turned = jnp.concatenate(
        [lower * cosine - upper * sine, lower * sine + upper * cosine], axis=-1
    )
    return turned.reshape(values.shape).astype(jnp.bfloat16)


def block_terms(query_all, cache_k, cache_v, keys_new, values_new, length, cache_start, new_start):
    query_count = query_all.shape[0]
    cache_rows = cache_k.shape[0]
    piece_rows = keys_new.shape[0]
    query_heads = query_all.reshape(query_count, HEADS, HD)
    key_heads = jnp.concatenate([cache_k, keys_new], 0).reshape(-1, HEADS, HD)
    value_heads = jnp.concatenate([cache_v, values_new], 0).reshape(-1, HEADS, HD)
    scores = jnp.einsum(
        "qhd,khd->hqk", query_heads, key_heads, preferred_element_type=jnp.float32
    ) * HD ** (-0.5)
    cache_valid = cache_start + jnp.arange(cache_rows, dtype=jnp.int32) < length
    new_valid = (new_start + jnp.arange(piece_rows, dtype=jnp.int32))[None, :] <= jnp.arange(
        query_count, dtype=jnp.int32
    )[:, None]
    valid = jnp.concatenate(
        [jnp.broadcast_to(cache_valid[None, :], (query_count, cache_rows)), new_valid], 1
    )[None]
    masked = jnp.where(valid, scores, NEG_FILL)
    score_peak = jnp.max(masked, -1)
    weights = jnp.where(valid, jnp.exp(masked - score_peak[..., None]), 0.0)
    weight_sum = jnp.sum(weights, -1)
    mixed = jnp.einsum(
        "hqk,khd->qhd",
        weights.astype(jnp.bfloat16),
        value_heads,
        preferred_element_type=jnp.float32,
    )
    return (mixed, score_peak.T, weight_sum.T)


def expert_half(rows, gate_part, up_part, down_part):
    gate_val = jnp.dot(rows, gate_part, preferred_element_type=jnp.float32)
    up_val = jnp.dot(rows, up_part, preferred_element_type=jnp.float32)
    activation = (jax.nn.silu(gate_val) * up_val).astype(jnp.bfloat16)
    return jnp.dot(activation, down_part, preferred_element_type=jnp.float32).astype(jnp.bfloat16)


def deliver(rows):
    return lax.all_to_all(rows, ("req", "ep"), split_axis=0, concat_axis=0, tiled=True)


def collect(rows):
    return lax.all_to_all(rows, ("req", "ep"), split_axis=0, concat_axis=0, tiled=True)


def head_attention(keys, values, query, length, half_index, piece_rows, cache_rows):
    pieces, query_rows = query.shape[0], query.shape[1]
    block_rows = cache_rows + piece_rows
    query = query.reshape(pieces * query_rows, HD)
    scores = jnp.einsum(
        "qd,bkd->bqk", query, keys, preferred_element_type=jnp.float32
    ) * HD ** (-0.5)
    block = jnp.arange(pieces, dtype=jnp.int32)[:, None, None]
    key_pos = jnp.arange(block_rows, dtype=jnp.int32)[None, None, :]
    query_row = jnp.arange(pieces * query_rows, dtype=jnp.int32)
    query_index = (
        (query_row // query_rows) * piece_rows + half_index * query_rows + query_row % query_rows
    )[None, :, None]
    cache_valid = block * cache_rows + key_pos < length
    new_valid = block * piece_rows + (key_pos - cache_rows) <= query_index
    valid = jnp.where(key_pos < cache_rows, cache_valid, new_valid)
    masked = jnp.where(valid, scores, NEG_FILL)
    score_peak = jnp.max(masked, -1)
    weights = jnp.where(valid, jnp.exp(masked - score_peak[..., None]), 0.0)
    weight_sum = jnp.sum(weights, -1)
    mixed = jnp.einsum(
        "bqk,bkd->bqd",
        weights.astype(jnp.bfloat16),
        values,
        preferred_element_type=jnp.float32,
    )
    peak = jnp.max(score_peak, 0, keepdims=True)
    factor = jnp.exp(score_peak - peak)
    summed = jnp.sum(factor[..., None] * mixed, 0)
    denominator = jnp.sum(factor * weight_sum, 0)
    return (summed / denominator[:, None]).astype(jnp.bfloat16)


def attention_kernel(scalars, kc_ref, vc_ref, kn_ref, vn_ref, q_ref, o_ref, m_scr, acc_scr, den_scr, *, cache_rows, piece_rows, query_rows):
    block = pl.program_id(0)
    length = scalars[0]
    half = scalars[1]

    @pl.when(block == 0)
    def _():
        m_scr[...] = jnp.full(m_scr.shape, NEG_FILL, jnp.float32)
        acc_scr[...] = jnp.zeros(acc_scr.shape, jnp.float32)
        den_scr[...] = jnp.zeros(den_scr.shape, jnp.float32)

    query = q_ref[...].reshape(-1, HD)
    count = query.shape[0]
    dims = (((1,), (1,)), ((), ()))
    s_cache = lax.dot_general(query, kc_ref[0], dims, preferred_element_type=jnp.float32) * HD ** (-0.5)
    s_new = lax.dot_general(query, kn_ref[0], dims, preferred_element_type=jnp.float32) * HD ** (-0.5)
    cache_pos = lax.broadcasted_iota(jnp.int32, (count, cache_rows), 1)
    cache_ok = block * cache_rows + cache_pos < length
    new_pos = lax.broadcasted_iota(jnp.int32, (count, piece_rows), 1)
    row = lax.broadcasted_iota(jnp.int32, (count, piece_rows), 0)
    query_index = (row // query_rows) * piece_rows + half * query_rows + row % query_rows
    new_ok = block * piece_rows + new_pos <= query_index
    masked_cache = jnp.where(cache_ok, s_cache, NEG_FILL)
    masked_new = jnp.where(new_ok, s_new, NEG_FILL)
    peak = jnp.maximum(
        jnp.max(masked_cache, axis=1, keepdims=True), jnp.max(masked_new, axis=1, keepdims=True)
    )
    p_cache = jnp.where(cache_ok, jnp.exp(masked_cache - peak), 0.0)
    p_new = jnp.where(new_ok, jnp.exp(masked_new - peak), 0.0)
    total = jnp.sum(p_cache, axis=1, keepdims=True) + jnp.sum(p_new, axis=1, keepdims=True)
    mixed = jnp.dot(p_cache.astype(jnp.bfloat16), vc_ref[0], preferred_element_type=jnp.float32) + jnp.dot(
        p_new.astype(jnp.bfloat16), vn_ref[0], preferred_element_type=jnp.float32
    )
    old = m_scr[...]
    top = jnp.maximum(old, peak)
    keep = jnp.exp(old - top)
    scale = jnp.exp(peak - top)
    acc_scr[...] = acc_scr[...] * keep + scale * mixed
    den_scr[...] = den_scr[...] * keep + scale * total
    m_scr[...] = top

    @pl.when(block == pl.num_programs(0) - 1)
    def _():
        o_ref[...] = (acc_scr[...] / den_scr[...]).astype(o_ref.dtype)


def head_attention_kernel(cache_got, new_got, length, half_index, piece_rows, cache_rows):
    pieces = cache_got.shape[0]
    query_rows = new_got.shape[1] - 2 * piece_rows
    count = pieces * query_rows
    scalars = jnp.stack([length, half_index]).astype(jnp.int32)
    kernel = functools.partial(attention_kernel, cache_rows=cache_rows, piece_rows=piece_rows, query_rows=query_rows)
    grid_spec = pltpu.PrefetchScalarGridSpec(
        num_scalar_prefetch=1,
        grid=(pieces,),
        in_specs=[
            pl.BlockSpec((1, cache_rows, HD), lambda b, s: (b, 0, 0)),
            pl.BlockSpec((1, cache_rows, HD), lambda b, s: (b, 1, 0)),
            pl.BlockSpec((1, piece_rows, HD), lambda b, s: (b, 0, 0)),
            pl.BlockSpec((1, piece_rows, HD), lambda b, s: (b, 1, 0)),
            pl.BlockSpec((pieces, query_rows, HD), lambda b, s: (0, 2 * piece_rows // query_rows, 0)),
        ],
        out_specs=pl.BlockSpec((count, HD), lambda b, s: (0, 0)),
        scratch_shapes=[
            pltpu.VMEM((count, 1), jnp.float32),
            pltpu.VMEM((count, HD), jnp.float32),
            pltpu.VMEM((count, 1), jnp.float32),
        ],
    )
    return pl.pallas_call(
        kernel,
        grid_spec=grid_spec,
        out_shape=jax.ShapeDtypeStruct((count, HD), jnp.bfloat16),
        compiler_params=pltpu.CompilerParams(dimension_semantics=("arbitrary",)),
    )(scalars, cache_got, cache_got, new_got, new_got, new_got)


def shards(
    residual_in,
    queries,
    new_keys,
    new_values,
    cache_keys,
    cache_values,
    cached_len,
    rope_offset,
    out_weight,
    gate_weight,
    up_weight,
    down_weight,
    expert_ids,
    gate_share,
):
    req_count = lax.axis_size("req")
    piece_count = lax.axis_size("ep")
    devices = req_count * piece_count
    experts = devices // 2
    groups, piece_rows, _ = queries.shape
    cache_rows = cache_keys.shape[1]
    top_count = expert_ids.shape[2]
    capacity = (piece_rows * top_count + experts - 1) // experts + 1
    piece_index = lax.axis_index("ep")
    new_index = piece_index * piece_rows + jnp.arange(piece_rows, dtype=jnp.int32)
    positions = rope_offset[:, None] + cached_len[:, None] + new_index[None, :]
    query_turned = rotate_rows(queries, positions, HEADS)[0]
    key_turned = rotate_rows(new_keys, positions, HEADS)[0]
    splits = piece_count // HEADS
    query_rows = piece_rows // splits

    def by_head(rows):
        return jnp.transpose(rows.reshape(rows.shape[0], HEADS, HD), (1, 0, 2))

    def both_halves(parts):
        joined = jnp.concatenate(parts, 1)
        return jnp.broadcast_to(joined[:, None], (HEADS, splits) + joined.shape[1:]).reshape(
            (piece_count,) + joined.shape[1:]
        )

    cache_sent = both_halves([by_head(cache_keys[0]), by_head(cache_values[0])])
    cache_got = lax.all_to_all(cache_sent, "ep", split_axis=0, concat_axis=0, tiled=True)
    q_parts = jnp.transpose(
        query_turned.reshape(splits, query_rows, HEADS, HD), (2, 0, 1, 3)
    ).reshape(piece_count, query_rows, HD)
    new_sent = jnp.concatenate(
        [both_halves([by_head(key_turned), by_head(new_values[0])]), q_parts], 1
    )
    new_sent, cache_got = lax.optimization_barrier((new_sent, cache_got))
    new_got = lax.all_to_all(new_sent, "ep", split_axis=0, concat_axis=0, tiled=True)
    head_out = head_attention_kernel(
        cache_got, new_got, cached_len[0], piece_index % splits, piece_rows, cache_rows
    ).reshape(piece_count, query_rows, HD)
    returned = lax.all_to_all(head_out, "ep", split_axis=0, concat_axis=0, tiled=True)
    attended = jnp.transpose(
        returned.reshape(HEADS, splits, query_rows, HD), (1, 2, 0, 3)
    ).reshape(groups, piece_rows, HEADS * HD)
    hidden = residual_in.astype(jnp.float32) + jnp.einsum(
        "gtc,cd->gtd", attended, out_weight, preferred_element_type=jnp.float32
    )
    inv_root = lax.rsqrt(jnp.mean(hidden * hidden, -1, keepdims=True) + EPS)
    normed = (hidden * inv_root).astype(jnp.bfloat16)
    width = normed.shape[-1]
    rows = normed[0]
    slots = capacity
    ids = expert_ids[0]
    matches = (ids[..., None] == jnp.arange(experts, dtype=jnp.int32)).astype(jnp.int32)
    flat_matches = matches.reshape(piece_rows * top_count, experts)
    earlier = jnp.cumsum(flat_matches, 0) - flat_matches
    slot_index = jnp.sum(earlier * flat_matches, -1).reshape(piece_rows, top_count)
    target = ids * slots + slot_index
    chosen = target[..., None] == jnp.arange(experts * slots, dtype=jnp.int32)
    picked = jnp.any(chosen, 1).reshape(piece_rows, experts, 1, slots)
    weight = jnp.sum(jnp.where(chosen, gate_share[0][..., None], 0.0), 1)
    select = jnp.broadcast_to(picked, (piece_rows, experts, 2, slots)).astype(jnp.bfloat16)
    weight = weight.reshape(piece_rows, experts, slots)
    routed = jnp.zeros((piece_rows, width), jnp.float32)
    lane = 128
    for low, high in ((0, 8), (8, slots)):
        chunk = high - low
        travel = (chunk, width) if chunk % 8 == 0 else (chunk * width // lane, lane)
        sending = jnp.einsum(
            "teks,tw->eksw",
            select[..., low:high],
            rows,
            preferred_element_type=jnp.float32,
        ).astype(jnp.bfloat16).reshape((devices,) + travel)
        arrived = deliver(sending)
        produced = expert_half(
            arrived.reshape(-1, width), gate_weight[0], up_weight[0], down_weight[0]
        ).reshape((devices,) + travel)
        came_back = collect(produced).reshape(experts, 2, chunk, width)
        joined = (
            came_back[:, 0].astype(jnp.float32) + came_back[:, 1].astype(jnp.float32)
        ).astype(jnp.bfloat16)
        routed = routed + jnp.dot(
            weight[..., low:high].reshape(piece_rows, experts * chunk),
            joined.reshape(experts * chunk, width).astype(jnp.float32),
            precision=lax.Precision.HIGHEST,
        )
    return (hidden + routed[None]).astype(jnp.bfloat16)


def solution(mesh):
    in_specs = (
        P("req", "ep", None),
        P("req", "ep", None),
        P("req", "ep", None),
        P("req", "ep", None),
        P("req", "ep", None),
        P("req", "ep", None),
        P("req"),
        P("req"),
        P(),
        P(("req", "ep"), None, None),
        P(("req", "ep"), None, None),
        P(("req", "ep"), None, None),
        P("req", "ep", None),
        P("req", "ep", None),
    )
    out_specs = P("req", "ep", None)
    return jax.shard_map(shards, mesh=mesh, in_specs=in_specs, out_specs=out_specs, check_vma=False)
```

```python
import functools

import jax
import jax.numpy as jnp
from jax import lax
from jax.experimental import pallas as pl
from jax.experimental.pallas import tpu as pltpu
from jax.sharding import PartitionSpec as P

HEADS = 8
HD = 128


NEG_FILL = -1e30
EPS = 1e-06
ROPE_BASE = 10000.0


def rotate_rows(values, positions, head_count):
    width_each = values.shape[-1] // head_count
    half_size = width_each // 2
    frequency = ROPE_BASE ** (
        -jnp.arange(half_size, dtype=jnp.int32).astype(jnp.float32) / half_size
    )
    angles = positions.astype(jnp.float32)[..., None] * frequency
    cosine = jnp.cos(angles)[..., None, :]
    sine = jnp.sin(angles)[..., None, :]
    shaped = values.astype(jnp.float32).reshape(values.shape[:-1] + (head_count, width_each))
    lower = shaped[..., :half_size]
    upper = shaped[..., half_size:]
    turned = jnp.concatenate(
        [lower * cosine - upper * sine, lower * sine + upper * cosine], axis=-1
    )
    return turned.reshape(values.shape).astype(jnp.bfloat16)


def block_terms(query_all, cache_k, cache_v, keys_new, values_new, length, cache_start, new_start):
    query_count = query_all.shape[0]
    cache_rows = cache_k.shape[0]
    piece_rows = keys_new.shape[0]
    query_heads = query_all.reshape(query_count, HEADS, HD)
    key_heads = jnp.concatenate([cache_k, keys_new], 0).reshape(-1, HEADS, HD)
    value_heads = jnp.concatenate([cache_v, values_new], 0).reshape(-1, HEADS, HD)
    scores = jnp.einsum(
        "qhd,khd->hqk", query_heads, key_heads, preferred_element_type=jnp.float32
    ) * HD ** (-0.5)
    cache_valid = cache_start + jnp.arange(cache_rows, dtype=jnp.int32) < length
    new_valid = (new_start + jnp.arange(piece_rows, dtype=jnp.int32))[None, :] <= jnp.arange(
        query_count, dtype=jnp.int32
    )[:, None]
    valid = jnp.concatenate(
        [jnp.broadcast_to(cache_valid[None, :], (query_count, cache_rows)), new_valid], 1
    )[None]
    masked = jnp.where(valid, scores, NEG_FILL)
    score_peak = jnp.max(masked, -1)
    weights = jnp.where(valid, jnp.exp(masked - score_peak[..., None]), 0.0)
    weight_sum = jnp.sum(weights, -1)
    mixed = jnp.einsum(
        "hqk,khd->qhd",
        weights.astype(jnp.bfloat16),
        value_heads,
        preferred_element_type=jnp.float32,
    )
    return (mixed, score_peak.T, weight_sum.T)


def expert_half(rows, gate_part, up_part, down_part):
    gate_val = jnp.dot(rows, gate_part, preferred_element_type=jnp.float32)
    up_val = jnp.dot(rows, up_part, preferred_element_type=jnp.float32)
    activation = (jax.nn.silu(gate_val) * up_val).astype(jnp.bfloat16)
    return jnp.dot(activation, down_part, preferred_element_type=jnp.float32).astype(jnp.bfloat16)


def deliver(rows):
    return lax.all_to_all(rows, ("req", "ep"), split_axis=0, concat_axis=0, tiled=True)


def collect(rows):
    return lax.all_to_all(rows, ("req", "ep"), split_axis=0, concat_axis=0, tiled=True)


def head_attention(keys, values, query, length, half_index, piece_rows, cache_rows):
    pieces, query_rows = query.shape[0], query.shape[1]
    block_rows = cache_rows + piece_rows
    query = query.reshape(pieces * query_rows, HD)
    scores = jnp.einsum(
        "qd,bkd->bqk", query, keys, preferred_element_type=jnp.float32
    ) * HD ** (-0.5)
    block = jnp.arange(pieces, dtype=jnp.int32)[:, None, None]
    key_pos = jnp.arange(block_rows, dtype=jnp.int32)[None, None, :]
    query_row = jnp.arange(pieces * query_rows, dtype=jnp.int32)
    query_index = (
        (query_row // query_rows) * piece_rows + half_index * query_rows + query_row % query_rows
    )[None, :, None]
    cache_valid = block * cache_rows + key_pos < length
    new_valid = block * piece_rows + (key_pos - cache_rows) <= query_index
    valid = jnp.where(key_pos < cache_rows, cache_valid, new_valid)
    masked = jnp.where(valid, scores, NEG_FILL)
    score_peak = jnp.max(masked, -1)
    weights = jnp.where(valid, jnp.exp(masked - score_peak[..., None]), 0.0)
    weight_sum = jnp.sum(weights, -1)
    mixed = jnp.einsum(
        "bqk,bkd->bqd",
        weights.astype(jnp.bfloat16),
        values,
        preferred_element_type=jnp.float32,
    )
    peak = jnp.max(score_peak, 0, keepdims=True)
    factor = jnp.exp(score_peak - peak)
    summed = jnp.sum(factor[..., None] * mixed, 0)
    denominator = jnp.sum(factor * weight_sum, 0)
    return (summed / denominator[:, None]).astype(jnp.bfloat16)


def attention_kernel(scalars, kc_ref, vc_ref, kn_ref, vn_ref, q_ref, o_ref, m_scr, acc_scr, den_scr, *, cache_rows, piece_rows, query_rows):
    step = pl.program_id(0)
    length = scalars[0]
    half = scalars[1]
    per_step = kc_ref.shape[0]
    root = HD ** (-0.5)

    @pl.when(step == 0)
    def _():
        m_scr[...] = jnp.full(m_scr.shape, NEG_FILL, jnp.float32)
        acc_scr[...] = jnp.zeros(acc_scr.shape, jnp.float32)
        den_scr[...] = jnp.zeros(den_scr.shape, jnp.float32)

    query = q_ref[...].reshape(-1, HD)
    count = query.shape[0]
    dims = (((1,), (1,)), ((), ()))
    row = lax.broadcasted_iota(jnp.int32, (count, 1), 0)
    query_index = (row // query_rows) * piece_rows + half * query_rows + row % query_rows
    cache_pos = lax.broadcasted_iota(jnp.int32, (1, cache_rows), 1)
    new_pos = lax.broadcasted_iota(jnp.int32, (1, piece_rows), 1)
    for sub in range(per_step):
        block = step * per_step + sub
        s_cache = lax.dot_general(query, kc_ref[sub], dims, preferred_element_type=jnp.float32)
        s_new = lax.dot_general(query, kn_ref[sub], dims, preferred_element_type=jnp.float32)
        cache_bias = jnp.where(block * cache_rows + cache_pos < length, 0.0, NEG_FILL)
        masked_cache = s_cache + cache_bias
        masked_new = jnp.where(block * piece_rows + new_pos <= query_index, s_new, NEG_FILL)
        peak = jnp.maximum(
            jnp.max(masked_cache, axis=1, keepdims=True), jnp.max(masked_new, axis=1, keepdims=True)
        )
        p_cache = jnp.exp((masked_cache - peak) * root)
        p_new = jnp.exp((masked_new - peak) * root)
        total = jnp.sum(p_cache, axis=1, keepdims=True) + jnp.sum(p_new, axis=1, keepdims=True)
        mixed = jnp.dot(
            p_cache.astype(jnp.bfloat16), vc_ref[sub], preferred_element_type=jnp.float32
        ) + jnp.dot(p_new.astype(jnp.bfloat16), vn_ref[sub], preferred_element_type=jnp.float32)
        peak = jnp.where(peak > 0.5 * NEG_FILL, peak * root, NEG_FILL)
        old = m_scr[...]
        top = jnp.maximum(old, peak)
        keep = jnp.exp(old - top)
        scale = jnp.exp(peak - top)
        acc_scr[...] = acc_scr[...] * keep + scale * mixed
        den_scr[...] = den_scr[...] * keep + scale * total
        m_scr[...] = top

    @pl.when(step == pl.num_programs(0) - 1)
    def _():
        o_ref[...] = (acc_scr[...] / den_scr[...]).astype(o_ref.dtype)


def head_attention_kernel(cache_got, new_got, length, half_index, piece_rows, cache_rows):
    pieces = cache_got.shape[0]
    per_step = 2
    query_rows = new_got.shape[1] - 2 * piece_rows
    count = pieces * query_rows
    scalars = jnp.stack([length, half_index]).astype(jnp.int32)
    kernel = functools.partial(attention_kernel, cache_rows=cache_rows, piece_rows=piece_rows, query_rows=query_rows)
    grid_spec = pltpu.PrefetchScalarGridSpec(
        num_scalar_prefetch=1,
        grid=(pieces // per_step,),
        in_specs=[
            pl.BlockSpec((per_step, cache_rows, HD), lambda b, s: (b, 0, 0)),
            pl.BlockSpec((per_step, cache_rows, HD), lambda b, s: (b, 1, 0)),
            pl.BlockSpec((per_step, piece_rows, HD), lambda b, s: (b, 0, 0)),
            pl.BlockSpec((per_step, piece_rows, HD), lambda b, s: (b, 1, 0)),
            pl.BlockSpec((pieces, query_rows, HD), lambda b, s: (0, 2 * piece_rows // query_rows, 0)),
        ],
        out_specs=pl.BlockSpec((count, HD), lambda b, s: (0, 0)),
        scratch_shapes=[
            pltpu.VMEM((count, 1), jnp.float32),
            pltpu.VMEM((count, HD), jnp.float32),
            pltpu.VMEM((count, 1), jnp.float32),
        ],
    )
    return pl.pallas_call(
        kernel,
        grid_spec=grid_spec,
        out_shape=jax.ShapeDtypeStruct((count, HD), jnp.bfloat16),
        compiler_params=pltpu.CompilerParams(dimension_semantics=("arbitrary",)),
    )(scalars, cache_got, cache_got, new_got, new_got, new_got)


def shards(
    residual_in,
    queries,
    new_keys,
    new_values,
    cache_keys,
    cache_values,
    cached_len,
    rope_offset,
    out_weight,
    gate_weight,
    up_weight,
    down_weight,
    expert_ids,
    gate_share,
):
    req_count = lax.axis_size("req")
    piece_count = lax.axis_size("ep")
    devices = req_count * piece_count
    experts = devices // 2
    groups, piece_rows, _ = queries.shape
    cache_rows = cache_keys.shape[1]
    top_count = expert_ids.shape[2]
    capacity = (piece_rows * top_count + experts - 1) // experts + 1
    piece_index = lax.axis_index("ep")
    new_index = piece_index * piece_rows + jnp.arange(piece_rows, dtype=jnp.int32)
    positions = rope_offset[:, None] + cached_len[:, None] + new_index[None, :]
    query_turned = rotate_rows(queries, positions, HEADS)[0]
    key_turned = rotate_rows(new_keys, positions, HEADS)[0]
    splits = piece_count // HEADS
    query_rows = piece_rows // splits

    def by_head(rows):
        return jnp.transpose(rows.reshape(rows.shape[0], HEADS, HD), (1, 0, 2))

    def both_halves(parts):
        joined = jnp.concatenate(parts, 1)
        return jnp.broadcast_to(joined[:, None], (HEADS, splits) + joined.shape[1:]).reshape(
            (piece_count,) + joined.shape[1:]
        )

    cache_sent = both_halves([by_head(cache_keys[0]), by_head(cache_values[0])])
    cache_got = lax.all_to_all(cache_sent, "ep", split_axis=0, concat_axis=0, tiled=True)
    q_parts = jnp.transpose(
        query_turned.reshape(splits, query_rows, HEADS, HD), (2, 0, 1, 3)
    ).reshape(piece_count, query_rows, HD)
    new_sent = jnp.concatenate(
        [both_halves([by_head(key_turned), by_head(new_values[0])]), q_parts], 1
    )
    new_sent, cache_got = lax.optimization_barrier((new_sent, cache_got))
    new_got = lax.all_to_all(new_sent, "ep", split_axis=0, concat_axis=0, tiled=True)
    head_out = head_attention_kernel(
        cache_got, new_got, cached_len[0], piece_index % splits, piece_rows, cache_rows
    ).reshape(piece_count, query_rows, HD)
    returned = lax.all_to_all(head_out, "ep", split_axis=0, concat_axis=0, tiled=True)
    attended = jnp.transpose(
        returned.reshape(HEADS, splits, query_rows, HD), (1, 2, 0, 3)
    ).reshape(groups, piece_rows, HEADS * HD)
    hidden = residual_in.astype(jnp.float32) + jnp.einsum(
        "gtc,cd->gtd", attended, out_weight, preferred_element_type=jnp.float32
    )
    inv_root = lax.rsqrt(jnp.mean(hidden * hidden, -1, keepdims=True) + EPS)
    normed = (hidden * inv_root).astype(jnp.bfloat16)
    width = normed.shape[-1]
    rows = normed[0]
    slots = capacity
    ids = expert_ids[0]
    matches = (ids[..., None] == jnp.arange(experts, dtype=jnp.int32)).astype(jnp.int32)
    flat_matches = matches.reshape(piece_rows * top_count, experts)
    earlier = jnp.cumsum(flat_matches, 0) - flat_matches
    slot_index = jnp.sum(earlier * flat_matches, -1).reshape(piece_rows, top_count)
    target = ids * slots + slot_index
    chosen = target[..., None] == jnp.arange(experts * slots, dtype=jnp.int32)
    picked = jnp.any(chosen, 1).reshape(piece_rows, experts, 1, slots)
    weight = jnp.sum(jnp.where(chosen, gate_share[0][..., None], 0.0), 1)
    select = jnp.broadcast_to(picked, (piece_rows, experts, 2, slots)).astype(jnp.bfloat16)
    weight = weight.reshape(piece_rows, experts, slots)
    routed = jnp.zeros((piece_rows, width), jnp.float32)
    lane = 128
    for low, high in ((0, 8), (8, slots)):
        chunk = high - low
        travel = (chunk, width) if chunk % 8 == 0 else (chunk * width // lane, lane)
        sending = jnp.einsum(
            "teks,tw->eksw",
            select[..., low:high],
            rows,
            preferred_element_type=jnp.float32,
        ).astype(jnp.bfloat16).reshape((devices,) + travel)
        arrived = deliver(sending)
        produced = expert_half(
            arrived.reshape(-1, width), gate_weight[0], up_weight[0], down_weight[0]
        ).reshape((devices,) + travel)
        came_back = collect(produced).reshape(experts, 2, chunk, width)
        joined = (
            came_back[:, 0].astype(jnp.float32) + came_back[:, 1].astype(jnp.float32)
        ).astype(jnp.bfloat16)
        routed = routed + jnp.dot(
            weight[..., low:high].reshape(piece_rows, experts * chunk),
            joined.reshape(experts * chunk, width).astype(jnp.float32),
            precision=lax.Precision.HIGHEST,
        )
    return (hidden + routed[None]).astype(jnp.bfloat16)


def solution(mesh):
    in_specs = (
        P("req", "ep", None),
        P("req", "ep", None),
        P("req", "ep", None),
        P("req", "ep", None),
        P("req", "ep", None),
        P("req", "ep", None),
        P("req"),
        P("req"),
        P(),
        P(("req", "ep"), None, None),
        P(("req", "ep"), None, None),
        P(("req", "ep"), None, None),
        P("req", "ep", None),
        P("req", "ep", None),
    )
    out_specs = P("req", "ep", None)
    return jax.shard_map(shards, mesh=mesh, in_specs=in_specs, out_specs=out_specs, check_vma=False)
```

```python
import functools

import jax
import jax.numpy as jnp
from jax import lax
from jax.experimental import pallas as pl
from jax.experimental.pallas import tpu as pltpu
from jax.sharding import PartitionSpec as P

HEADS = 8
HD = 128


NEG_FILL = -1e30
EPS = 1e-06
ROPE_BASE = 10000.0


def rotate_rows(values, positions, head_count):
    width_each = values.shape[-1] // head_count
    half_size = width_each // 2
    frequency = ROPE_BASE ** (
        -jnp.arange(half_size, dtype=jnp.int32).astype(jnp.float32) / half_size
    )
    angles = positions.astype(jnp.float32)[..., None] * frequency
    cosine = jnp.cos(angles)[..., None, :]
    sine = jnp.sin(angles)[..., None, :]
    shaped = values.astype(jnp.float32).reshape(values.shape[:-1] + (head_count, width_each))
    lower = shaped[..., :half_size]
    upper = shaped[..., half_size:]
    turned = jnp.concatenate(
        [lower * cosine - upper * sine, lower * sine + upper * cosine], axis=-1
    )
    return turned.reshape(values.shape).astype(jnp.bfloat16)


def block_terms(query_all, cache_k, cache_v, keys_new, values_new, length, cache_start, new_start):
    query_count = query_all.shape[0]
    cache_rows = cache_k.shape[0]
    piece_rows = keys_new.shape[0]
    query_heads = query_all.reshape(query_count, HEADS, HD)
    key_heads = jnp.concatenate([cache_k, keys_new], 0).reshape(-1, HEADS, HD)
    value_heads = jnp.concatenate([cache_v, values_new], 0).reshape(-1, HEADS, HD)
    scores = jnp.einsum(
        "qhd,khd->hqk", query_heads, key_heads, preferred_element_type=jnp.float32
    ) * HD ** (-0.5)
    cache_valid = cache_start + jnp.arange(cache_rows, dtype=jnp.int32) < length
    new_valid = (new_start + jnp.arange(piece_rows, dtype=jnp.int32))[None, :] <= jnp.arange(
        query_count, dtype=jnp.int32
    )[:, None]
    valid = jnp.concatenate(
        [jnp.broadcast_to(cache_valid[None, :], (query_count, cache_rows)), new_valid], 1
    )[None]
    masked = jnp.where(valid, scores, NEG_FILL)
    score_peak = jnp.max(masked, -1)
    weights = jnp.where(valid, jnp.exp(masked - score_peak[..., None]), 0.0)
    weight_sum = jnp.sum(weights, -1)
    mixed = jnp.einsum(
        "hqk,khd->qhd",
        weights.astype(jnp.bfloat16),
        value_heads,
        preferred_element_type=jnp.float32,
    )
    return (mixed, score_peak.T, weight_sum.T)


def expert_half(rows, gate_part, up_part, down_part):
    gate_val = jnp.dot(rows, gate_part, preferred_element_type=jnp.float32)
    up_val = jnp.dot(rows, up_part, preferred_element_type=jnp.float32)
    activation = (jax.nn.silu(gate_val) * up_val).astype(jnp.bfloat16)
    return jnp.dot(activation, down_part, preferred_element_type=jnp.float32).astype(jnp.bfloat16)


def deliver(rows):
    return lax.all_to_all(rows, ("req", "ep"), split_axis=0, concat_axis=0, tiled=True)


def collect(rows):
    return lax.all_to_all(rows, ("req", "ep"), split_axis=0, concat_axis=0, tiled=True)


def head_attention(keys, values, query, length, half_index, piece_rows, cache_rows):
    pieces, query_rows = query.shape[0], query.shape[1]
    block_rows = cache_rows + piece_rows
    query = query.reshape(pieces * query_rows, HD)
    scores = jnp.einsum(
        "qd,bkd->bqk", query, keys, preferred_element_type=jnp.float32
    ) * HD ** (-0.5)
    block = jnp.arange(pieces, dtype=jnp.int32)[:, None, None]
    key_pos = jnp.arange(block_rows, dtype=jnp.int32)[None, None, :]
    query_row = jnp.arange(pieces * query_rows, dtype=jnp.int32)
    query_index = (
        (query_row // query_rows) * piece_rows + half_index * query_rows + query_row % query_rows
    )[None, :, None]
    cache_valid = block * cache_rows + key_pos < length
    new_valid = block * piece_rows + (key_pos - cache_rows) <= query_index
    valid = jnp.where(key_pos < cache_rows, cache_valid, new_valid)
    masked = jnp.where(valid, scores, NEG_FILL)
    score_peak = jnp.max(masked, -1)
    weights = jnp.where(valid, jnp.exp(masked - score_peak[..., None]), 0.0)
    weight_sum = jnp.sum(weights, -1)
    mixed = jnp.einsum(
        "bqk,bkd->bqd",
        weights.astype(jnp.bfloat16),
        values,
        preferred_element_type=jnp.float32,
    )
    peak = jnp.max(score_peak, 0, keepdims=True)
    factor = jnp.exp(score_peak - peak)
    summed = jnp.sum(factor[..., None] * mixed, 0)
    denominator = jnp.sum(factor * weight_sum, 0)
    return (summed / denominator[:, None]).astype(jnp.bfloat16)


def attention_kernel(scalars, kc_ref, vc_ref, kn_ref, vn_ref, q_ref, o_ref, m_scr, acc_scr, den_scr, *, cache_rows, piece_rows, query_rows):
    step = pl.program_id(0)
    length = scalars[0]
    half = scalars[1]
    per_step = kc_ref.shape[0]
    root = HD ** (-0.5)

    @pl.when(step == 0)
    def _():
        m_scr[...] = jnp.full(m_scr.shape, NEG_FILL, jnp.float32)
        acc_scr[...] = jnp.zeros(acc_scr.shape, jnp.float32)
        den_scr[...] = jnp.zeros(den_scr.shape, jnp.float32)

    query = q_ref[...].reshape(-1, HD)
    count = query.shape[0]
    dims = (((1,), (1,)), ((), ()))
    row = lax.broadcasted_iota(jnp.int32, (count, 1), 0)
    query_index = (row // query_rows) * piece_rows + half * query_rows + row % query_rows
    cache_pos = lax.broadcasted_iota(jnp.int32, (1, cache_rows), 1)
    new_pos = lax.broadcasted_iota(jnp.int32, (1, piece_rows), 1)
    for sub in range(per_step):
        block = step * per_step + sub
        s_cache = lax.dot_general(query, kc_ref[sub], dims, preferred_element_type=jnp.float32)
        s_new = lax.dot_general(query, kn_ref[sub], dims, preferred_element_type=jnp.float32)
        cache_bias = jnp.where(block * cache_rows + cache_pos < length, 0.0, NEG_FILL)
        masked_cache = s_cache + cache_bias
        masked_new = jnp.where(block * piece_rows + new_pos <= query_index, s_new, NEG_FILL)
        peak = jnp.maximum(
            jnp.max(masked_cache, axis=1, keepdims=True), jnp.max(masked_new, axis=1, keepdims=True)
        )
        p_cache = jnp.exp((masked_cache - peak) * root)
        p_new = jnp.exp((masked_new - peak) * root)
        total = jnp.sum(p_cache, axis=1, keepdims=True) + jnp.sum(p_new, axis=1, keepdims=True)
        mixed = jnp.dot(
            p_cache.astype(jnp.bfloat16), vc_ref[sub], preferred_element_type=jnp.float32
        ) + jnp.dot(p_new.astype(jnp.bfloat16), vn_ref[sub], preferred_element_type=jnp.float32)
        peak = jnp.where(peak > 0.5 * NEG_FILL, peak * root, NEG_FILL)
        old = m_scr[...]
        top = jnp.maximum(old, peak)
        keep = jnp.exp(old - top)
        scale = jnp.exp(peak - top)
        acc_scr[...] = acc_scr[...] * keep + scale * mixed
        den_scr[...] = den_scr[...] * keep + scale * total
        m_scr[...] = top

    @pl.when(step == pl.num_programs(0) - 1)
    def _():
        o_ref[...] = (acc_scr[...] / den_scr[...]).astype(o_ref.dtype)


def head_attention_kernel(cache_got, new_got, length, half_index, piece_rows, cache_rows):
    pieces = cache_got.shape[0]
    per_step = 2
    query_rows = new_got.shape[1] - 2 * piece_rows
    count = pieces * query_rows
    scalars = jnp.stack([length, half_index]).astype(jnp.int32)
    kernel = functools.partial(attention_kernel, cache_rows=cache_rows, piece_rows=piece_rows, query_rows=query_rows)
    grid_spec = pltpu.PrefetchScalarGridSpec(
        num_scalar_prefetch=1,
        grid=(pieces // per_step,),
        in_specs=[
            pl.BlockSpec((per_step, cache_rows, HD), lambda b, s: (b, 0, 0)),
            pl.BlockSpec((per_step, cache_rows, HD), lambda b, s: (b, 1, 0)),
            pl.BlockSpec((per_step, piece_rows, HD), lambda b, s: (b, 0, 0)),
            pl.BlockSpec((per_step, piece_rows, HD), lambda b, s: (b, 1, 0)),
            pl.BlockSpec((pieces, query_rows, HD), lambda b, s: (0, 2 * piece_rows // query_rows, 0)),
        ],
        out_specs=pl.BlockSpec((count, HD), lambda b, s: (0, 0)),
        scratch_shapes=[
            pltpu.VMEM((count, 1), jnp.float32),
            pltpu.VMEM((count, HD), jnp.float32),
            pltpu.VMEM((count, 1), jnp.float32),
        ],
    )
    return pl.pallas_call(
        kernel,
        grid_spec=grid_spec,
        out_shape=jax.ShapeDtypeStruct((count, HD), jnp.bfloat16),
        compiler_params=pltpu.CompilerParams(dimension_semantics=("arbitrary",)),
    )(scalars, cache_got, cache_got, new_got, new_got, new_got)


def shards(
    residual_in,
    queries,
    new_keys,
    new_values,
    cache_keys,
    cache_values,
    cached_len,
    rope_offset,
    out_weight,
    gate_weight,
    up_weight,
    down_weight,
    expert_ids,
    gate_share,
):
    req_count = lax.axis_size("req")
    piece_count = lax.axis_size("ep")
    devices = req_count * piece_count
    experts = devices // 2
    groups, piece_rows, _ = queries.shape
    cache_rows = cache_keys.shape[1]
    top_count = expert_ids.shape[2]
    capacity = (piece_rows * top_count + experts - 1) // experts + 1
    piece_index = lax.axis_index("ep")
    new_index = piece_index * piece_rows + jnp.arange(piece_rows, dtype=jnp.int32)
    positions = rope_offset[:, None] + cached_len[:, None] + new_index[None, :]
    query_turned = rotate_rows(queries, positions, HEADS)[0]
    key_turned = rotate_rows(new_keys, positions, HEADS)[0]
    splits = piece_count // HEADS
    query_rows = piece_rows // splits

    def by_head(rows):
        return jnp.transpose(rows.reshape(rows.shape[0], HEADS, HD), (1, 0, 2))

    def both_halves(parts):
        joined = jnp.concatenate(parts, 1)
        return jnp.broadcast_to(joined[:, None], (HEADS, splits) + joined.shape[1:]).reshape(
            (piece_count,) + joined.shape[1:]
        )

    cache_sent = both_halves([by_head(cache_keys[0]), by_head(cache_values[0])])
    cache_got = lax.all_to_all(cache_sent, "ep", split_axis=0, concat_axis=0, tiled=True)
    q_parts = jnp.transpose(
        query_turned.reshape(splits, query_rows, HEADS, HD), (2, 0, 1, 3)
    ).reshape(piece_count, query_rows, HD)
    new_sent = jnp.concatenate(
        [both_halves([by_head(key_turned), by_head(new_values[0])]), q_parts], 1
    )
    new_sent, cache_got = lax.optimization_barrier((new_sent, cache_got))
    new_got = lax.all_to_all(new_sent, "ep", split_axis=0, concat_axis=0, tiled=True)
    head_out = head_attention_kernel(
        cache_got, new_got, cached_len[0], piece_index % splits, piece_rows, cache_rows
    ).reshape(piece_count, query_rows, HD)
    returned = lax.all_to_all(head_out, "ep", split_axis=0, concat_axis=0, tiled=True)
    attended = jnp.transpose(
        returned.reshape(HEADS, splits, query_rows, HD), (1, 2, 0, 3)
    ).reshape(groups, piece_rows, HEADS * HD)
    hidden = residual_in.astype(jnp.float32) + jnp.einsum(
        "gtc,cd->gtd", attended, out_weight, preferred_element_type=jnp.float32
    )
    inv_root = lax.rsqrt(jnp.mean(hidden * hidden, -1, keepdims=True) + EPS)
    normed = (hidden * inv_root).astype(jnp.bfloat16)
    width = normed.shape[-1]
    rows = normed[0]
    slots = capacity
    ids = expert_ids[0]
    matches = (ids[..., None] == jnp.arange(experts, dtype=jnp.int32)).astype(jnp.int32)
    flat_matches = matches.reshape(piece_rows * top_count, experts)
    earlier = jnp.cumsum(flat_matches, 0) - flat_matches
    slot_index = jnp.sum(earlier * flat_matches, -1).reshape(piece_rows, top_count)
    target = ids * slots + slot_index
    chosen = target[..., None] == jnp.arange(experts * slots, dtype=jnp.int32)
    picked = jnp.any(chosen, 1).reshape(piece_rows, experts, 1, slots)
    weight = jnp.sum(jnp.where(chosen, gate_share[0][..., None], 0.0), 1)
    weight = weight.reshape(piece_rows, experts, slots)
    routed = jnp.zeros((piece_rows, width), jnp.float32)
    lane = 128
    for low, high in ((8, slots), (0, 8)):
        chunk = high - low
        travel = (chunk, width) if chunk % 8 == 0 else (chunk * width // lane, lane)
        chunk_select = picked[..., low:high].astype(jnp.bfloat16)
        once = jnp.einsum(
            "teks,tw->eksw", chunk_select, rows, preferred_element_type=jnp.float32
        ).astype(jnp.bfloat16).reshape((experts, 1) + travel)
        sending = jnp.broadcast_to(once, (experts, 2) + travel).reshape((devices,) + travel)
        arrived = deliver(sending)
        produced = expert_half(
            arrived.reshape(-1, width), gate_weight[0], up_weight[0], down_weight[0]
        ).reshape((devices,) + travel)
        came_back = collect(produced).reshape((experts, 2) + travel)
        joined = (
            came_back[:, 0].astype(jnp.float32) + came_back[:, 1].astype(jnp.float32)
        ).astype(jnp.bfloat16)
        routed = routed + jnp.dot(
            weight[..., low:high].reshape(piece_rows, experts * chunk),
            joined.reshape(experts * chunk, width).astype(jnp.float32),
            precision=lax.Precision.HIGHEST,
        )
    return (hidden + routed[None]).astype(jnp.bfloat16)


def solution(mesh):
    in_specs = (
        P("req", "ep", None),
        P("req", "ep", None),
        P("req", "ep", None),
        P("req", "ep", None),
        P("req", "ep", None),
        P("req", "ep", None),
        P("req"),
        P("req"),
        P(),
        P(("req", "ep"), None, None),
        P(("req", "ep"), None, None),
        P(("req", "ep"), None, None),
        P("req", "ep", None),
        P("req", "ep", None),
    )
    out_specs = P("req", "ep", None)
    return jax.shard_map(shards, mesh=mesh, in_specs=in_specs, out_specs=out_specs, check_vma=False)
```

```python
import functools

import jax
import jax.numpy as jnp
from jax import lax
from jax.experimental import pallas as pl
from jax.experimental.pallas import tpu as pltpu
from jax.sharding import PartitionSpec as P

HEADS = 8
HD = 128


NEG_FILL = -1e30
EPS = 1e-06
ROPE_BASE = 10000.0


def rotate_rows(values, positions, head_count):
    width_each = values.shape[-1] // head_count
    half_size = width_each // 2
    frequency = ROPE_BASE ** (
        -jnp.arange(half_size, dtype=jnp.int32).astype(jnp.float32) / half_size
    )
    angles = positions.astype(jnp.float32)[..., None] * frequency
    cosine = jnp.cos(angles)[..., None, :]
    sine = jnp.sin(angles)[..., None, :]
    shaped = values.astype(jnp.float32).reshape(values.shape[:-1] + (head_count, width_each))
    lower = shaped[..., :half_size]
    upper = shaped[..., half_size:]
    turned = jnp.concatenate(
        [lower * cosine - upper * sine, lower * sine + upper * cosine], axis=-1
    )
    return turned.reshape(values.shape).astype(jnp.bfloat16)


def block_terms(query_all, cache_k, cache_v, keys_new, values_new, length, cache_start, new_start):
    query_count = query_all.shape[0]
    cache_rows = cache_k.shape[0]
    piece_rows = keys_new.shape[0]
    query_heads = query_all.reshape(query_count, HEADS, HD)
    key_heads = jnp.concatenate([cache_k, keys_new], 0).reshape(-1, HEADS, HD)
    value_heads = jnp.concatenate([cache_v, values_new], 0).reshape(-1, HEADS, HD)
    scores = jnp.einsum(
        "qhd,khd->hqk", query_heads, key_heads, preferred_element_type=jnp.float32
    ) * HD ** (-0.5)
    cache_valid = cache_start + jnp.arange(cache_rows, dtype=jnp.int32) < length
    new_valid = (new_start + jnp.arange(piece_rows, dtype=jnp.int32))[None, :] <= jnp.arange(
        query_count, dtype=jnp.int32
    )[:, None]
    valid = jnp.concatenate(
        [jnp.broadcast_to(cache_valid[None, :], (query_count, cache_rows)), new_valid], 1
    )[None]
    masked = jnp.where(valid, scores, NEG_FILL)
    score_peak = jnp.max(masked, -1)
    weights = jnp.where(valid, jnp.exp(masked - score_peak[..., None]), 0.0)
    weight_sum = jnp.sum(weights, -1)
    mixed = jnp.einsum(
        "hqk,khd->qhd",
        weights.astype(jnp.bfloat16),
        value_heads,
        preferred_element_type=jnp.float32,
    )
    return (mixed, score_peak.T, weight_sum.T)


def expert_half(rows, gate_part, up_part, down_part):
    gate_val = jnp.dot(rows, gate_part, preferred_element_type=jnp.float32)
    up_val = jnp.dot(rows, up_part, preferred_element_type=jnp.float32)
    activation = (jax.nn.silu(gate_val) * up_val).astype(jnp.bfloat16)
    return jnp.dot(activation, down_part, preferred_element_type=jnp.float32).astype(jnp.bfloat16)


def deliver(rows):
    return lax.all_to_all(rows, ("req", "ep"), split_axis=0, concat_axis=0, tiled=True)


def collect(rows):
    return lax.all_to_all(rows, ("req", "ep"), split_axis=0, concat_axis=0, tiled=True)


def head_attention(keys, values, query, length, half_index, piece_rows, cache_rows):
    pieces, query_rows = query.shape[0], query.shape[1]
    block_rows = cache_rows + piece_rows
    query = query.reshape(pieces * query_rows, HD)
    scores = jnp.einsum(
        "qd,bkd->bqk", query, keys, preferred_element_type=jnp.float32
    ) * HD ** (-0.5)
    block = jnp.arange(pieces, dtype=jnp.int32)[:, None, None]
    key_pos = jnp.arange(block_rows, dtype=jnp.int32)[None, None, :]
    query_row = jnp.arange(pieces * query_rows, dtype=jnp.int32)
    query_index = (
        (query_row // query_rows) * piece_rows + half_index * query_rows + query_row % query_rows
    )[None, :, None]
    cache_valid = block * cache_rows + key_pos < length
    new_valid = block * piece_rows + (key_pos - cache_rows) <= query_index
    valid = jnp.where(key_pos < cache_rows, cache_valid, new_valid)
    masked = jnp.where(valid, scores, NEG_FILL)
    score_peak = jnp.max(masked, -1)
    weights = jnp.where(valid, jnp.exp(masked - score_peak[..., None]), 0.0)
    weight_sum = jnp.sum(weights, -1)
    mixed = jnp.einsum(
        "bqk,bkd->bqd",
        weights.astype(jnp.bfloat16),
        values,
        preferred_element_type=jnp.float32,
    )
    peak = jnp.max(score_peak, 0, keepdims=True)
    factor = jnp.exp(score_peak - peak)
    summed = jnp.sum(factor[..., None] * mixed, 0)
    denominator = jnp.sum(factor * weight_sum, 0)
    return (summed / denominator[:, None]).astype(jnp.bfloat16)


def attention_kernel(scalars, kc_ref, vc_ref, kn_ref, vn_ref, q_ref, o_ref, m_scr, acc_scr, den_scr, *, cache_rows, piece_rows, query_rows):
    step = pl.program_id(0)
    length = scalars[0]
    half = scalars[1]
    per_step = kc_ref.shape[0]
    root = HD ** (-0.5)

    @pl.when(step == 0)
    def _():
        m_scr[...] = jnp.full(m_scr.shape, NEG_FILL, jnp.float32)
        acc_scr[...] = jnp.zeros(acc_scr.shape, jnp.float32)
        den_scr[...] = jnp.zeros(den_scr.shape, jnp.float32)

    query = q_ref[...].reshape(-1, HD)
    count = query.shape[0]
    dims = (((1,), (1,)), ((), ()))
    row = lax.broadcasted_iota(jnp.int32, (count, 1), 0)
    query_index = (row // query_rows) * piece_rows + half * query_rows + row % query_rows
    cache_pos = lax.broadcasted_iota(jnp.int32, (1, cache_rows), 1)
    new_pos = lax.broadcasted_iota(jnp.int32, (1, piece_rows), 1)
    for sub in range(per_step):
        block = step * per_step + sub
        s_cache = lax.dot_general(query, kc_ref[sub], dims, preferred_element_type=jnp.float32)
        s_new = lax.dot_general(query, kn_ref[sub], dims, preferred_element_type=jnp.float32)
        cache_bias = jnp.where(block * cache_rows + cache_pos < length, 0.0, NEG_FILL)
        masked_cache = s_cache + cache_bias
        masked_new = jnp.where(block * piece_rows + new_pos <= query_index, s_new, NEG_FILL)
        peak = jnp.maximum(
            jnp.max(masked_cache, axis=1, keepdims=True), jnp.max(masked_new, axis=1, keepdims=True)
        )
        p_cache = jnp.exp((masked_cache - peak) * root)
        p_new = jnp.exp((masked_new - peak) * root)
        total = jnp.sum(p_cache, axis=1, keepdims=True) + jnp.sum(p_new, axis=1, keepdims=True)
        mixed = jnp.dot(
            p_cache.astype(jnp.bfloat16), vc_ref[sub], preferred_element_type=jnp.float32
        ) + jnp.dot(p_new.astype(jnp.bfloat16), vn_ref[sub], preferred_element_type=jnp.float32)
        peak = jnp.where(peak > 0.5 * NEG_FILL, peak * root, NEG_FILL)
        old = m_scr[...]
        top = jnp.maximum(old, peak)
        keep = jnp.exp(old - top)
        scale = jnp.exp(peak - top)
        acc_scr[...] = acc_scr[...] * keep + scale * mixed
        den_scr[...] = den_scr[...] * keep + scale * total
        m_scr[...] = top

    @pl.when(step == pl.num_programs(0) - 1)
    def _():
        o_ref[...] = (acc_scr[...] / den_scr[...]).astype(o_ref.dtype)


def head_attention_kernel(cache_got, new_got, length, half_index, piece_rows, cache_rows):
    pieces = cache_got.shape[0]
    per_step = 2
    query_rows = new_got.shape[1] - 2 * piece_rows
    count = pieces * query_rows
    scalars = jnp.stack([length, half_index]).astype(jnp.int32)
    kernel = functools.partial(attention_kernel, cache_rows=cache_rows, piece_rows=piece_rows, query_rows=query_rows)
    grid_spec = pltpu.PrefetchScalarGridSpec(
        num_scalar_prefetch=1,
        grid=(pieces // per_step,),
        in_specs=[
            pl.BlockSpec((per_step, cache_rows, HD), lambda b, s: (b, 0, 0)),
            pl.BlockSpec((per_step, cache_rows, HD), lambda b, s: (b, 1, 0)),
            pl.BlockSpec((per_step, piece_rows, HD), lambda b, s: (b, 0, 0)),
            pl.BlockSpec((per_step, piece_rows, HD), lambda b, s: (b, 1, 0)),
            pl.BlockSpec((pieces, query_rows, HD), lambda b, s: (0, 2 * piece_rows // query_rows, 0)),
        ],
        out_specs=pl.BlockSpec((count, HD), lambda b, s: (0, 0)),
        scratch_shapes=[
            pltpu.VMEM((count, 1), jnp.float32),
            pltpu.VMEM((count, HD), jnp.float32),
            pltpu.VMEM((count, 1), jnp.float32),
        ],
    )
    return pl.pallas_call(
        kernel,
        grid_spec=grid_spec,
        out_shape=jax.ShapeDtypeStruct((count, HD), jnp.bfloat16),
        compiler_params=pltpu.CompilerParams(dimension_semantics=("arbitrary",)),
    )(scalars, cache_got, cache_got, new_got, new_got, new_got)


def shards(
    residual_in,
    queries,
    new_keys,
    new_values,
    cache_keys,
    cache_values,
    cached_len,
    rope_offset,
    out_weight,
    gate_weight,
    up_weight,
    down_weight,
    expert_ids,
    gate_share,
):
    req_count = lax.axis_size("req")
    piece_count = lax.axis_size("ep")
    devices = req_count * piece_count
    experts = devices // 2
    groups, piece_rows, _ = queries.shape
    cache_rows = cache_keys.shape[1]
    top_count = expert_ids.shape[2]
    capacity = (piece_rows * top_count + experts - 1) // experts + 1
    piece_index = lax.axis_index("ep")
    new_index = piece_index * piece_rows + jnp.arange(piece_rows, dtype=jnp.int32)
    positions = rope_offset[:, None] + cached_len[:, None] + new_index[None, :]
    query_turned = rotate_rows(queries, positions, HEADS)[0]
    key_turned = rotate_rows(new_keys, positions, HEADS)[0]
    splits = piece_count // HEADS
    query_rows = piece_rows // splits

    def by_head(rows):
        return jnp.transpose(rows.reshape(rows.shape[0], HEADS, HD), (1, 0, 2))

    def both_halves(parts):
        joined = jnp.concatenate(parts, 1)
        return jnp.broadcast_to(joined[:, None], (HEADS, splits) + joined.shape[1:]).reshape(
            (piece_count,) + joined.shape[1:]
        )

    cache_sent = both_halves([by_head(cache_keys[0]), by_head(cache_values[0])])
    cache_got = lax.all_to_all(cache_sent, "ep", split_axis=0, concat_axis=0, tiled=True)
    q_parts = jnp.transpose(
        query_turned.reshape(splits, query_rows, HEADS, HD), (2, 0, 1, 3)
    ).reshape(piece_count, query_rows, HD)
    new_sent = jnp.concatenate(
        [both_halves([by_head(key_turned), by_head(new_values[0])]), q_parts], 1
    )
    new_sent, cache_got = lax.optimization_barrier((new_sent, cache_got))
    new_got = lax.all_to_all(new_sent, "ep", split_axis=0, concat_axis=0, tiled=True)
    head_out = head_attention_kernel(
        cache_got, new_got, cached_len[0], piece_index % splits, piece_rows, cache_rows
    ).reshape(piece_count, query_rows, HD)
    returned = lax.all_to_all(head_out, "ep", split_axis=0, concat_axis=0, tiled=True)
    attended = jnp.transpose(
        returned.reshape(HEADS, splits, query_rows, HD), (1, 2, 0, 3)
    ).reshape(groups, piece_rows, HEADS * HD)
    hidden = residual_in.astype(jnp.float32) + jnp.einsum(
        "gtc,cd->gtd", attended, out_weight, preferred_element_type=jnp.float32
    )
    inv_root = lax.rsqrt(jnp.mean(hidden * hidden, -1, keepdims=True) + EPS)
    normed = (hidden * inv_root).astype(jnp.bfloat16)
    width = normed.shape[-1]
    rows = normed[0]
    slots = capacity
    ids = expert_ids[0]
    matches = (ids[..., None] == jnp.arange(experts, dtype=jnp.int32)).astype(jnp.int32)
    flat_matches = matches.reshape(piece_rows * top_count, experts)
    earlier = jnp.cumsum(flat_matches, 0) - flat_matches
    slot_index = jnp.sum(earlier * flat_matches, -1).reshape(piece_rows, top_count)
    target = ids * slots + slot_index
    chosen = target[..., None] == jnp.arange(experts * slots, dtype=jnp.int32)
    picked = jnp.any(chosen, 1).reshape(piece_rows, experts, 1, slots)
    weight = jnp.sum(jnp.where(chosen, gate_share[0][..., None], 0.0), 1)
    weight = weight.reshape(piece_rows, experts, slots)
    routed = jnp.zeros((piece_rows, width), jnp.float32)
    lane = 128
    for low, high in ((8, slots), (0, 8)):
        chunk = high - low
        travel = (chunk, width) if chunk % 8 == 0 else (chunk * width // lane, lane)
        chunk_select = picked[..., low:high].astype(jnp.bfloat16)
        if chunk % 8 == 0:
            chunk_select = jnp.broadcast_to(chunk_select, (piece_rows, experts, 2, chunk))
        once = jnp.einsum(
            "teks,tw->eksw", chunk_select, rows, preferred_element_type=jnp.float32
        ).astype(jnp.bfloat16)
        sending = jnp.broadcast_to(
            once.reshape((experts, -1) + travel), (experts, 2) + travel
        ).reshape((devices,) + travel)
        arrived = deliver(sending)
        produced = expert_half(
            arrived.reshape(-1, width), gate_weight[0], up_weight[0], down_weight[0]
        ).reshape((devices,) + travel)
        came_back = collect(produced).reshape((experts, 2) + travel)
        joined = (
            came_back[:, 0].astype(jnp.float32) + came_back[:, 1].astype(jnp.float32)
        ).astype(jnp.bfloat16)
        routed = routed + jnp.dot(
            weight[..., low:high].reshape(piece_rows, experts * chunk),
            joined.reshape(experts * chunk, width).astype(jnp.float32),
            precision=lax.Precision.HIGHEST,
        )
    return (hidden + routed[None]).astype(jnp.bfloat16)


def solution(mesh):
    in_specs = (
        P("req", "ep", None),
        P("req", "ep", None),
        P("req", "ep", None),
        P("req", "ep", None),
        P("req", "ep", None),
        P("req", "ep", None),
        P("req"),
        P("req"),
        P(),
        P(("req", "ep"), None, None),
        P(("req", "ep"), None, None),
        P(("req", "ep"), None, None),
        P("req", "ep", None),
        P("req", "ep", None),
    )
    out_specs = P("req", "ep", None)
    return jax.shard_map(shards, mesh=mesh, in_specs=in_specs, out_specs=out_specs, check_vma=False)
```

```python
import functools

import jax
import jax.numpy as jnp
from jax import lax
from jax.experimental import pallas as pl
from jax.experimental.pallas import tpu as pltpu
from jax.sharding import PartitionSpec as P

HEADS = 8
HD = 128


NEG_FILL = -1e30
EPS = 1e-06
ROPE_BASE = 10000.0


def rotate_rows(values, positions, head_count):
    width_each = values.shape[-1] // head_count
    half_size = width_each // 2
    frequency = ROPE_BASE ** (
        -jnp.arange(half_size, dtype=jnp.int32).astype(jnp.float32) / half_size
    )
    angles = positions.astype(jnp.float32)[..., None] * frequency
    cosine = jnp.cos(angles)[..., None, :]
    sine = jnp.sin(angles)[..., None, :]
    shaped = values.astype(jnp.float32).reshape(values.shape[:-1] + (head_count, width_each))
    lower = shaped[..., :half_size]
    upper = shaped[..., half_size:]
    turned = jnp.concatenate(
        [lower * cosine - upper * sine, lower * sine + upper * cosine], axis=-1
    )
    return turned.reshape(values.shape).astype(jnp.bfloat16)


def block_terms(query_all, cache_k, cache_v, keys_new, values_new, length, cache_start, new_start):
    query_count = query_all.shape[0]
    cache_rows = cache_k.shape[0]
    piece_rows = keys_new.shape[0]
    query_heads = query_all.reshape(query_count, HEADS, HD)
    key_heads = jnp.concatenate([cache_k, keys_new], 0).reshape(-1, HEADS, HD)
    value_heads = jnp.concatenate([cache_v, values_new], 0).reshape(-1, HEADS, HD)
    scores = jnp.einsum(
        "qhd,khd->hqk", query_heads, key_heads, preferred_element_type=jnp.float32
    ) * HD ** (-0.5)
    cache_valid = cache_start + jnp.arange(cache_rows, dtype=jnp.int32) < length
    new_valid = (new_start + jnp.arange(piece_rows, dtype=jnp.int32))[None, :] <= jnp.arange(
        query_count, dtype=jnp.int32
    )[:, None]
    valid = jnp.concatenate(
        [jnp.broadcast_to(cache_valid[None, :], (query_count, cache_rows)), new_valid], 1
    )[None]
    masked = jnp.where(valid, scores, NEG_FILL)
    score_peak = jnp.max(masked, -1)
    weights = jnp.where(valid, jnp.exp(masked - score_peak[..., None]), 0.0)
    weight_sum = jnp.sum(weights, -1)
    mixed = jnp.einsum(
        "hqk,khd->qhd",
        weights.astype(jnp.bfloat16),
        value_heads,
        preferred_element_type=jnp.float32,
    )
    return (mixed, score_peak.T, weight_sum.T)


def expert_half(rows, gate_part, up_part, down_part):
    gate_val = jnp.dot(rows, gate_part, preferred_element_type=jnp.float32)
    up_val = jnp.dot(rows, up_part, preferred_element_type=jnp.float32)
    activation = (jax.nn.silu(gate_val) * up_val).astype(jnp.bfloat16)
    return jnp.dot(activation, down_part, preferred_element_type=jnp.float32).astype(jnp.bfloat16)


def deliver(rows):
    return lax.all_to_all(rows, ("req", "ep"), split_axis=0, concat_axis=0, tiled=True)


def collect(rows):
    return lax.all_to_all(rows, ("req", "ep"), split_axis=0, concat_axis=0, tiled=True)


def head_attention(keys, values, query, length, half_index, piece_rows, cache_rows):
    pieces, query_rows = query.shape[0], query.shape[1]
    block_rows = cache_rows + piece_rows
    query = query.reshape(pieces * query_rows, HD)
    scores = jnp.einsum(
        "qd,bkd->bqk", query, keys, preferred_element_type=jnp.float32
    ) * HD ** (-0.5)
    block = jnp.arange(pieces, dtype=jnp.int32)[:, None, None]
    key_pos = jnp.arange(block_rows, dtype=jnp.int32)[None, None, :]
    query_row = jnp.arange(pieces * query_rows, dtype=jnp.int32)
    query_index = (
        (query_row // query_rows) * piece_rows + half_index * query_rows + query_row % query_rows
    )[None, :, None]
    cache_valid = block * cache_rows + key_pos < length
    new_valid = block * piece_rows + (key_pos - cache_rows) <= query_index
    valid = jnp.where(key_pos < cache_rows, cache_valid, new_valid)
    masked = jnp.where(valid, scores, NEG_FILL)
    score_peak = jnp.max(masked, -1)
    weights = jnp.where(valid, jnp.exp(masked - score_peak[..., None]), 0.0)
    weight_sum = jnp.sum(weights, -1)
    mixed = jnp.einsum(
        "bqk,bkd->bqd",
        weights.astype(jnp.bfloat16),
        values,
        preferred_element_type=jnp.float32,
    )
    peak = jnp.max(score_peak, 0, keepdims=True)
    factor = jnp.exp(score_peak - peak)
    summed = jnp.sum(factor[..., None] * mixed, 0)
    denominator = jnp.sum(factor * weight_sum, 0)
    return (summed / denominator[:, None]).astype(jnp.bfloat16)


def fold_block(masked, values, m_ref, acc_ref, den_ref):
    root = HD ** (-0.5)
    peak = jnp.max(masked, axis=1, keepdims=True)
    weights = jnp.exp((masked - peak) * root)
    total = jnp.sum(weights, axis=1, keepdims=True)
    mixed = jnp.dot(weights.astype(jnp.bfloat16), values, preferred_element_type=jnp.float32)
    peak = jnp.where(peak > 0.5 * NEG_FILL, peak * root, NEG_FILL)
    old = m_ref[...]
    top = jnp.maximum(old, peak)
    keep = jnp.exp(old - top)
    scale = jnp.exp(peak - top)
    acc_ref[...] = acc_ref[...] * keep + scale * mixed
    den_ref[...] = den_ref[...] * keep + scale * total
    m_ref[...] = top


def cache_kernel(scalars, k_ref, v_ref, q_ref, m_ref, acc_ref, den_ref):
    step = pl.program_id(0)
    per_step, rows = k_ref.shape[0], k_ref.shape[1]

    @pl.when(step == 0)
    def _():
        m_ref[...] = jnp.full(m_ref.shape, NEG_FILL, jnp.float32)
        acc_ref[...] = jnp.zeros(acc_ref.shape, jnp.float32)
        den_ref[...] = jnp.zeros(den_ref.shape, jnp.float32)

    query = q_ref[...].reshape(-1, HD)
    dims = (((1,), (1,)), ((), ()))
    position = lax.broadcasted_iota(jnp.int32, (1, rows), 1)
    for sub in range(per_step):
        block = step * per_step + sub
        scores = lax.dot_general(query, k_ref[sub], dims, preferred_element_type=jnp.float32)
        bias = jnp.where(block * rows + position < scalars[0], 0.0, NEG_FILL)
        fold_block(scores + bias, v_ref[sub], m_ref, acc_ref, den_ref)


def new_kernel(scalars, k_ref, v_ref, q_ref, m_in, acc_in, den_in, o_ref, m_ref, acc_ref, den_ref):
    step = pl.program_id(0)
    per_step, rows = k_ref.shape[0], k_ref.shape[1]
    query_rows = q_ref.shape[1]

    @pl.when(step == 0)
    def _():
        m_ref[...] = m_in[...]
        acc_ref[...] = acc_in[...]
        den_ref[...] = den_in[...]

    query = q_ref[...].reshape(-1, HD)
    count = query.shape[0]
    dims = (((1,), (1,)), ((), ()))
    row = lax.broadcasted_iota(jnp.int32, (count, 1), 0)
    query_index = (row // query_rows) * rows + scalars[1] * query_rows + row % query_rows
    position = lax.broadcasted_iota(jnp.int32, (1, rows), 1)
    for sub in range(per_step):
        block = step * per_step + sub
        scores = lax.dot_general(query, k_ref[sub], dims, preferred_element_type=jnp.float32)
        masked = jnp.where(block * rows + position <= query_index, scores, NEG_FILL)
        fold_block(masked, v_ref[sub], m_ref, acc_ref, den_ref)

    @pl.when(step == pl.num_programs(0) - 1)
    def _():
        o_ref[...] = (acc_ref[...] / den_ref[...]).astype(o_ref.dtype)


def head_attention_kernel(cache_got, new_got, length, half_index, piece_rows, cache_rows):
    pieces = cache_got.shape[0]
    per_step = 2
    query_rows = cache_got.shape[1] - 2 * cache_rows
    count = pieces * query_rows
    scalars = jnp.stack([length, half_index]).astype(jnp.int32)
    query_spec = pl.BlockSpec(
        (pieces, query_rows, HD), lambda b, s: (0, 2 * cache_rows // query_rows, 0)
    )
    state_specs = [
        pl.BlockSpec((count, 1), lambda b, s: (0, 0)),
        pl.BlockSpec((count, HD), lambda b, s: (0, 0)),
        pl.BlockSpec((count, 1), lambda b, s: (0, 0)),
    ]
    state_shapes = (
        jax.ShapeDtypeStruct((count, 1), jnp.float32),
        jax.ShapeDtypeStruct((count, HD), jnp.float32),
        jax.ShapeDtypeStruct((count, 1), jnp.float32),
    )
    params = pltpu.CompilerParams(dimension_semantics=("arbitrary",))
    state = pl.pallas_call(
        cache_kernel,
        grid_spec=pltpu.PrefetchScalarGridSpec(
            num_scalar_prefetch=1,
            grid=(pieces // per_step,),
            in_specs=[
                pl.BlockSpec((per_step, cache_rows, HD), lambda b, s: (b, 0, 0)),
                pl.BlockSpec((per_step, cache_rows, HD), lambda b, s: (b, 1, 0)),
                query_spec,
            ],
            out_specs=state_specs,
        ),
        out_shape=state_shapes,
        compiler_params=params,
    )(scalars, cache_got, cache_got, cache_got)
    return pl.pallas_call(
        new_kernel,
        grid_spec=pltpu.PrefetchScalarGridSpec(
            num_scalar_prefetch=1,
            grid=(pieces // per_step,),
            in_specs=[
                pl.BlockSpec((per_step, piece_rows, HD), lambda b, s: (b, 0, 0)),
                pl.BlockSpec((per_step, piece_rows, HD), lambda b, s: (b, 1, 0)),
                query_spec,
            ]
            + state_specs,
            out_specs=pl.BlockSpec((count, HD), lambda b, s: (0, 0)),
            scratch_shapes=[
                pltpu.VMEM((count, 1), jnp.float32),
                pltpu.VMEM((count, HD), jnp.float32),
                pltpu.VMEM((count, 1), jnp.float32),
            ],
        ),
        out_shape=jax.ShapeDtypeStruct((count, HD), jnp.bfloat16),
        compiler_params=params,
    )(scalars, new_got, new_got, cache_got, *state)


def shards(
    residual_in,
    queries,
    new_keys,
    new_values,
    cache_keys,
    cache_values,
    cached_len,
    rope_offset,
    out_weight,
    gate_weight,
    up_weight,
    down_weight,
    expert_ids,
    gate_share,
):
    req_count = lax.axis_size("req")
    piece_count = lax.axis_size("ep")
    devices = req_count * piece_count
    experts = devices // 2
    groups, piece_rows, _ = queries.shape
    cache_rows = cache_keys.shape[1]
    top_count = expert_ids.shape[2]
    capacity = (piece_rows * top_count + experts - 1) // experts + 1
    piece_index = lax.axis_index("ep")
    new_index = piece_index * piece_rows + jnp.arange(piece_rows, dtype=jnp.int32)
    positions = rope_offset[:, None] + cached_len[:, None] + new_index[None, :]
    query_turned = rotate_rows(queries, positions, HEADS)[0]
    key_turned = rotate_rows(new_keys, positions, HEADS)[0]
    splits = piece_count // HEADS
    query_rows = piece_rows // splits

    def by_head(rows):
        return jnp.transpose(rows.reshape(rows.shape[0], HEADS, HD), (1, 0, 2))

    def both_halves(parts):
        joined = jnp.concatenate(parts, 1)
        return jnp.broadcast_to(joined[:, None], (HEADS, splits) + joined.shape[1:]).reshape(
            (piece_count,) + joined.shape[1:]
        )

    q_parts = jnp.transpose(
        query_turned.reshape(splits, query_rows, HEADS, HD), (2, 0, 1, 3)
    ).reshape(piece_count, query_rows, HD)
    cache_sent = jnp.concatenate(
        [both_halves([by_head(cache_keys[0]), by_head(cache_values[0])]), q_parts], 1
    )
    cache_got = lax.all_to_all(cache_sent, "ep", split_axis=0, concat_axis=0, tiled=True)
    new_sent = both_halves([by_head(key_turned), by_head(new_values[0])])
    new_sent, cache_got = lax.optimization_barrier((new_sent, cache_got))
    new_got = lax.all_to_all(new_sent, "ep", split_axis=0, concat_axis=0, tiled=True)
    head_out = head_attention_kernel(
        cache_got, new_got, cached_len[0], piece_index % splits, piece_rows, cache_rows
    ).reshape(piece_count, query_rows, HD)
    returned = lax.all_to_all(head_out, "ep", split_axis=0, concat_axis=0, tiled=True)
    attended = jnp.transpose(
        returned.reshape(HEADS, splits, query_rows, HD), (1, 2, 0, 3)
    ).reshape(groups, piece_rows, HEADS * HD)
    hidden = residual_in.astype(jnp.float32) + jnp.einsum(
        "gtc,cd->gtd", attended, out_weight, preferred_element_type=jnp.float32
    )
    inv_root = lax.rsqrt(jnp.mean(hidden * hidden, -1, keepdims=True) + EPS)
    normed = (hidden * inv_root).astype(jnp.bfloat16)
    width = normed.shape[-1]
    rows = normed[0]
    slots = capacity
    ids = expert_ids[0]
    matches = (ids[..., None] == jnp.arange(experts, dtype=jnp.int32)).astype(jnp.int32)
    flat_matches = matches.reshape(piece_rows * top_count, experts)
    earlier = jnp.cumsum(flat_matches, 0) - flat_matches
    slot_index = jnp.sum(earlier * flat_matches, -1).reshape(piece_rows, top_count)
    target = ids * slots + slot_index
    chosen = target[..., None] == jnp.arange(experts * slots, dtype=jnp.int32)
    picked = jnp.any(chosen, 1).reshape(piece_rows, experts, 1, slots)
    weight = jnp.sum(jnp.where(chosen, gate_share[0][..., None], 0.0), 1)
    weight = weight.reshape(piece_rows, experts, slots)
    routed = jnp.zeros((piece_rows, width), jnp.float32)
    lane = 128
    for low, high in ((8, slots), (0, 8)):
        chunk = high - low
        travel = (chunk, width) if chunk % 8 == 0 else (chunk * width // lane, lane)
        chunk_select = picked[..., low:high].astype(jnp.bfloat16)
        if chunk % 8 == 0:
            chunk_select = jnp.broadcast_to(chunk_select, (piece_rows, experts, 2, chunk))
        once = jnp.einsum(
            "teks,tw->eksw", chunk_select, rows, preferred_element_type=jnp.float32
        ).astype(jnp.bfloat16)
        sending = jnp.broadcast_to(
            once.reshape((experts, -1) + travel), (experts, 2) + travel
        ).reshape((devices,) + travel)
        arrived = deliver(sending)
        produced = expert_half(
            arrived.reshape(-1, width), gate_weight[0], up_weight[0], down_weight[0]
        ).reshape((devices,) + travel)
        came_back = collect(produced).reshape((experts, 2) + travel)
        joined = (
            came_back[:, 0].astype(jnp.float32) + came_back[:, 1].astype(jnp.float32)
        ).astype(jnp.bfloat16)
        routed = routed + jnp.dot(
            weight[..., low:high].reshape(piece_rows, experts * chunk),
            joined.reshape(experts * chunk, width).astype(jnp.float32),
            precision=lax.Precision.HIGHEST,
        )
    return (hidden + routed[None]).astype(jnp.bfloat16)


def solution(mesh):
    in_specs = (
        P("req", "ep", None),
        P("req", "ep", None),
        P("req", "ep", None),
        P("req", "ep", None),
        P("req", "ep", None),
        P("req", "ep", None),
        P("req"),
        P("req"),
        P(),
        P(("req", "ep"), None, None),
        P(("req", "ep"), None, None),
        P(("req", "ep"), None, None),
        P("req", "ep", None),
        P("req", "ep", None),
    )
    out_specs = P("req", "ep", None)
    return jax.shard_map(shards, mesh=mesh, in_specs=in_specs, out_specs=out_specs, check_vma=False)
```

```python
import functools

import jax
import jax.numpy as jnp
from jax import lax
from jax.experimental import pallas as pl
from jax.experimental.pallas import tpu as pltpu
from jax.sharding import PartitionSpec as P

HEADS = 8
HD = 128


NEG_FILL = -1e30
EPS = 1e-06
ROPE_BASE = 10000.0


def rotate_rows(values, positions, head_count):
    width_each = values.shape[-1] // head_count
    half_size = width_each // 2
    frequency = ROPE_BASE ** (
        -jnp.arange(half_size, dtype=jnp.int32).astype(jnp.float32) / half_size
    )
    angles = positions.astype(jnp.float32)[..., None] * frequency
    cosine = jnp.cos(angles)[..., None, :]
    sine = jnp.sin(angles)[..., None, :]
    shaped = values.astype(jnp.float32).reshape(values.shape[:-1] + (head_count, width_each))
    lower = shaped[..., :half_size]
    upper = shaped[..., half_size:]
    turned = jnp.concatenate(
        [lower * cosine - upper * sine, lower * sine + upper * cosine], axis=-1
    )
    return turned.reshape(values.shape).astype(jnp.bfloat16)


def block_terms(query_all, cache_k, cache_v, keys_new, values_new, length, cache_start, new_start):
    query_count = query_all.shape[0]
    cache_rows = cache_k.shape[0]
    piece_rows = keys_new.shape[0]
    query_heads = query_all.reshape(query_count, HEADS, HD)
    key_heads = jnp.concatenate([cache_k, keys_new], 0).reshape(-1, HEADS, HD)
    value_heads = jnp.concatenate([cache_v, values_new], 0).reshape(-1, HEADS, HD)
    scores = jnp.einsum(
        "qhd,khd->hqk", query_heads, key_heads, preferred_element_type=jnp.float32
    ) * HD ** (-0.5)
    cache_valid = cache_start + jnp.arange(cache_rows, dtype=jnp.int32) < length
    new_valid = (new_start + jnp.arange(piece_rows, dtype=jnp.int32))[None, :] <= jnp.arange(
        query_count, dtype=jnp.int32
    )[:, None]
    valid = jnp.concatenate(
        [jnp.broadcast_to(cache_valid[None, :], (query_count, cache_rows)), new_valid], 1
    )[None]
    masked = jnp.where(valid, scores, NEG_FILL)
    score_peak = jnp.max(masked, -1)
    weights = jnp.where(valid, jnp.exp(masked - score_peak[..., None]), 0.0)
    weight_sum = jnp.sum(weights, -1)
    mixed = jnp.einsum(
        "hqk,khd->qhd",
        weights.astype(jnp.bfloat16),
        value_heads,
        preferred_element_type=jnp.float32,
    )
    return (mixed, score_peak.T, weight_sum.T)


def expert_half(rows, gate_part, up_part, down_part):
    gate_val = jnp.dot(rows, gate_part, preferred_element_type=jnp.float32)
    up_val = jnp.dot(rows, up_part, preferred_element_type=jnp.float32)
    activation = (jax.nn.silu(gate_val) * up_val).astype(jnp.bfloat16)
    return jnp.dot(activation, down_part, preferred_element_type=jnp.float32).astype(jnp.bfloat16)


def deliver(rows):
    return lax.all_to_all(rows, ("req", "ep"), split_axis=0, concat_axis=0, tiled=True)


def collect(rows):
    return lax.all_to_all(rows, ("req", "ep"), split_axis=0, concat_axis=0, tiled=True)


def head_attention(keys, values, query, length, half_index, piece_rows, cache_rows):
    pieces, query_rows = query.shape[0], query.shape[1]
    block_rows = cache_rows + piece_rows
    query = query.reshape(pieces * query_rows, HD)
    scores = jnp.einsum(
        "qd,bkd->bqk", query, keys, preferred_element_type=jnp.float32
    ) * HD ** (-0.5)
    block = jnp.arange(pieces, dtype=jnp.int32)[:, None, None]
    key_pos = jnp.arange(block_rows, dtype=jnp.int32)[None, None, :]
    query_row = jnp.arange(pieces * query_rows, dtype=jnp.int32)
    query_index = (
        (query_row // query_rows) * piece_rows + half_index * query_rows + query_row % query_rows
    )[None, :, None]
    cache_valid = block * cache_rows + key_pos < length
    new_valid = block * piece_rows + (key_pos - cache_rows) <= query_index
    valid = jnp.where(key_pos < cache_rows, cache_valid, new_valid)
    masked = jnp.where(valid, scores, NEG_FILL)
    score_peak = jnp.max(masked, -1)
    weights = jnp.where(valid, jnp.exp(masked - score_peak[..., None]), 0.0)
    weight_sum = jnp.sum(weights, -1)
    mixed = jnp.einsum(
        "bqk,bkd->bqd",
        weights.astype(jnp.bfloat16),
        values,
        preferred_element_type=jnp.float32,
    )
    peak = jnp.max(score_peak, 0, keepdims=True)
    factor = jnp.exp(score_peak - peak)
    summed = jnp.sum(factor[..., None] * mixed, 0)
    denominator = jnp.sum(factor * weight_sum, 0)
    return (summed / denominator[:, None]).astype(jnp.bfloat16)


def attention_kernel(scalars, kc_ref, vc_ref, kn_ref, vn_ref, q_ref, o_ref, m_scr, acc_scr, den_scr, *, cache_rows, piece_rows, query_rows):
    step = pl.program_id(0)
    length = scalars[0]
    half = scalars[1]
    per_step = kc_ref.shape[0]
    root = HD ** (-0.5)

    @pl.when(step == 0)
    def _():
        m_scr[...] = jnp.full(m_scr.shape, NEG_FILL, jnp.float32)
        acc_scr[...] = jnp.zeros(acc_scr.shape, jnp.float32)
        den_scr[...] = jnp.zeros(den_scr.shape, jnp.float32)

    query = q_ref[...].reshape(-1, HD)
    count = query.shape[0]
    dims = (((1,), (1,)), ((), ()))
    row = lax.broadcasted_iota(jnp.int32, (count, 1), 0)
    query_index = (row // query_rows) * piece_rows + half * query_rows + row % query_rows
    cache_pos = lax.broadcasted_iota(jnp.int32, (1, cache_rows), 1)
    new_pos = lax.broadcasted_iota(jnp.int32, (1, piece_rows), 1)
    for sub in range(per_step):
        block = step * per_step + sub
        s_cache = lax.dot_general(query, kc_ref[sub], dims, preferred_element_type=jnp.float32)
        s_new = lax.dot_general(query, kn_ref[sub], dims, preferred_element_type=jnp.float32)
        cache_bias = jnp.where(block * cache_rows + cache_pos < length, 0.0, NEG_FILL)
        masked_cache = s_cache + cache_bias
        masked_new = jnp.where(block * piece_rows + new_pos <= query_index, s_new, NEG_FILL)
        peak = jnp.maximum(
            jnp.max(masked_cache, axis=1, keepdims=True), jnp.max(masked_new, axis=1, keepdims=True)
        )
        p_cache = jnp.exp((masked_cache - peak) * root)
        p_new = jnp.exp((masked_new - peak) * root)
        total = jnp.sum(p_cache, axis=1, keepdims=True) + jnp.sum(p_new, axis=1, keepdims=True)
        mixed = jnp.dot(
            p_cache.astype(jnp.bfloat16), vc_ref[sub], preferred_element_type=jnp.float32
        ) + jnp.dot(p_new.astype(jnp.bfloat16), vn_ref[sub], preferred_element_type=jnp.float32)
        peak = jnp.where(peak > 0.5 * NEG_FILL, peak * root, NEG_FILL)
        old = m_scr[...]
        top = jnp.maximum(old, peak)
        keep = jnp.exp(old - top)
        scale = jnp.exp(peak - top)
        acc_scr[...] = acc_scr[...] * keep + scale * mixed
        den_scr[...] = den_scr[...] * keep + scale * total
        m_scr[...] = top

    @pl.when(step == pl.num_programs(0) - 1)
    def _():
        o_ref[...] = (acc_scr[...] / den_scr[...]).astype(o_ref.dtype)


def head_attention_kernel(cache_got, new_got, length, half_index, piece_rows, cache_rows):
    pieces = cache_got.shape[0]
    per_step = 2
    query_rows = new_got.shape[1] - 2 * piece_rows
    count = pieces * query_rows
    scalars = jnp.stack([length, half_index]).astype(jnp.int32)
    kernel = functools.partial(attention_kernel, cache_rows=cache_rows, piece_rows=piece_rows, query_rows=query_rows)
    grid_spec = pltpu.PrefetchScalarGridSpec(
        num_scalar_prefetch=1,
        grid=(pieces // per_step,),
        in_specs=[
            pl.BlockSpec((per_step, cache_rows, HD), lambda b, s: (b, 0, 0)),
            pl.BlockSpec((per_step, cache_rows, HD), lambda b, s: (b, 1, 0)),
            pl.BlockSpec((per_step, piece_rows, HD), lambda b, s: (b, 0, 0)),
            pl.BlockSpec((per_step, piece_rows, HD), lambda b, s: (b, 1, 0)),
            pl.BlockSpec((pieces, query_rows, HD), lambda b, s: (0, 2 * piece_rows // query_rows, 0)),
        ],
        out_specs=pl.BlockSpec((count, HD), lambda b, s: (0, 0)),
        scratch_shapes=[
            pltpu.VMEM((count, 1), jnp.float32),
            pltpu.VMEM((count, HD), jnp.float32),
            pltpu.VMEM((count, 1), jnp.float32),
        ],
    )
    return pl.pallas_call(
        kernel,
        grid_spec=grid_spec,
        out_shape=jax.ShapeDtypeStruct((count, HD), jnp.bfloat16),
        compiler_params=pltpu.CompilerParams(dimension_semantics=("arbitrary",)),
    )(scalars, cache_got, cache_got, new_got, new_got, new_got)


def shards(
    residual_in,
    queries,
    new_keys,
    new_values,
    cache_keys,
    cache_values,
    cached_len,
    rope_offset,
    out_weight,
    gate_weight,
    up_weight,
    down_weight,
    expert_ids,
    gate_share,
):
    req_count = lax.axis_size("req")
    piece_count = lax.axis_size("ep")
    devices = req_count * piece_count
    experts = devices // 2
    groups, piece_rows, _ = queries.shape
    cache_rows = cache_keys.shape[1]
    top_count = expert_ids.shape[2]
    capacity = (piece_rows * top_count + experts - 1) // experts + 1
    piece_index = lax.axis_index("ep")
    splits = piece_count // HEADS
    query_rows = piece_rows // splits

    def by_head(rows):
        return jnp.transpose(rows.reshape(rows.shape[0], HEADS, HD), (1, 0, 2))

    def both_halves(parts):
        joined = jnp.concatenate(parts, 1)
        return jnp.broadcast_to(joined[:, None], (HEADS, splits) + joined.shape[1:]).reshape(
            (piece_count,) + joined.shape[1:]
        )

    q_parts = jnp.transpose(
        queries[0].reshape(splits, query_rows, HEADS, HD), (2, 0, 1, 3)
    ).reshape(piece_count, query_rows, HD)
    sent = jnp.concatenate(
        [
            both_halves(
                [
                    by_head(cache_keys[0]),
                    by_head(cache_values[0]),
                    by_head(new_keys[0]),
                    by_head(new_values[0]),
                ]
            ),
            q_parts,
        ],
        1,
    )
    got = lax.all_to_all(sent, "ep", split_axis=0, concat_axis=0, tiled=True)
    cache_got = got
    new_start = 2 * cache_rows
    source = jnp.arange(piece_count, dtype=jnp.int32)[:, None]
    base = rope_offset[0] + cached_len[0] + source * piece_rows
    key_positions = base + jnp.arange(piece_rows, dtype=jnp.int32)[None, :]
    query_positions = (
        base + (piece_index % splits) * query_rows + jnp.arange(query_rows, dtype=jnp.int32)[None, :]
    )
    new_got = jnp.concatenate(
        [
            rotate_rows(got[:, new_start : new_start + piece_rows], key_positions, 1),
            got[:, new_start + piece_rows : new_start + 2 * piece_rows],
            rotate_rows(got[:, new_start + 2 * piece_rows :], query_positions, 1),
        ],
        1,
    )
    head_out = head_attention_kernel(
        cache_got, new_got, cached_len[0], piece_index % splits, piece_rows, cache_rows
    ).reshape(piece_count, query_rows, HD)
    returned = lax.all_to_all(head_out, "ep", split_axis=0, concat_axis=0, tiled=True)
    attended = jnp.transpose(
        returned.reshape(HEADS, splits, query_rows, HD), (1, 2, 0, 3)
    ).reshape(groups, piece_rows, HEADS * HD)
    hidden = residual_in.astype(jnp.float32) + jnp.einsum(
        "gtc,cd->gtd", attended, out_weight, preferred_element_type=jnp.float32
    )
    inv_root = lax.rsqrt(jnp.mean(hidden * hidden, -1, keepdims=True) + EPS)
    normed = (hidden * inv_root).astype(jnp.bfloat16)
    width = normed.shape[-1]
    rows = normed[0]
    slots = capacity
    ids = expert_ids[0]
    matches = (ids[..., None] == jnp.arange(experts, dtype=jnp.int32)).astype(jnp.int32)
    flat_matches = matches.reshape(piece_rows * top_count, experts)
    earlier = jnp.cumsum(flat_matches, 0) - flat_matches
    slot_index = jnp.sum(earlier * flat_matches, -1).reshape(piece_rows, top_count)
    target = ids * slots + slot_index
    chosen = target[..., None] == jnp.arange(experts * slots, dtype=jnp.int32)
    picked = jnp.any(chosen, 1).reshape(piece_rows, experts, 1, slots)
    weight = jnp.sum(jnp.where(chosen, gate_share[0][..., None], 0.0), 1)
    weight = weight.reshape(piece_rows, experts, slots)
    routed = jnp.zeros((piece_rows, width), jnp.float32)
    lane = 128
    for low, high in ((8, slots), (0, 8)):
        chunk = high - low
        travel = (chunk, width) if chunk % 8 == 0 else (chunk * width // lane, lane)
        chunk_select = picked[..., low:high].astype(jnp.bfloat16)
        if chunk % 8 == 0:
            chunk_select = jnp.broadcast_to(chunk_select, (piece_rows, experts, 2, chunk))
        once = jnp.einsum(
            "teks,tw->eksw", chunk_select, rows, preferred_element_type=jnp.float32
        ).astype(jnp.bfloat16)
        sending = jnp.broadcast_to(
            once.reshape((experts, -1) + travel), (experts, 2) + travel
        ).reshape((devices,) + travel)
        arrived = deliver(sending)
        produced = expert_half(
            arrived.reshape(-1, width), gate_weight[0], up_weight[0], down_weight[0]
        ).reshape((devices,) + travel)
        came_back = collect(produced).reshape((experts, 2) + travel)
        joined = (
            came_back[:, 0].astype(jnp.float32) + came_back[:, 1].astype(jnp.float32)
        ).astype(jnp.bfloat16)
        routed = routed + jnp.dot(
            weight[..., low:high].reshape(piece_rows, experts * chunk),
            joined.reshape(experts * chunk, width).astype(jnp.float32),
            precision=lax.Precision.HIGHEST,
        )
    return (hidden + routed[None]).astype(jnp.bfloat16)


def solution(mesh):
    in_specs = (
        P("req", "ep", None),
        P("req", "ep", None),
        P("req", "ep", None),
        P("req", "ep", None),
        P("req", "ep", None),
        P("req", "ep", None),
        P("req"),
        P("req"),
        P(),
        P(("req", "ep"), None, None),
        P(("req", "ep"), None, None),
        P(("req", "ep"), None, None),
        P("req", "ep", None),
        P("req", "ep", None),
    )
    out_specs = P("req", "ep", None)
    return jax.shard_map(shards, mesh=mesh, in_specs=in_specs, out_specs=out_specs, check_vma=False)
```

```python
import functools

import jax
import jax.numpy as jnp
from jax import lax
from jax.experimental import pallas as pl
from jax.experimental.pallas import tpu as pltpu
from jax.sharding import PartitionSpec as P

HEADS = 8
HD = 128


NEG_FILL = -1e30
EPS = 1e-06
ROPE_BASE = 10000.0


def rotate_rows(values, positions, head_count):
    width_each = values.shape[-1] // head_count
    half_size = width_each // 2
    frequency = ROPE_BASE ** (
        -jnp.arange(half_size, dtype=jnp.int32).astype(jnp.float32) / half_size
    )
    angles = positions.astype(jnp.float32)[..., None] * frequency
    cosine = jnp.cos(angles)[..., None, :]
    sine = jnp.sin(angles)[..., None, :]
    shaped = values.astype(jnp.float32).reshape(values.shape[:-1] + (head_count, width_each))
    lower = shaped[..., :half_size]
    upper = shaped[..., half_size:]
    turned = jnp.concatenate(
        [lower * cosine - upper * sine, lower * sine + upper * cosine], axis=-1
    )
    return turned.reshape(values.shape).astype(jnp.bfloat16)


def block_terms(query_all, cache_k, cache_v, keys_new, values_new, length, cache_start, new_start):
    query_count = query_all.shape[0]
    cache_rows = cache_k.shape[0]
    piece_rows = keys_new.shape[0]
    query_heads = query_all.reshape(query_count, HEADS, HD)
    key_heads = jnp.concatenate([cache_k, keys_new], 0).reshape(-1, HEADS, HD)
    value_heads = jnp.concatenate([cache_v, values_new], 0).reshape(-1, HEADS, HD)
    scores = jnp.einsum(
        "qhd,khd->hqk", query_heads, key_heads, preferred_element_type=jnp.float32
    ) * HD ** (-0.5)
    cache_valid = cache_start + jnp.arange(cache_rows, dtype=jnp.int32) < length
    new_valid = (new_start + jnp.arange(piece_rows, dtype=jnp.int32))[None, :] <= jnp.arange(
        query_count, dtype=jnp.int32
    )[:, None]
    valid = jnp.concatenate(
        [jnp.broadcast_to(cache_valid[None, :], (query_count, cache_rows)), new_valid], 1
    )[None]
    masked = jnp.where(valid, scores, NEG_FILL)
    score_peak = jnp.max(masked, -1)
    weights = jnp.where(valid, jnp.exp(masked - score_peak[..., None]), 0.0)
    weight_sum = jnp.sum(weights, -1)
    mixed = jnp.einsum(
        "hqk,khd->qhd",
        weights.astype(jnp.bfloat16),
        value_heads,
        preferred_element_type=jnp.float32,
    )
    return (mixed, score_peak.T, weight_sum.T)


def expert_half(rows, gate_part, up_part, down_part):
    gate_val = jnp.dot(rows, gate_part, preferred_element_type=jnp.float32)
    up_val = jnp.dot(rows, up_part, preferred_element_type=jnp.float32)
    activation = (jax.nn.silu(gate_val) * up_val).astype(jnp.bfloat16)
    return jnp.dot(activation, down_part, preferred_element_type=jnp.float32).astype(jnp.bfloat16)


def deliver(rows):
    return lax.all_to_all(rows, ("req", "ep"), split_axis=0, concat_axis=0, tiled=True)


def collect(rows):
    return lax.all_to_all(rows, ("req", "ep"), split_axis=0, concat_axis=0, tiled=True)


def head_attention(keys, values, query, length, half_index, piece_rows, cache_rows):
    pieces, query_rows = query.shape[0], query.shape[1]
    block_rows = cache_rows + piece_rows
    query = query.reshape(pieces * query_rows, HD)
    scores = jnp.einsum(
        "qd,bkd->bqk", query, keys, preferred_element_type=jnp.float32
    ) * HD ** (-0.5)
    block = jnp.arange(pieces, dtype=jnp.int32)[:, None, None]
    key_pos = jnp.arange(block_rows, dtype=jnp.int32)[None, None, :]
    query_row = jnp.arange(pieces * query_rows, dtype=jnp.int32)
    query_index = (
        (query_row // query_rows) * piece_rows + half_index * query_rows + query_row % query_rows
    )[None, :, None]
    cache_valid = block * cache_rows + key_pos < length
    new_valid = block * piece_rows + (key_pos - cache_rows) <= query_index
    valid = jnp.where(key_pos < cache_rows, cache_valid, new_valid)
    masked = jnp.where(valid, scores, NEG_FILL)
    score_peak = jnp.max(masked, -1)
    weights = jnp.where(valid, jnp.exp(masked - score_peak[..., None]), 0.0)
    weight_sum = jnp.sum(weights, -1)
    mixed = jnp.einsum(
        "bqk,bkd->bqd",
        weights.astype(jnp.bfloat16),
        values,
        preferred_element_type=jnp.float32,
    )
    peak = jnp.max(score_peak, 0, keepdims=True)
    factor = jnp.exp(score_peak - peak)
    summed = jnp.sum(factor[..., None] * mixed, 0)
    denominator = jnp.sum(factor * weight_sum, 0)
    return (summed / denominator[:, None]).astype(jnp.bfloat16)


def attention_kernel(scalars, kc_ref, vc_ref, kn_ref, vn_ref, q_ref, o_ref, m_scr, acc_scr, den_scr, *, cache_rows, piece_rows, query_rows):
    step = pl.program_id(0)
    length = scalars[0]
    half = scalars[1]
    per_step = kc_ref.shape[0]
    root = HD ** (-0.5)

    @pl.when(step == 0)
    def _():
        m_scr[...] = jnp.full(m_scr.shape, NEG_FILL, jnp.float32)
        acc_scr[...] = jnp.zeros(acc_scr.shape, jnp.float32)
        den_scr[...] = jnp.zeros(den_scr.shape, jnp.float32)

    query = q_ref[...].reshape(-1, HD)
    count = query.shape[0]
    dims = (((1,), (1,)), ((), ()))
    row = lax.broadcasted_iota(jnp.int32, (count, 1), 0)
    query_index = (row // query_rows) * piece_rows + half * query_rows + row % query_rows
    cache_pos = lax.broadcasted_iota(jnp.int32, (1, cache_rows), 1)
    new_pos = lax.broadcasted_iota(jnp.int32, (1, piece_rows), 1)
    for sub in range(per_step):
        block = step * per_step + sub
        s_cache = lax.dot_general(query, kc_ref[sub], dims, preferred_element_type=jnp.float32)
        s_new = lax.dot_general(query, kn_ref[sub], dims, preferred_element_type=jnp.float32)
        cache_bias = jnp.where(block * cache_rows + cache_pos < length, 0.0, NEG_FILL)
        masked_cache = s_cache + cache_bias
        masked_new = jnp.where(block * piece_rows + new_pos <= query_index, s_new, NEG_FILL)
        peak = jnp.maximum(
            jnp.max(masked_cache, axis=1, keepdims=True), jnp.max(masked_new, axis=1, keepdims=True)
        )
        p_cache = jnp.exp((masked_cache - peak) * root)
        p_new = jnp.exp((masked_new - peak) * root)
        total = jnp.sum(p_cache, axis=1, keepdims=True) + jnp.sum(p_new, axis=1, keepdims=True)
        mixed = jnp.dot(
            p_cache.astype(jnp.bfloat16), vc_ref[sub], preferred_element_type=jnp.float32
        ) + jnp.dot(p_new.astype(jnp.bfloat16), vn_ref[sub], preferred_element_type=jnp.float32)
        peak = jnp.where(peak > 0.5 * NEG_FILL, peak * root, NEG_FILL)
        old = m_scr[...]
        top = jnp.maximum(old, peak)
        keep = jnp.exp(old - top)
        scale = jnp.exp(peak - top)
        acc_scr[...] = acc_scr[...] * keep + scale * mixed
        den_scr[...] = den_scr[...] * keep + scale * total
        m_scr[...] = top

    @pl.when(step == pl.num_programs(0) - 1)
    def _():
        o_ref[...] = (acc_scr[...] / den_scr[...]).astype(o_ref.dtype)


def head_attention_kernel(cache_got, new_got, length, half_index, piece_rows, cache_rows):
    pieces = cache_got.shape[0]
    per_step = 4
    query_rows = new_got.shape[1] - 2 * piece_rows
    count = pieces * query_rows
    scalars = jnp.stack([length, half_index]).astype(jnp.int32)
    kernel = functools.partial(attention_kernel, cache_rows=cache_rows, piece_rows=piece_rows, query_rows=query_rows)
    grid_spec = pltpu.PrefetchScalarGridSpec(
        num_scalar_prefetch=1,
        grid=(pieces // per_step,),
        in_specs=[
            pl.BlockSpec((per_step, cache_rows, HD), lambda b, s: (b, 0, 0)),
            pl.BlockSpec((per_step, cache_rows, HD), lambda b, s: (b, 1, 0)),
            pl.BlockSpec((per_step, piece_rows, HD), lambda b, s: (b, 0, 0)),
            pl.BlockSpec((per_step, piece_rows, HD), lambda b, s: (b, 1, 0)),
            pl.BlockSpec((pieces, query_rows, HD), lambda b, s: (0, 2 * piece_rows // query_rows, 0)),
        ],
        out_specs=pl.BlockSpec((count, HD), lambda b, s: (0, 0)),
        scratch_shapes=[
            pltpu.VMEM((count, 1), jnp.float32),
            pltpu.VMEM((count, HD), jnp.float32),
            pltpu.VMEM((count, 1), jnp.float32),
        ],
    )
    return pl.pallas_call(
        kernel,
        grid_spec=grid_spec,
        out_shape=jax.ShapeDtypeStruct((count, HD), jnp.bfloat16),
        compiler_params=pltpu.CompilerParams(dimension_semantics=("arbitrary",)),
    )(scalars, cache_got, cache_got, new_got, new_got, new_got)


def shards(
    residual_in,
    queries,
    new_keys,
    new_values,
    cache_keys,
    cache_values,
    cached_len,
    rope_offset,
    out_weight,
    gate_weight,
    up_weight,
    down_weight,
    expert_ids,
    gate_share,
):
    req_count = lax.axis_size("req")
    piece_count = lax.axis_size("ep")
    devices = req_count * piece_count
    experts = devices // 2
    groups, piece_rows, _ = queries.shape
    cache_rows = cache_keys.shape[1]
    top_count = expert_ids.shape[2]
    capacity = (piece_rows * top_count + experts - 1) // experts + 1
    piece_index = lax.axis_index("ep")
    new_index = piece_index * piece_rows + jnp.arange(piece_rows, dtype=jnp.int32)
    positions = rope_offset[:, None] + cached_len[:, None] + new_index[None, :]
    query_turned = rotate_rows(queries, positions, HEADS)[0]
    key_turned = rotate_rows(new_keys, positions, HEADS)[0]
    splits = piece_count // HEADS
    query_rows = piece_rows // splits

    def by_head(rows):
        return jnp.transpose(rows.reshape(rows.shape[0], HEADS, HD), (1, 0, 2))

    def both_halves(parts):
        joined = jnp.concatenate(parts, 1)
        return jnp.broadcast_to(joined[:, None], (HEADS, splits) + joined.shape[1:]).reshape(
            (piece_count,) + joined.shape[1:]
        )

    cache_sent = both_halves([by_head(cache_keys[0]), by_head(cache_values[0])])
    cache_got = lax.all_to_all(cache_sent, "ep", split_axis=0, concat_axis=0, tiled=True)
    q_parts = jnp.transpose(
        query_turned.reshape(splits, query_rows, HEADS, HD), (2, 0, 1, 3)
    ).reshape(piece_count, query_rows, HD)
    new_sent = jnp.concatenate(
        [both_halves([by_head(key_turned), by_head(new_values[0])]), q_parts], 1
    )
    new_sent, cache_got = lax.optimization_barrier((new_sent, cache_got))
    new_got = lax.all_to_all(new_sent, "ep", split_axis=0, concat_axis=0, tiled=True)
    head_out = head_attention_kernel(
        cache_got, new_got, cached_len[0], piece_index % splits, piece_rows, cache_rows
    ).reshape(piece_count, query_rows, HD)
    returned = lax.all_to_all(head_out, "ep", split_axis=0, concat_axis=0, tiled=True)
    attended = jnp.transpose(
        returned.reshape(HEADS, splits, query_rows, HD), (1, 2, 0, 3)
    ).reshape(groups, piece_rows, HEADS * HD)
    hidden = residual_in.astype(jnp.float32) + jnp.einsum(
        "gtc,cd->gtd", attended, out_weight, preferred_element_type=jnp.float32
    )
    inv_root = lax.rsqrt(jnp.mean(hidden * hidden, -1, keepdims=True) + EPS)
    normed = (hidden * inv_root).astype(jnp.bfloat16)
    width = normed.shape[-1]
    rows = normed[0]
    slots = capacity
    ids = expert_ids[0]
    matches = (ids[..., None] == jnp.arange(experts, dtype=jnp.int32)).astype(jnp.int32)
    flat_matches = matches.reshape(piece_rows * top_count, experts)
    earlier = jnp.cumsum(flat_matches, 0) - flat_matches
    slot_index = jnp.sum(earlier * flat_matches, -1).reshape(piece_rows, top_count)
    target = ids * slots + slot_index
    chosen = target[..., None] == jnp.arange(experts * slots, dtype=jnp.int32)
    picked = jnp.any(chosen, 1).reshape(piece_rows, experts, 1, slots)
    weight = jnp.sum(jnp.where(chosen, gate_share[0][..., None], 0.0), 1)
    weight = weight.reshape(piece_rows, experts, slots)
    routed = jnp.zeros((piece_rows, width), jnp.float32)
    lane = 128
    for low, high in ((8, slots), (0, 8)):
        chunk = high - low
        travel = (chunk, width) if chunk % 8 == 0 else (chunk * width // lane, lane)
        chunk_select = picked[..., low:high].astype(jnp.bfloat16)
        if chunk % 8 == 0:
            chunk_select = jnp.broadcast_to(chunk_select, (piece_rows, experts, 2, chunk))
        once = jnp.einsum(
            "teks,tw->eksw", chunk_select, rows, preferred_element_type=jnp.float32
        ).astype(jnp.bfloat16)
        sending = jnp.broadcast_to(
            once.reshape((experts, -1) + travel), (experts, 2) + travel
        ).reshape((devices,) + travel)
        arrived = deliver(sending)
        produced = expert_half(
            arrived.reshape(-1, width), gate_weight[0], up_weight[0], down_weight[0]
        ).reshape((devices,) + travel)
        came_back = collect(produced).reshape((experts, 2) + travel)
        joined = (
            came_back[:, 0].astype(jnp.float32) + came_back[:, 1].astype(jnp.float32)
        ).astype(jnp.bfloat16)
        share = weight[..., low:high].reshape(piece_rows, experts * chunk)
        high_part = share.astype(jnp.bfloat16)
        low_part = (share - high_part.astype(jnp.float32)).astype(jnp.bfloat16)
        flat = joined.reshape(experts * chunk, width)
        routed = (
            routed
            + jnp.dot(high_part, flat, preferred_element_type=jnp.float32)
            + jnp.dot(low_part, flat, preferred_element_type=jnp.float32)
        )
    return (hidden + routed[None]).astype(jnp.bfloat16)


def solution(mesh):
    in_specs = (
        P("req", "ep", None),
        P("req", "ep", None),
        P("req", "ep", None),
        P("req", "ep", None),
        P("req", "ep", None),
        P("req", "ep", None),
        P("req"),
        P("req"),
        P(),
        P(("req", "ep"), None, None),
        P(("req", "ep"), None, None),
        P(("req", "ep"), None, None),
        P("req", "ep", None),
        P("req", "ep", None),
    )
    out_specs = P("req", "ep", None)
    return jax.shard_map(shards, mesh=mesh, in_specs=in_specs, out_specs=out_specs, check_vma=False)
```

```python
import functools

import jax
import jax.numpy as jnp
from jax import lax
from jax.experimental import pallas as pl
from jax.experimental.pallas import tpu as pltpu
from jax.sharding import PartitionSpec as P

HEADS = 8
HD = 128


NEG_FILL = -1e30
EPS = 1e-06
ROPE_BASE = 10000.0


def rotate_rows(values, positions, head_count):
    width_each = values.shape[-1] // head_count
    half_size = width_each // 2
    frequency = ROPE_BASE ** (
        -jnp.arange(half_size, dtype=jnp.int32).astype(jnp.float32) / half_size
    )
    angles = positions.astype(jnp.float32)[..., None] * frequency
    cosine = jnp.cos(angles)[..., None, :]
    sine = jnp.sin(angles)[..., None, :]
    shaped = values.astype(jnp.float32).reshape(values.shape[:-1] + (head_count, width_each))
    lower = shaped[..., :half_size]
    upper = shaped[..., half_size:]
    turned = jnp.concatenate(
        [lower * cosine - upper * sine, lower * sine + upper * cosine], axis=-1
    )
    return turned.reshape(values.shape).astype(jnp.bfloat16)


def block_terms(query_all, cache_k, cache_v, keys_new, values_new, length, cache_start, new_start):
    query_count = query_all.shape[0]
    cache_rows = cache_k.shape[0]
    piece_rows = keys_new.shape[0]
    query_heads = query_all.reshape(query_count, HEADS, HD)
    key_heads = jnp.concatenate([cache_k, keys_new], 0).reshape(-1, HEADS, HD)
    value_heads = jnp.concatenate([cache_v, values_new], 0).reshape(-1, HEADS, HD)
    scores = jnp.einsum(
        "qhd,khd->hqk", query_heads, key_heads, preferred_element_type=jnp.float32
    ) * HD ** (-0.5)
    cache_valid = cache_start + jnp.arange(cache_rows, dtype=jnp.int32) < length
    new_valid = (new_start + jnp.arange(piece_rows, dtype=jnp.int32))[None, :] <= jnp.arange(
        query_count, dtype=jnp.int32
    )[:, None]
    valid = jnp.concatenate(
        [jnp.broadcast_to(cache_valid[None, :], (query_count, cache_rows)), new_valid], 1
    )[None]
    masked = jnp.where(valid, scores, NEG_FILL)
    score_peak = jnp.max(masked, -1)
    weights = jnp.where(valid, jnp.exp(masked - score_peak[..., None]), 0.0)
    weight_sum = jnp.sum(weights, -1)
    mixed = jnp.einsum(
        "hqk,khd->qhd",
        weights.astype(jnp.bfloat16),
        value_heads,
        preferred_element_type=jnp.float32,
    )
    return (mixed, score_peak.T, weight_sum.T)


def expert_half(rows, gate_part, up_part, down_part):
    gate_val = jnp.dot(rows, gate_part, preferred_element_type=jnp.float32)
    up_val = jnp.dot(rows, up_part, preferred_element_type=jnp.float32)
    activation = (jax.nn.silu(gate_val) * up_val).astype(jnp.bfloat16)
    return jnp.dot(activation, down_part, preferred_element_type=jnp.float32).astype(jnp.bfloat16)


def deliver(rows):
    return lax.all_to_all(rows, ("req", "ep"), split_axis=0, concat_axis=0, tiled=True)


def collect(rows):
    return lax.all_to_all(rows, ("req", "ep"), split_axis=0, concat_axis=0, tiled=True)


def head_attention(keys, values, query, length, half_index, piece_rows, cache_rows):
    pieces, query_rows = query.shape[0], query.shape[1]
    block_rows = cache_rows + piece_rows
    query = query.reshape(pieces * query_rows, HD)
    scores = jnp.einsum(
        "qd,bkd->bqk", query, keys, preferred_element_type=jnp.float32
    ) * HD ** (-0.5)
    block = jnp.arange(pieces, dtype=jnp.int32)[:, None, None]
    key_pos = jnp.arange(block_rows, dtype=jnp.int32)[None, None, :]
    query_row = jnp.arange(pieces * query_rows, dtype=jnp.int32)
    query_index = (
        (query_row // query_rows) * piece_rows + half_index * query_rows + query_row % query_rows
    )[None, :, None]
    cache_valid = block * cache_rows + key_pos < length
    new_valid = block * piece_rows + (key_pos - cache_rows) <= query_index
    valid = jnp.where(key_pos < cache_rows, cache_valid, new_valid)
    masked = jnp.where(valid, scores, NEG_FILL)
    score_peak = jnp.max(masked, -1)
    weights = jnp.where(valid, jnp.exp(masked - score_peak[..., None]), 0.0)
    weight_sum = jnp.sum(weights, -1)
    mixed = jnp.einsum(
        "bqk,bkd->bqd",
        weights.astype(jnp.bfloat16),
        values,
        preferred_element_type=jnp.float32,
    )
    peak = jnp.max(score_peak, 0, keepdims=True)
    factor = jnp.exp(score_peak - peak)
    summed = jnp.sum(factor[..., None] * mixed, 0)
    denominator = jnp.sum(factor * weight_sum, 0)
    return (summed / denominator[:, None]).astype(jnp.bfloat16)


def attention_kernel(scalars, kc_ref, vc_ref, kn_ref, vn_ref, q_ref, o_ref, m_scr, acc_scr, den_scr, *, cache_rows, piece_rows, query_rows):
    step = pl.program_id(0)
    length = scalars[0]
    half = scalars[1]
    per_step = kc_ref.shape[0]
    root = HD ** (-0.5)

    @pl.when(step == 0)
    def _():
        m_scr[...] = jnp.full(m_scr.shape, NEG_FILL, jnp.float32)
        acc_scr[...] = jnp.zeros(acc_scr.shape, jnp.float32)
        den_scr[...] = jnp.zeros(den_scr.shape, jnp.float32)

    query = q_ref[...].reshape(-1, HD)
    count = query.shape[0]
    dims = (((1,), (1,)), ((), ()))
    row = lax.broadcasted_iota(jnp.int32, (count, 1), 0)
    query_index = (row // query_rows) * piece_rows + half * query_rows + row % query_rows
    cache_pos = lax.broadcasted_iota(jnp.int32, (1, cache_rows), 1)
    new_pos = lax.broadcasted_iota(jnp.int32, (1, piece_rows), 1)
    for sub in range(per_step):
        block = step * per_step + sub
        s_cache = lax.dot_general(query, kc_ref[sub], dims, preferred_element_type=jnp.float32)
        s_new = lax.dot_general(query, kn_ref[sub], dims, preferred_element_type=jnp.float32)
        cache_bias = jnp.where(block * cache_rows + cache_pos < length, 0.0, NEG_FILL)
        masked_cache = s_cache + cache_bias
        masked_new = jnp.where(block * piece_rows + new_pos <= query_index, s_new, NEG_FILL)
        peak = jnp.maximum(
            jnp.max(masked_cache, axis=1, keepdims=True), jnp.max(masked_new, axis=1, keepdims=True)
        )
        p_cache = jnp.exp((masked_cache - peak) * root)
        p_new = jnp.exp((masked_new - peak) * root)
        total = jnp.sum(p_cache, axis=1, keepdims=True) + jnp.sum(p_new, axis=1, keepdims=True)
        mixed = jnp.dot(
            p_cache.astype(jnp.bfloat16), vc_ref[sub], preferred_element_type=jnp.float32
        ) + jnp.dot(p_new.astype(jnp.bfloat16), vn_ref[sub], preferred_element_type=jnp.float32)
        peak = jnp.where(peak > 0.5 * NEG_FILL, peak * root, NEG_FILL)
        old = m_scr[...]
        top = jnp.maximum(old, peak)
        keep = jnp.exp(old - top)
        scale = jnp.exp(peak - top)
        acc_scr[...] = acc_scr[...] * keep + scale * mixed
        den_scr[...] = den_scr[...] * keep + scale * total
        m_scr[...] = top

    @pl.when(step == pl.num_programs(0) - 1)
    def _():
        o_ref[...] = (acc_scr[...] / den_scr[...]).astype(o_ref.dtype)


def head_attention_kernel(cache_got, new_got, length, half_index, piece_rows, cache_rows):
    pieces = cache_got.shape[0]
    per_step = 2
    query_rows = new_got.shape[1] - 2 * piece_rows
    count = pieces * query_rows
    scalars = jnp.stack([length, half_index]).astype(jnp.int32)
    kernel = functools.partial(attention_kernel, cache_rows=cache_rows, piece_rows=piece_rows, query_rows=query_rows)
    grid_spec = pltpu.PrefetchScalarGridSpec(
        num_scalar_prefetch=1,
        grid=(pieces // per_step,),
        in_specs=[
            pl.BlockSpec((per_step, cache_rows, HD), lambda b, s: (b, 0, 0)),
            pl.BlockSpec((per_step, cache_rows, HD), lambda b, s: (b, 1, 0)),
            pl.BlockSpec((per_step, piece_rows, HD), lambda b, s: (b, 0, 0)),
            pl.BlockSpec((per_step, piece_rows, HD), lambda b, s: (b, 1, 0)),
            pl.BlockSpec((pieces, query_rows, HD), lambda b, s: (0, 2 * piece_rows // query_rows, 0)),
        ],
        out_specs=pl.BlockSpec((count, HD), lambda b, s: (0, 0)),
        scratch_shapes=[
            pltpu.VMEM((count, 1), jnp.float32),
            pltpu.VMEM((count, HD), jnp.float32),
            pltpu.VMEM((count, 1), jnp.float32),
        ],
    )
    return pl.pallas_call(
        kernel,
        grid_spec=grid_spec,
        out_shape=jax.ShapeDtypeStruct((count, HD), jnp.bfloat16),
        compiler_params=pltpu.CompilerParams(dimension_semantics=("arbitrary",)),
    )(scalars, cache_got, cache_got, new_got, new_got, new_got)


def shards(
    residual_in,
    queries,
    new_keys,
    new_values,
    cache_keys,
    cache_values,
    cached_len,
    rope_offset,
    out_weight,
    gate_weight,
    up_weight,
    down_weight,
    expert_ids,
    gate_share,
):
    req_count = lax.axis_size("req")
    piece_count = lax.axis_size("ep")
    devices = req_count * piece_count
    experts = devices // 2
    groups, piece_rows, _ = queries.shape
    cache_rows = cache_keys.shape[1]
    top_count = expert_ids.shape[2]
    capacity = (piece_rows * top_count + experts - 1) // experts + 1
    piece_index = lax.axis_index("ep")
    new_index = piece_index * piece_rows + jnp.arange(piece_rows, dtype=jnp.int32)
    positions = rope_offset[:, None] + cached_len[:, None] + new_index[None, :]
    query_turned = rotate_rows(queries, positions, HEADS)[0]
    key_turned = rotate_rows(new_keys, positions, HEADS)[0]
    splits = piece_count // HEADS
    query_rows = piece_rows // splits

    def by_head(rows):
        return jnp.transpose(rows.reshape(rows.shape[0], HEADS, HD), (1, 0, 2))

    def both_halves(parts):
        joined = jnp.concatenate(parts, 1)
        return jnp.broadcast_to(joined[:, None], (HEADS, splits) + joined.shape[1:]).reshape(
            (piece_count,) + joined.shape[1:]
        )

    cache_sent = both_halves([by_head(cache_keys[0]), by_head(cache_values[0])])
    cache_got = lax.all_to_all(cache_sent, "ep", split_axis=0, concat_axis=0, tiled=True)
    q_parts = jnp.transpose(
        query_turned.reshape(splits, query_rows, HEADS, HD), (2, 0, 1, 3)
    ).reshape(piece_count, query_rows, HD)
    new_sent = jnp.concatenate(
        [both_halves([by_head(key_turned), by_head(new_values[0])]), q_parts], 1
    )
    new_sent, cache_got = lax.optimization_barrier((new_sent, cache_got))
    new_got = lax.all_to_all(new_sent, "ep", split_axis=0, concat_axis=0, tiled=True)
    head_out = head_attention_kernel(
        cache_got, new_got, cached_len[0], piece_index % splits, piece_rows, cache_rows
    ).reshape(piece_count, query_rows, HD)
    returned = lax.all_to_all(head_out, "ep", split_axis=0, concat_axis=0, tiled=True)
    attended = jnp.transpose(
        returned.reshape(HEADS, splits, query_rows, HD), (1, 2, 0, 3)
    ).reshape(groups, piece_rows, HEADS * HD)
    hidden = residual_in.astype(jnp.float32) + jnp.einsum(
        "gtc,cd->gtd", attended, out_weight, preferred_element_type=jnp.float32
    )
    inv_root = lax.rsqrt(jnp.mean(hidden * hidden, -1, keepdims=True) + EPS)
    normed = (hidden * inv_root).astype(jnp.bfloat16)
    width = normed.shape[-1]
    rows = normed[0]
    slots = capacity
    ids = expert_ids[0]
    matches = (ids[..., None] == jnp.arange(experts, dtype=jnp.int32)).astype(jnp.int32)
    flat_matches = matches.reshape(piece_rows * top_count, experts)
    earlier = jnp.cumsum(flat_matches, 0) - flat_matches
    slot_index = jnp.sum(earlier * flat_matches, -1).reshape(piece_rows, top_count)
    target = ids * slots + slot_index
    chosen = target[..., None] == jnp.arange(experts * slots, dtype=jnp.int32)
    picked = jnp.any(chosen, 1).reshape(piece_rows, experts, 1, slots)
    weight = jnp.sum(jnp.where(chosen, gate_share[0][..., None], 0.0), 1)
    weight = weight.reshape(piece_rows, experts, slots)
    routed = jnp.zeros((piece_rows, width), jnp.float32)
    lane = 128
    previous = None
    for low, high in ((0, 8), (8, slots)):
        chunk = high - low
        travel = (chunk, width) if chunk % 8 == 0 else (chunk * width // lane, lane)
        chunk_select = picked[..., low:high].astype(jnp.bfloat16)
        if chunk % 8 == 0:
            chunk_select = jnp.broadcast_to(chunk_select, (piece_rows, experts, 2, chunk))
        once = jnp.einsum(
            "teks,tw->eksw", chunk_select, rows, preferred_element_type=jnp.float32
        ).astype(jnp.bfloat16)
        sending = jnp.broadcast_to(
            once.reshape((experts, -1) + travel), (experts, 2) + travel
        ).reshape((devices,) + travel)
        if previous is not None:
            sending, previous = lax.optimization_barrier((sending, previous))
        arrived = deliver(sending)
        previous = arrived
        produced = expert_half(
            arrived.reshape(-1, width), gate_weight[0], up_weight[0], down_weight[0]
        ).reshape((devices,) + travel)
        came_back = collect(produced).reshape((experts, 2) + travel)
        joined = (
            came_back[:, 0].astype(jnp.float32) + came_back[:, 1].astype(jnp.float32)
        ).astype(jnp.bfloat16)
        routed = routed + jnp.dot(
            weight[..., low:high].reshape(piece_rows, experts * chunk),
            joined.reshape(experts * chunk, width).astype(jnp.float32),
            precision=lax.Precision.HIGHEST,
        )
    return (hidden + routed[None]).astype(jnp.bfloat16)


def solution(mesh):
    in_specs = (
        P("req", "ep", None),
        P("req", "ep", None),
        P("req", "ep", None),
        P("req", "ep", None),
        P("req", "ep", None),
        P("req", "ep", None),
        P("req"),
        P("req"),
        P(),
        P(("req", "ep"), None, None),
        P(("req", "ep"), None, None),
        P(("req", "ep"), None, None),
        P("req", "ep", None),
        P("req", "ep", None),
    )
    out_specs = P("req", "ep", None)
    return jax.shard_map(shards, mesh=mesh, in_specs=in_specs, out_specs=out_specs, check_vma=False)
```

```python
import functools

import jax
import jax.numpy as jnp
from jax import lax
from jax.experimental import pallas as pl
from jax.experimental.pallas import tpu as pltpu
from jax.sharding import PartitionSpec as P

HEADS = 8
HD = 128


NEG_FILL = -1e30
EPS = 1e-06
ROPE_BASE = 10000.0


def rotate_rows(values, positions, head_count):
    width_each = values.shape[-1] // head_count
    half_size = width_each // 2
    frequency = ROPE_BASE ** (
        -jnp.arange(half_size, dtype=jnp.int32).astype(jnp.float32) / half_size
    )
    angles = positions.astype(jnp.float32)[..., None] * frequency
    cosine = jnp.cos(angles)[..., None, :]
    sine = jnp.sin(angles)[..., None, :]
    shaped = values.astype(jnp.float32).reshape(values.shape[:-1] + (head_count, width_each))
    lower = shaped[..., :half_size]
    upper = shaped[..., half_size:]
    turned = jnp.concatenate(
        [lower * cosine - upper * sine, lower * sine + upper * cosine], axis=-1
    )
    return turned.reshape(values.shape).astype(jnp.bfloat16)


def block_terms(query_all, cache_k, cache_v, keys_new, values_new, length, cache_start, new_start):
    query_count = query_all.shape[0]
    cache_rows = cache_k.shape[0]
    piece_rows = keys_new.shape[0]
    query_heads = query_all.reshape(query_count, HEADS, HD)
    key_heads = jnp.concatenate([cache_k, keys_new], 0).reshape(-1, HEADS, HD)
    value_heads = jnp.concatenate([cache_v, values_new], 0).reshape(-1, HEADS, HD)
    scores = jnp.einsum(
        "qhd,khd->hqk", query_heads, key_heads, preferred_element_type=jnp.float32
    ) * HD ** (-0.5)
    cache_valid = cache_start + jnp.arange(cache_rows, dtype=jnp.int32) < length
    new_valid = (new_start + jnp.arange(piece_rows, dtype=jnp.int32))[None, :] <= jnp.arange(
        query_count, dtype=jnp.int32
    )[:, None]
    valid = jnp.concatenate(
        [jnp.broadcast_to(cache_valid[None, :], (query_count, cache_rows)), new_valid], 1
    )[None]
    masked = jnp.where(valid, scores, NEG_FILL)
    score_peak = jnp.max(masked, -1)
    weights = jnp.where(valid, jnp.exp(masked - score_peak[..., None]), 0.0)
    weight_sum = jnp.sum(weights, -1)
    mixed = jnp.einsum(
        "hqk,khd->qhd",
        weights.astype(jnp.bfloat16),
        value_heads,
        preferred_element_type=jnp.float32,
    )
    return (mixed, score_peak.T, weight_sum.T)


def expert_half(rows, gate_part, up_part, down_part):
    gate_val = jnp.dot(rows, gate_part, preferred_element_type=jnp.float32)
    up_val = jnp.dot(rows, up_part, preferred_element_type=jnp.float32)
    activation = (jax.nn.silu(gate_val) * up_val).astype(jnp.bfloat16)
    return jnp.dot(activation, down_part, preferred_element_type=jnp.float32).astype(jnp.bfloat16)


def deliver(rows):
    return lax.all_to_all(rows, ("req", "ep"), split_axis=0, concat_axis=0, tiled=True)


def collect(rows):
    return lax.all_to_all(rows, ("req", "ep"), split_axis=0, concat_axis=0, tiled=True)


def head_attention(keys, values, query, length, half_index, piece_rows, cache_rows):
    pieces, query_rows = query.shape[0], query.shape[1]
    block_rows = cache_rows + piece_rows
    query = query.reshape(pieces * query_rows, HD)
    scores = jnp.einsum(
        "qd,bkd->bqk", query, keys, preferred_element_type=jnp.float32
    ) * HD ** (-0.5)
    block = jnp.arange(pieces, dtype=jnp.int32)[:, None, None]
    key_pos = jnp.arange(block_rows, dtype=jnp.int32)[None, None, :]
    query_row = jnp.arange(pieces * query_rows, dtype=jnp.int32)
    query_index = (
        (query_row // query_rows) * piece_rows + half_index * query_rows + query_row % query_rows
    )[None, :, None]
    cache_valid = block * cache_rows + key_pos < length
    new_valid = block * piece_rows + (key_pos - cache_rows) <= query_index
    valid = jnp.where(key_pos < cache_rows, cache_valid, new_valid)
    masked = jnp.where(valid, scores, NEG_FILL)
    score_peak = jnp.max(masked, -1)
    weights = jnp.where(valid, jnp.exp(masked - score_peak[..., None]), 0.0)
    weight_sum = jnp.sum(weights, -1)
    mixed = jnp.einsum(
        "bqk,bkd->bqd",
        weights.astype(jnp.bfloat16),
        values,
        preferred_element_type=jnp.float32,
    )
    peak = jnp.max(score_peak, 0, keepdims=True)
    factor = jnp.exp(score_peak - peak)
    summed = jnp.sum(factor[..., None] * mixed, 0)
    denominator = jnp.sum(factor * weight_sum, 0)
    return (summed / denominator[:, None]).astype(jnp.bfloat16)


def attention_kernel(scalars, kc_ref, vc_ref, kn_ref, vn_ref, q_ref, o_ref, m_scr, acc_scr, den_scr, *, cache_rows, piece_rows, query_rows):
    step = pl.program_id(0)
    length = scalars[0]
    half = scalars[1]
    per_step = kc_ref.shape[0]
    root = HD ** (-0.5)

    @pl.when(step == 0)
    def _():
        m_scr[...] = jnp.full(m_scr.shape, NEG_FILL, jnp.float32)
        acc_scr[...] = jnp.zeros(acc_scr.shape, jnp.float32)
        den_scr[...] = jnp.zeros(den_scr.shape, jnp.float32)

    query = q_ref[...].reshape(-1, HD)
    count = query.shape[0]
    dims = (((1,), (1,)), ((), ()))
    row = lax.broadcasted_iota(jnp.int32, (count, 1), 0)
    query_index = (row // query_rows) * piece_rows + half * query_rows + row % query_rows
    cache_pos = lax.broadcasted_iota(jnp.int32, (1, cache_rows), 1)
    new_pos = lax.broadcasted_iota(jnp.int32, (1, piece_rows), 1)
    for sub in range(per_step):
        block = step * per_step + sub
        s_cache = lax.dot_general(query, kc_ref[sub], dims, preferred_element_type=jnp.float32)
        s_new = lax.dot_general(query, kn_ref[sub], dims, preferred_element_type=jnp.float32)
        cache_bias = jnp.where(block * cache_rows + cache_pos < length, 0.0, NEG_FILL)
        masked_cache = s_cache + cache_bias
        masked_new = jnp.where(block * piece_rows + new_pos <= query_index, s_new, NEG_FILL)
        peak = jnp.maximum(
            jnp.max(masked_cache, axis=1, keepdims=True), jnp.max(masked_new, axis=1, keepdims=True)
        )
        p_cache = jnp.exp((masked_cache - peak) * root)
        p_new = jnp.exp((masked_new - peak) * root)
        total = jnp.sum(p_cache, axis=1, keepdims=True) + jnp.sum(p_new, axis=1, keepdims=True)
        mixed = jnp.dot(
            p_cache.astype(jnp.bfloat16), vc_ref[sub], preferred_element_type=jnp.float32
        ) + jnp.dot(p_new.astype(jnp.bfloat16), vn_ref[sub], preferred_element_type=jnp.float32)
        peak = jnp.where(peak > 0.5 * NEG_FILL, peak * root, NEG_FILL)
        old = m_scr[...]
        top = jnp.maximum(old, peak)
        keep = jnp.exp(old - top)
        scale = jnp.exp(peak - top)
        acc_scr[...] = acc_scr[...] * keep + scale * mixed
        den_scr[...] = den_scr[...] * keep + scale * total
        m_scr[...] = top

    @pl.when(step == pl.num_programs(0) - 1)
    def _():
        o_ref[...] = (acc_scr[...] / den_scr[...]).astype(o_ref.dtype)


def head_attention_kernel(cache_got, new_got, length, half_index, piece_rows, cache_rows):
    pieces = cache_got.shape[0]
    per_step = 2
    query_rows = new_got.shape[1] - 2 * piece_rows
    count = pieces * query_rows
    scalars = jnp.stack([length, half_index]).astype(jnp.int32)
    kernel = functools.partial(attention_kernel, cache_rows=cache_rows, piece_rows=piece_rows, query_rows=query_rows)
    grid_spec = pltpu.PrefetchScalarGridSpec(
        num_scalar_prefetch=1,
        grid=(pieces // per_step,),
        in_specs=[
            pl.BlockSpec((per_step, cache_rows, HD), lambda b, s: (b, 0, 0)),
            pl.BlockSpec((per_step, cache_rows, HD), lambda b, s: (b, 1, 0)),
            pl.BlockSpec((per_step, piece_rows, HD), lambda b, s: (b, 0, 0)),
            pl.BlockSpec((per_step, piece_rows, HD), lambda b, s: (b, 1, 0)),
            pl.BlockSpec((pieces, query_rows, HD), lambda b, s: (0, 2 * piece_rows // query_rows, 0)),
        ],
        out_specs=pl.BlockSpec((count, HD), lambda b, s: (0, 0)),
        scratch_shapes=[
            pltpu.VMEM((count, 1), jnp.float32),
            pltpu.VMEM((count, HD), jnp.float32),
            pltpu.VMEM((count, 1), jnp.float32),
        ],
    )
    return pl.pallas_call(
        kernel,
        grid_spec=grid_spec,
        out_shape=jax.ShapeDtypeStruct((count, HD), jnp.bfloat16),
        compiler_params=pltpu.CompilerParams(dimension_semantics=("arbitrary",)),
    )(scalars, cache_got, cache_got, new_got, new_got, new_got)


def shards(
    residual_in,
    queries,
    new_keys,
    new_values,
    cache_keys,
    cache_values,
    cached_len,
    rope_offset,
    out_weight,
    gate_weight,
    up_weight,
    down_weight,
    expert_ids,
    gate_share,
):
    req_count = lax.axis_size("req")
    piece_count = lax.axis_size("ep")
    devices = req_count * piece_count
    experts = devices // 2
    groups, piece_rows, _ = queries.shape
    cache_rows = cache_keys.shape[1]
    top_count = expert_ids.shape[2]
    capacity = (piece_rows * top_count + experts - 1) // experts + 1
    piece_index = lax.axis_index("ep")
    new_index = piece_index * piece_rows + jnp.arange(piece_rows, dtype=jnp.int32)
    positions = rope_offset[:, None] + cached_len[:, None] + new_index[None, :]
    query_turned = rotate_rows(queries, positions, HEADS)[0]
    key_turned = rotate_rows(new_keys, positions, HEADS)[0]
    splits = piece_count // HEADS
    query_rows = piece_rows // splits

    def by_head(rows):
        return jnp.transpose(rows.reshape(rows.shape[0], HEADS, HD), (1, 0, 2))

    def both_halves(parts):
        joined = jnp.concatenate(parts, 1)
        return jnp.broadcast_to(joined[:, None], (HEADS, splits) + joined.shape[1:]).reshape(
            (piece_count,) + joined.shape[1:]
        )

    cache_sent = both_halves([by_head(cache_keys[0]), by_head(cache_values[0])])
    cache_got = lax.all_to_all(cache_sent, "ep", split_axis=0, concat_axis=0, tiled=True)
    q_parts = jnp.transpose(
        query_turned.reshape(splits, query_rows, HEADS, HD), (2, 0, 1, 3)
    ).reshape(piece_count, query_rows, HD)
    new_sent = jnp.concatenate(
        [both_halves([by_head(key_turned), by_head(new_values[0])]), q_parts], 1
    )
    new_sent, cache_got = lax.optimization_barrier((new_sent, cache_got))
    new_got = lax.all_to_all(new_sent, "ep", split_axis=0, concat_axis=0, tiled=True)
    head_out = head_attention_kernel(
        cache_got, new_got, cached_len[0], piece_index % splits, piece_rows, cache_rows
    ).reshape(piece_count, query_rows, HD)
    returned = lax.all_to_all(head_out, "ep", split_axis=0, concat_axis=0, tiled=True)
    attended = jnp.transpose(
        returned.reshape(HEADS, splits, query_rows, HD), (1, 2, 0, 3)
    ).reshape(groups, piece_rows, HEADS * HD)
    hidden = residual_in.astype(jnp.float32) + jnp.einsum(
        "gtc,cd->gtd", attended, out_weight, preferred_element_type=jnp.float32
    )
    inv_root = lax.rsqrt(jnp.mean(hidden * hidden, -1, keepdims=True) + EPS)
    normed = (hidden * inv_root).astype(jnp.bfloat16)
    width = normed.shape[-1]
    rows = normed[0]
    slots = capacity
    ids = expert_ids[0]
    matches = (ids[..., None] == jnp.arange(experts, dtype=jnp.int32)).astype(jnp.int32)
    flat_matches = matches.reshape(piece_rows * top_count, experts)
    earlier = jnp.cumsum(flat_matches, 0) - flat_matches
    slot_index = jnp.sum(earlier * flat_matches, -1).reshape(piece_rows, top_count)
    target = ids * slots + slot_index
    chosen = target[..., None] == jnp.arange(experts * slots, dtype=jnp.int32)
    picked = jnp.any(chosen, 1).reshape(piece_rows, experts, 1, slots)
    weight = jnp.sum(jnp.where(chosen, gate_share[0][..., None], 0.0), 1)
    weight = weight.reshape(piece_rows, experts, slots)
    routed = jnp.zeros((piece_rows, width), jnp.float32)
    lane = 128
    previous = None
    for low, high in ((0, 8), (8, slots)):
        chunk = high - low
        travel = (chunk, width) if chunk % 8 == 0 else (chunk * width // lane, lane)
        chunk_select = picked[..., low:high].astype(jnp.bfloat16)
        chunk_select = jnp.broadcast_to(chunk_select, (piece_rows, experts, 2, chunk))
        once = jnp.einsum(
            "teks,tw->eksw", chunk_select, rows, preferred_element_type=jnp.float32
        ).astype(jnp.bfloat16)
        sending = jnp.broadcast_to(
            once.reshape((experts, -1) + travel), (experts, 2) + travel
        ).reshape((devices,) + travel)
        if previous is not None:
            sending, previous = lax.optimization_barrier((sending, previous))
        arrived = deliver(sending)
        previous = arrived
        produced = expert_half(
            arrived.reshape(-1, width), gate_weight[0], up_weight[0], down_weight[0]
        ).reshape((devices,) + travel)
        came_back = collect(produced).reshape((experts, 2) + travel)
        joined = (
            came_back[:, 0].astype(jnp.float32) + came_back[:, 1].astype(jnp.float32)
        ).astype(jnp.bfloat16)
        routed = routed + jnp.dot(
            weight[..., low:high].reshape(piece_rows, experts * chunk),
            joined.reshape(experts * chunk, width).astype(jnp.float32),
            precision=lax.Precision.HIGHEST,
        )
    return (hidden + routed[None]).astype(jnp.bfloat16)


def solution(mesh):
    in_specs = (
        P("req", "ep", None),
        P("req", "ep", None),
        P("req", "ep", None),
        P("req", "ep", None),
        P("req", "ep", None),
        P("req", "ep", None),
        P("req"),
        P("req"),
        P(),
        P(("req", "ep"), None, None),
        P(("req", "ep"), None, None),
        P(("req", "ep"), None, None),
        P("req", "ep", None),
        P("req", "ep", None),
    )
    out_specs = P("req", "ep", None)
    return jax.shard_map(shards, mesh=mesh, in_specs=in_specs, out_specs=out_specs, check_vma=False)
```

```python
import functools

import jax
import jax.numpy as jnp
from jax import lax
from jax.experimental import pallas as pl
from jax.experimental.pallas import tpu as pltpu
from jax.sharding import PartitionSpec as P

HEADS = 8
HD = 128


NEG_FILL = -1e30
EPS = 1e-06
ROPE_BASE = 10000.0


def rotate_rows(values, positions, head_count):
    width_each = values.shape[-1] // head_count
    half_size = width_each // 2
    frequency = ROPE_BASE ** (
        -jnp.arange(half_size, dtype=jnp.int32).astype(jnp.float32) / half_size
    )
    angles = positions.astype(jnp.float32)[..., None] * frequency
    cosine = jnp.cos(angles)[..., None, :]
    sine = jnp.sin(angles)[..., None, :]
    shaped = values.astype(jnp.float32).reshape(values.shape[:-1] + (head_count, width_each))
    lower = shaped[..., :half_size]
    upper = shaped[..., half_size:]
    turned = jnp.concatenate(
        [lower * cosine - upper * sine, lower * sine + upper * cosine], axis=-1
    )
    return turned.reshape(values.shape).astype(jnp.bfloat16)


def block_terms(query_all, cache_k, cache_v, keys_new, values_new, length, cache_start, new_start):
    query_count = query_all.shape[0]
    cache_rows = cache_k.shape[0]
    piece_rows = keys_new.shape[0]
    query_heads = query_all.reshape(query_count, HEADS, HD)
    key_heads = jnp.concatenate([cache_k, keys_new], 0).reshape(-1, HEADS, HD)
    value_heads = jnp.concatenate([cache_v, values_new], 0).reshape(-1, HEADS, HD)
    scores = jnp.einsum(
        "qhd,khd->hqk", query_heads, key_heads, preferred_element_type=jnp.float32
    ) * HD ** (-0.5)
    cache_valid = cache_start + jnp.arange(cache_rows, dtype=jnp.int32) < length
    new_valid = (new_start + jnp.arange(piece_rows, dtype=jnp.int32))[None, :] <= jnp.arange(
        query_count, dtype=jnp.int32
    )[:, None]
    valid = jnp.concatenate(
        [jnp.broadcast_to(cache_valid[None, :], (query_count, cache_rows)), new_valid], 1
    )[None]
    masked = jnp.where(valid, scores, NEG_FILL)
    score_peak = jnp.max(masked, -1)
    weights = jnp.where(valid, jnp.exp(masked - score_peak[..., None]), 0.0)
    weight_sum = jnp.sum(weights, -1)
    mixed = jnp.einsum(
        "hqk,khd->qhd",
        weights.astype(jnp.bfloat16),
        value_heads,
        preferred_element_type=jnp.float32,
    )
    return (mixed, score_peak.T, weight_sum.T)


def expert_half(rows, gate_part, up_part, down_part):
    gate_val = jnp.dot(rows, gate_part, preferred_element_type=jnp.float32)
    up_val = jnp.dot(rows, up_part, preferred_element_type=jnp.float32)
    activation = (jax.nn.silu(gate_val) * up_val).astype(jnp.bfloat16)
    return jnp.dot(activation, down_part, preferred_element_type=jnp.float32).astype(jnp.bfloat16)


def deliver(rows):
    return lax.all_to_all(rows, ("req", "ep"), split_axis=0, concat_axis=0, tiled=True)


def collect(rows):
    return lax.all_to_all(rows, ("req", "ep"), split_axis=0, concat_axis=0, tiled=True)


def head_attention(keys, values, query, length, half_index, piece_rows, cache_rows):
    pieces, query_rows = query.shape[0], query.shape[1]
    block_rows = cache_rows + piece_rows
    query = query.reshape(pieces * query_rows, HD)
    scores = jnp.einsum(
        "qd,bkd->bqk", query, keys, preferred_element_type=jnp.float32
    ) * HD ** (-0.5)
    block = jnp.arange(pieces, dtype=jnp.int32)[:, None, None]
    key_pos = jnp.arange(block_rows, dtype=jnp.int32)[None, None, :]
    query_row = jnp.arange(pieces * query_rows, dtype=jnp.int32)
    query_index = (
        (query_row // query_rows) * piece_rows + half_index * query_rows + query_row % query_rows
    )[None, :, None]
    cache_valid = block * cache_rows + key_pos < length
    new_valid = block * piece_rows + (key_pos - cache_rows) <= query_index
    valid = jnp.where(key_pos < cache_rows, cache_valid, new_valid)
    masked = jnp.where(valid, scores, NEG_FILL)
    score_peak = jnp.max(masked, -1)
    weights = jnp.where(valid, jnp.exp(masked - score_peak[..., None]), 0.0)
    weight_sum = jnp.sum(weights, -1)
    mixed = jnp.einsum(
        "bqk,bkd->bqd",
        weights.astype(jnp.bfloat16),
        values,
        preferred_element_type=jnp.float32,
    )
    peak = jnp.max(score_peak, 0, keepdims=True)
    factor = jnp.exp(score_peak - peak)
    summed = jnp.sum(factor[..., None] * mixed, 0)
    denominator = jnp.sum(factor * weight_sum, 0)
    return (summed / denominator[:, None]).astype(jnp.bfloat16)


def attention_kernel(scalars, kc_ref, vc_ref, kn_ref, vn_ref, q_ref, o_ref, m_scr, acc_scr, den_scr, *, cache_rows, piece_rows, query_rows):
    step = pl.program_id(0)
    length = scalars[0]
    half = scalars[1]
    per_step = kc_ref.shape[0]
    root = HD ** (-0.5)

    @pl.when(step == 0)
    def _():
        m_scr[...] = jnp.full(m_scr.shape, NEG_FILL, jnp.float32)
        acc_scr[...] = jnp.zeros(acc_scr.shape, jnp.float32)
        den_scr[...] = jnp.zeros(den_scr.shape, jnp.float32)

    query = q_ref[...].reshape(-1, HD)
    count = query.shape[0]
    dims = (((1,), (1,)), ((), ()))
    row = lax.broadcasted_iota(jnp.int32, (count, 1), 0)
    query_index = (row // query_rows) * piece_rows + half * query_rows + row % query_rows
    cache_pos = lax.broadcasted_iota(jnp.int32, (1, cache_rows), 1)
    new_pos = lax.broadcasted_iota(jnp.int32, (1, piece_rows), 1)
    for sub in range(per_step):
        block = step * per_step + sub
        s_cache = lax.dot_general(query, kc_ref[sub], dims, preferred_element_type=jnp.float32)
        s_new = lax.dot_general(query, kn_ref[sub], dims, preferred_element_type=jnp.float32)
        cache_bias = jnp.where(block * cache_rows + cache_pos < length, 0.0, NEG_FILL)
        masked_cache = s_cache + cache_bias
        masked_new = jnp.where(block * piece_rows + new_pos <= query_index, s_new, NEG_FILL)
        peak = jnp.maximum(
            jnp.max(masked_cache, axis=1, keepdims=True), jnp.max(masked_new, axis=1, keepdims=True)
        )
        p_cache = jnp.exp((masked_cache - peak) * root)
        p_new = jnp.exp((masked_new - peak) * root)
        total = jnp.sum(p_cache, axis=1, keepdims=True) + jnp.sum(p_new, axis=1, keepdims=True)
        mixed = jnp.dot(
            p_cache.astype(jnp.bfloat16), vc_ref[sub], preferred_element_type=jnp.float32
        ) + jnp.dot(p_new.astype(jnp.bfloat16), vn_ref[sub], preferred_element_type=jnp.float32)
        peak = jnp.where(peak > 0.5 * NEG_FILL, peak * root, NEG_FILL)
        old = m_scr[...]
        top = jnp.maximum(old, peak)
        keep = jnp.exp(old - top)
        scale = jnp.exp(peak - top)
        acc_scr[...] = acc_scr[...] * keep + scale * mixed
        den_scr[...] = den_scr[...] * keep + scale * total
        m_scr[...] = top

    @pl.when(step == pl.num_programs(0) - 1)
    def _():
        o_ref[...] = (acc_scr[...] / den_scr[...]).astype(o_ref.dtype)


def head_attention_kernel(cache_got, new_got, length, half_index, piece_rows, cache_rows):
    pieces = cache_got.shape[0]
    per_step = 4
    query_rows = new_got.shape[1] - 2 * piece_rows
    count = pieces * query_rows
    scalars = jnp.stack([length, half_index]).astype(jnp.int32)
    kernel = functools.partial(attention_kernel, cache_rows=cache_rows, piece_rows=piece_rows, query_rows=query_rows)
    grid_spec = pltpu.PrefetchScalarGridSpec(
        num_scalar_prefetch=1,
        grid=(pieces // per_step,),
        in_specs=[
            pl.BlockSpec((per_step, cache_rows, HD), lambda b, s: (b, 0, 0)),
            pl.BlockSpec((per_step, cache_rows, HD), lambda b, s: (b, 1, 0)),
            pl.BlockSpec((per_step, piece_rows, HD), lambda b, s: (b, 0, 0)),
            pl.BlockSpec((per_step, piece_rows, HD), lambda b, s: (b, 1, 0)),
            pl.BlockSpec((pieces, query_rows, HD), lambda b, s: (0, 2 * piece_rows // query_rows, 0)),
        ],
        out_specs=pl.BlockSpec((count, HD), lambda b, s: (0, 0)),
        scratch_shapes=[
            pltpu.VMEM((count, 1), jnp.float32),
            pltpu.VMEM((count, HD), jnp.float32),
            pltpu.VMEM((count, 1), jnp.float32),
        ],
    )
    return pl.pallas_call(
        kernel,
        grid_spec=grid_spec,
        out_shape=jax.ShapeDtypeStruct((count, HD), jnp.bfloat16),
        compiler_params=pltpu.CompilerParams(dimension_semantics=("arbitrary",)),
    )(scalars, cache_got, cache_got, new_got, new_got, new_got)


def shards(
    residual_in,
    queries,
    new_keys,
    new_values,
    cache_keys,
    cache_values,
    cached_len,
    rope_offset,
    out_weight,
    gate_weight,
    up_weight,
    down_weight,
    expert_ids,
    gate_share,
):
    req_count = lax.axis_size("req")
    piece_count = lax.axis_size("ep")
    devices = req_count * piece_count
    experts = devices // 2
    groups, piece_rows, _ = queries.shape
    cache_rows = cache_keys.shape[1]
    top_count = expert_ids.shape[2]
    capacity = (piece_rows * top_count + experts - 1) // experts + 1
    piece_index = lax.axis_index("ep")
    new_index = piece_index * piece_rows + jnp.arange(piece_rows, dtype=jnp.int32)
    positions = rope_offset[:, None] + cached_len[:, None] + new_index[None, :]
    query_turned = rotate_rows(queries, positions, HEADS)[0]
    key_turned = rotate_rows(new_keys, positions, HEADS)[0]
    splits = piece_count // HEADS
    query_rows = piece_rows // splits

    def by_head(rows):
        return jnp.transpose(rows.reshape(rows.shape[0], HEADS, HD), (1, 0, 2))

    def both_halves(parts):
        joined = jnp.concatenate(parts, 1)
        return jnp.broadcast_to(joined[:, None], (HEADS, splits) + joined.shape[1:]).reshape(
            (piece_count,) + joined.shape[1:]
        )

    cache_sent = both_halves([by_head(cache_keys[0]), by_head(cache_values[0])])
    cache_got = lax.all_to_all(cache_sent, "ep", split_axis=0, concat_axis=0, tiled=True)
    q_parts = jnp.transpose(
        query_turned.reshape(splits, query_rows, HEADS, HD), (2, 0, 1, 3)
    ).reshape(piece_count, query_rows, HD)
    new_sent = jnp.concatenate(
        [both_halves([by_head(key_turned), by_head(new_values[0])]), q_parts], 1
    )
    new_sent, cache_got = lax.optimization_barrier((new_sent, cache_got))
    new_got = lax.all_to_all(new_sent, "ep", split_axis=0, concat_axis=0, tiled=True)
    head_out = head_attention_kernel(
        cache_got, new_got, cached_len[0], piece_index % splits, piece_rows, cache_rows
    ).reshape(piece_count, query_rows, HD)
    returned = lax.all_to_all(head_out, "ep", split_axis=0, concat_axis=0, tiled=True)
    attended = jnp.transpose(
        returned.reshape(HEADS, splits, query_rows, HD), (1, 2, 0, 3)
    ).reshape(groups, piece_rows, HEADS * HD)
    hidden = residual_in.astype(jnp.float32) + jnp.einsum(
        "gtc,cd->gtd", attended, out_weight, preferred_element_type=jnp.float32
    )
    inv_root = lax.rsqrt(jnp.mean(hidden * hidden, -1, keepdims=True) + EPS)
    normed = (hidden * inv_root).astype(jnp.bfloat16)
    width = normed.shape[-1]
    rows = normed[0]
    slots = capacity
    ids = expert_ids[0]
    matches = (ids[..., None] == jnp.arange(experts, dtype=jnp.int32)).astype(jnp.int32)
    flat_matches = matches.reshape(piece_rows * top_count, experts)
    earlier = jnp.cumsum(flat_matches, 0) - flat_matches
    slot_index = jnp.sum(earlier * flat_matches, -1).reshape(piece_rows, top_count)
    target = ids * slots + slot_index
    chosen = target[..., None] == jnp.arange(experts * slots, dtype=jnp.int32)
    picked = jnp.any(chosen, 1).reshape(piece_rows, experts, 1, slots)
    weight = jnp.sum(jnp.where(chosen, gate_share[0][..., None], 0.0), 1)
    weight = weight.reshape(piece_rows, experts, slots)
    routed = jnp.zeros((piece_rows, width), jnp.float32)
    lane = 128
    previous = None
    for low, high in ((0, 8), (8, slots)):
        chunk = high - low
        travel = (chunk, width) if chunk % 8 == 0 else (chunk * width // lane, lane)
        chunk_select = picked[..., low:high].astype(jnp.bfloat16)
        chunk_select = jnp.broadcast_to(chunk_select, (piece_rows, experts, 2, chunk))
        once = jnp.einsum(
            "teks,tw->eksw", chunk_select, rows, preferred_element_type=jnp.float32
        ).astype(jnp.bfloat16)
        sending = jnp.broadcast_to(
            once.reshape((experts, -1) + travel), (experts, 2) + travel
        ).reshape((devices,) + travel)
        if previous is not None:
            sending, previous = lax.optimization_barrier((sending, previous))
        arrived = deliver(sending)
        previous = arrived
        produced = expert_half(
            arrived.reshape(-1, width), gate_weight[0], up_weight[0], down_weight[0]
        ).reshape((devices,) + travel)
        came_back = collect(produced).reshape((experts, 2) + travel)
        joined = (
            came_back[:, 0].astype(jnp.float32) + came_back[:, 1].astype(jnp.float32)
        ).astype(jnp.bfloat16)
        routed = routed + jnp.dot(
            weight[..., low:high].reshape(piece_rows, experts * chunk),
            joined.reshape(experts * chunk, width).astype(jnp.float32),
            precision=lax.Precision.HIGHEST,
        )
    return (hidden + routed[None]).astype(jnp.bfloat16)


def solution(mesh):
    in_specs = (
        P("req", "ep", None),
        P("req", "ep", None),
        P("req", "ep", None),
        P("req", "ep", None),
        P("req", "ep", None),
        P("req", "ep", None),
        P("req"),
        P("req"),
        P(),
        P(("req", "ep"), None, None),
        P(("req", "ep"), None, None),
        P(("req", "ep"), None, None),
        P("req", "ep", None),
        P("req", "ep", None),
    )
    out_specs = P("req", "ep", None)
    return jax.shard_map(shards, mesh=mesh, in_specs=in_specs, out_specs=out_specs, check_vma=False)
```

```python
import functools

import jax
import jax.numpy as jnp
from jax import lax
from jax.experimental import pallas as pl
from jax.experimental.pallas import tpu as pltpu
from jax.sharding import PartitionSpec as P

HEADS = 8
HD = 128


NEG_FILL = -1e30
EPS = 1e-06
ROPE_BASE = 10000.0


def rotate_rows(values, positions, head_count):
    width_each = values.shape[-1] // head_count
    half_size = width_each // 2
    frequency = ROPE_BASE ** (
        -jnp.arange(half_size, dtype=jnp.int32).astype(jnp.float32) / half_size
    )
    angles = positions.astype(jnp.float32)[..., None] * frequency
    cosine = jnp.cos(angles)[..., None, :]
    sine = jnp.sin(angles)[..., None, :]
    shaped = values.astype(jnp.float32).reshape(values.shape[:-1] + (head_count, width_each))
    lower = shaped[..., :half_size]
    upper = shaped[..., half_size:]
    turned = jnp.concatenate(
        [lower * cosine - upper * sine, lower * sine + upper * cosine], axis=-1
    )
    return turned.reshape(values.shape).astype(jnp.bfloat16)


def block_terms(query_all, cache_k, cache_v, keys_new, values_new, length, cache_start, new_start):
    query_count = query_all.shape[0]
    cache_rows = cache_k.shape[0]
    piece_rows = keys_new.shape[0]
    query_heads = query_all.reshape(query_count, HEADS, HD)
    key_heads = jnp.concatenate([cache_k, keys_new], 0).reshape(-1, HEADS, HD)
    value_heads = jnp.concatenate([cache_v, values_new], 0).reshape(-1, HEADS, HD)
    scores = jnp.einsum(
        "qhd,khd->hqk", query_heads, key_heads, preferred_element_type=jnp.float32
    ) * HD ** (-0.5)
    cache_valid = cache_start + jnp.arange(cache_rows, dtype=jnp.int32) < length
    new_valid = (new_start + jnp.arange(piece_rows, dtype=jnp.int32))[None, :] <= jnp.arange(
        query_count, dtype=jnp.int32
    )[:, None]
    valid = jnp.concatenate(
        [jnp.broadcast_to(cache_valid[None, :], (query_count, cache_rows)), new_valid], 1
    )[None]
    masked = jnp.where(valid, scores, NEG_FILL)
    score_peak = jnp.max(masked, -1)
    weights = jnp.where(valid, jnp.exp(masked - score_peak[..., None]), 0.0)
    weight_sum = jnp.sum(weights, -1)
    mixed = jnp.einsum(
        "hqk,khd->qhd",
        weights.astype(jnp.bfloat16),
        value_heads,
        preferred_element_type=jnp.float32,
    )
    return (mixed, score_peak.T, weight_sum.T)


def expert_half(rows, gate_part, up_part, down_part):
    gate_val = jnp.dot(rows, gate_part, preferred_element_type=jnp.float32)
    up_val = jnp.dot(rows, up_part, preferred_element_type=jnp.float32)
    activation = (jax.nn.silu(gate_val) * up_val).astype(jnp.bfloat16)
    return jnp.dot(activation, down_part, preferred_element_type=jnp.float32).astype(jnp.bfloat16)


def deliver(rows):
    return lax.all_to_all(rows, ("req", "ep"), split_axis=0, concat_axis=0, tiled=True)


def collect(rows):
    return lax.all_to_all(rows, ("req", "ep"), split_axis=0, concat_axis=0, tiled=True)


def head_attention(keys, values, query, length, half_index, piece_rows, cache_rows):
    pieces, query_rows = query.shape[0], query.shape[1]
    block_rows = cache_rows + piece_rows
    query = query.reshape(pieces * query_rows, HD)
    scores = jnp.einsum(
        "qd,bkd->bqk", query, keys, preferred_element_type=jnp.float32
    ) * HD ** (-0.5)
    block = jnp.arange(pieces, dtype=jnp.int32)[:, None, None]
    key_pos = jnp.arange(block_rows, dtype=jnp.int32)[None, None, :]
    query_row = jnp.arange(pieces * query_rows, dtype=jnp.int32)
    query_index = (
        (query_row // query_rows) * piece_rows + half_index * query_rows + query_row % query_rows
    )[None, :, None]
    cache_valid = block * cache_rows + key_pos < length
    new_valid = block * piece_rows + (key_pos - cache_rows) <= query_index
    valid = jnp.where(key_pos < cache_rows, cache_valid, new_valid)
    masked = jnp.where(valid, scores, NEG_FILL)
    score_peak = jnp.max(masked, -1)
    weights = jnp.where(valid, jnp.exp(masked - score_peak[..., None]), 0.0)
    weight_sum = jnp.sum(weights, -1)
    mixed = jnp.einsum(
        "bqk,bkd->bqd",
        weights.astype(jnp.bfloat16),
        values,
        preferred_element_type=jnp.float32,
    )
    peak = jnp.max(score_peak, 0, keepdims=True)
    factor = jnp.exp(score_peak - peak)
    summed = jnp.sum(factor[..., None] * mixed, 0)
    denominator = jnp.sum(factor * weight_sum, 0)
    return (summed / denominator[:, None]).astype(jnp.bfloat16)


def attention_kernel(scalars, kc_ref, vc_ref, kn_ref, vn_ref, q_ref, o_ref, m_scr, acc_scr, den_scr, *, cache_rows, piece_rows, query_rows):
    step = pl.program_id(0)
    length = scalars[0]
    half = scalars[1]
    per_step = kc_ref.shape[0]
    root = HD ** (-0.5)

    @pl.when(step == 0)
    def _():
        m_scr[...] = jnp.full(m_scr.shape, NEG_FILL, jnp.float32)
        acc_scr[...] = jnp.zeros(acc_scr.shape, jnp.float32)
        den_scr[...] = jnp.zeros(den_scr.shape, jnp.float32)

    query = q_ref[...].reshape(-1, HD)
    count = query.shape[0]
    dims = (((1,), (1,)), ((), ()))
    row = lax.broadcasted_iota(jnp.int32, (count, 1), 0)
    query_index = (row // query_rows) * piece_rows + half * query_rows + row % query_rows
    cache_pos = lax.broadcasted_iota(jnp.int32, (1, cache_rows), 1)
    new_pos = lax.broadcasted_iota(jnp.int32, (1, piece_rows), 1)
    for sub in range(per_step):
        block = step * per_step + sub
        s_cache = lax.dot_general(query, kc_ref[sub], dims, preferred_element_type=jnp.float32)
        s_new = lax.dot_general(query, kn_ref[sub], dims, preferred_element_type=jnp.float32)
        cache_bias = jnp.where(block * cache_rows + cache_pos < length, 0.0, NEG_FILL)
        masked_cache = s_cache + cache_bias
        masked_new = jnp.where(block * piece_rows + new_pos <= query_index, s_new, NEG_FILL)
        peak = jnp.maximum(
            jnp.max(masked_cache, axis=1, keepdims=True), jnp.max(masked_new, axis=1, keepdims=True)
        )
        p_cache = jnp.exp((masked_cache - peak) * root)
        p_new = jnp.exp((masked_new - peak) * root)
        total = jnp.sum(p_cache, axis=1, keepdims=True) + jnp.sum(p_new, axis=1, keepdims=True)
        mixed = jnp.dot(
            p_cache.astype(jnp.bfloat16), vc_ref[sub], preferred_element_type=jnp.float32
        ) + jnp.dot(p_new.astype(jnp.bfloat16), vn_ref[sub], preferred_element_type=jnp.float32)
        peak = jnp.where(peak > 0.5 * NEG_FILL, peak * root, NEG_FILL)
        old = m_scr[...]
        top = jnp.maximum(old, peak)
        keep = jnp.exp(old - top)
        scale = jnp.exp(peak - top)
        acc_scr[...] = acc_scr[...] * keep + scale * mixed
        den_scr[...] = den_scr[...] * keep + scale * total
        m_scr[...] = top

    @pl.when(step == pl.num_programs(0) - 1)
    def _():
        o_ref[...] = (acc_scr[...] / den_scr[...]).astype(o_ref.dtype)


def head_attention_kernel(cache_got, new_got, length, half_index, piece_rows, cache_rows):
    pieces = cache_got.shape[0]
    per_step = 2
    query_rows = new_got.shape[1] - 2 * piece_rows
    count = pieces * query_rows
    scalars = jnp.stack([length, half_index]).astype(jnp.int32)
    kernel = functools.partial(attention_kernel, cache_rows=cache_rows, piece_rows=piece_rows, query_rows=query_rows)
    grid_spec = pltpu.PrefetchScalarGridSpec(
        num_scalar_prefetch=1,
        grid=(pieces // per_step,),
        in_specs=[
            pl.BlockSpec((per_step, cache_rows, HD), lambda b, s: (b, 0, 0)),
            pl.BlockSpec((per_step, cache_rows, HD), lambda b, s: (b, 1, 0)),
            pl.BlockSpec((per_step, piece_rows, HD), lambda b, s: (b, 0, 0)),
            pl.BlockSpec((per_step, piece_rows, HD), lambda b, s: (b, 1, 0)),
            pl.BlockSpec((pieces, query_rows, HD), lambda b, s: (0, 2 * piece_rows // query_rows, 0)),
        ],
        out_specs=pl.BlockSpec((count, HD), lambda b, s: (0, 0)),
        scratch_shapes=[
            pltpu.VMEM((count, 1), jnp.float32),
            pltpu.VMEM((count, HD), jnp.float32),
            pltpu.VMEM((count, 1), jnp.float32),
        ],
    )
    return pl.pallas_call(
        kernel,
        grid_spec=grid_spec,
        out_shape=jax.ShapeDtypeStruct((count, HD), jnp.bfloat16),
        compiler_params=pltpu.CompilerParams(dimension_semantics=("arbitrary",)),
    )(scalars, cache_got, cache_got, new_got, new_got, new_got)


def shards(
    residual_in,
    queries,
    new_keys,
    new_values,
    cache_keys,
    cache_values,
    cached_len,
    rope_offset,
    out_weight,
    gate_weight,
    up_weight,
    down_weight,
    expert_ids,
    gate_share,
):
    req_count = lax.axis_size("req")
    piece_count = lax.axis_size("ep")
    devices = req_count * piece_count
    experts = devices // 2
    groups, piece_rows, _ = queries.shape
    cache_rows = cache_keys.shape[1]
    top_count = expert_ids.shape[2]
    capacity = (piece_rows * top_count + experts - 1) // experts + 1
    piece_index = lax.axis_index("ep")
    new_index = piece_index * piece_rows + jnp.arange(piece_rows, dtype=jnp.int32)
    positions = rope_offset[:, None] + cached_len[:, None] + new_index[None, :]
    query_turned = rotate_rows(queries, positions, HEADS)[0]
    key_turned = rotate_rows(new_keys, positions, HEADS)[0]
    splits = piece_count // HEADS
    query_rows = piece_rows // splits

    def by_head(rows):
        return jnp.transpose(rows.reshape(rows.shape[0], HEADS, HD), (1, 0, 2))

    def both_halves(parts):
        joined = jnp.concatenate(parts, 1)
        return jnp.broadcast_to(joined[:, None], (HEADS, splits) + joined.shape[1:]).reshape(
            (piece_count,) + joined.shape[1:]
        )

    cache_sent = both_halves([by_head(cache_keys[0]), by_head(cache_values[0])])
    cache_got = lax.all_to_all(cache_sent, "ep", split_axis=0, concat_axis=0, tiled=True)
    q_parts = jnp.transpose(
        query_turned.reshape(splits, query_rows, HEADS, HD), (2, 0, 1, 3)
    ).reshape(piece_count, query_rows, HD)
    new_sent = jnp.concatenate(
        [both_halves([by_head(key_turned), by_head(new_values[0])]), q_parts], 1
    )
    new_sent, cache_got = lax.optimization_barrier((new_sent, cache_got))
    new_got = lax.all_to_all(new_sent, "ep", split_axis=0, concat_axis=0, tiled=True)
    head_out = head_attention_kernel(
        cache_got, new_got, cached_len[0], piece_index % splits, piece_rows, cache_rows
    ).reshape(piece_count, query_rows, HD)
    returned = lax.all_to_all(head_out, "ep", split_axis=0, concat_axis=0, tiled=True)
    attended = jnp.transpose(
        returned.reshape(HEADS, splits, query_rows, HD), (1, 2, 0, 3)
    ).reshape(groups, piece_rows, HEADS * HD)
    hidden = residual_in.astype(jnp.float32) + jnp.einsum(
        "gtc,cd->gtd", attended, out_weight, preferred_element_type=jnp.float32
    )
    inv_root = lax.rsqrt(jnp.mean(hidden * hidden, -1, keepdims=True) + EPS)
    normed = (hidden * inv_root).astype(jnp.bfloat16)
    width = normed.shape[-1]
    rows = normed[0]
    slots = capacity
    ids = expert_ids[0]
    matches = (ids[..., None] == jnp.arange(experts, dtype=jnp.int32)).astype(jnp.int32)
    flat_matches = matches.reshape(piece_rows * top_count, experts)
    earlier = jnp.cumsum(flat_matches, 0) - flat_matches
    slot_index = jnp.sum(earlier * flat_matches, -1).reshape(piece_rows, top_count)
    target = ids * slots + slot_index
    chosen = target[..., None] == jnp.arange(experts * slots, dtype=jnp.int32)
    picked = jnp.any(chosen, 1).reshape(piece_rows, experts, 1, slots)
    weight = jnp.sum(jnp.where(chosen, gate_share[0][..., None], 0.0), 1)
    weight = weight.reshape(piece_rows, experts, slots)
    routed = jnp.zeros((piece_rows, width), jnp.float32)
    lane = 128
    previous = None
    for low, high in ((0, 8), (8, slots)):
        chunk = high - low
        travel = (chunk, width) if chunk % 8 == 0 else (chunk * width // lane, lane)
        chunk_select = picked[..., low:high].astype(jnp.bfloat16)
        chunk_select = jnp.broadcast_to(chunk_select, (piece_rows, experts, 2, chunk))
        once = jnp.einsum(
            "teks,tw->eksw", chunk_select, rows, preferred_element_type=jnp.float32
        ).astype(jnp.bfloat16)
        sending = jnp.broadcast_to(
            once.reshape((experts, -1) + travel), (experts, 2) + travel
        ).reshape((devices,) + travel)
        if previous is not None:
            sending, previous = lax.optimization_barrier((sending, previous))
        arrived = deliver(sending)
        previous = arrived
        produced = expert_half(
            arrived.reshape(-1, width), gate_weight[0], up_weight[0], down_weight[0]
        ).reshape((devices,) + travel)
        came_back = collect(produced).reshape((experts, 2) + travel)
        joined = (
            came_back[:, 0].astype(jnp.float32) + came_back[:, 1].astype(jnp.float32)
        ).astype(jnp.bfloat16)
        share = weight[..., low:high].reshape(piece_rows, experts * chunk)
        high_part = share.astype(jnp.bfloat16)
        low_part = (share - high_part.astype(jnp.float32)).astype(jnp.bfloat16)
        flat = joined.reshape(experts * chunk, width)
        routed = (
            routed
            + jnp.dot(high_part, flat, preferred_element_type=jnp.float32)
            + jnp.dot(low_part, flat, preferred_element_type=jnp.float32)
        )
    return (hidden + routed[None]).astype(jnp.bfloat16)


def solution(mesh):
    in_specs = (
        P("req", "ep", None),
        P("req", "ep", None),
        P("req", "ep", None),
        P("req", "ep", None),
        P("req", "ep", None),
        P("req", "ep", None),
        P("req"),
        P("req"),
        P(),
        P(("req", "ep"), None, None),
        P(("req", "ep"), None, None),
        P(("req", "ep"), None, None),
        P("req", "ep", None),
        P("req", "ep", None),
    )
    out_specs = P("req", "ep", None)
    return jax.shard_map(shards, mesh=mesh, in_specs=in_specs, out_specs=out_specs, check_vma=False)
```

```python
import functools

import jax
import jax.numpy as jnp
from jax import lax
from jax.experimental import pallas as pl
from jax.experimental.pallas import tpu as pltpu
from jax.sharding import PartitionSpec as P

HEADS = 8
HD = 128


NEG_FILL = -1e30
EPS = 1e-06
ROPE_BASE = 10000.0


def rotate_rows(values, positions, head_count):
    width_each = values.shape[-1] // head_count
    half_size = width_each // 2
    frequency = ROPE_BASE ** (
        -jnp.arange(half_size, dtype=jnp.int32).astype(jnp.float32) / half_size
    )
    angles = positions.astype(jnp.float32)[..., None] * frequency
    cosine = jnp.cos(angles)[..., None, :]
    sine = jnp.sin(angles)[..., None, :]
    shaped = values.astype(jnp.float32).reshape(values.shape[:-1] + (head_count, width_each))
    lower = shaped[..., :half_size]
    upper = shaped[..., half_size:]
    turned = jnp.concatenate(
        [lower * cosine - upper * sine, lower * sine + upper * cosine], axis=-1
    )
    return turned.reshape(values.shape).astype(jnp.bfloat16)


def block_terms(query_all, cache_k, cache_v, keys_new, values_new, length, cache_start, new_start):
    query_count = query_all.shape[0]
    cache_rows = cache_k.shape[0]
    piece_rows = keys_new.shape[0]
    query_heads = query_all.reshape(query_count, HEADS, HD)
    key_heads = jnp.concatenate([cache_k, keys_new], 0).reshape(-1, HEADS, HD)
    value_heads = jnp.concatenate([cache_v, values_new], 0).reshape(-1, HEADS, HD)
    scores = jnp.einsum(
        "qhd,khd->hqk", query_heads, key_heads, preferred_element_type=jnp.float32
    ) * HD ** (-0.5)
    cache_valid = cache_start + jnp.arange(cache_rows, dtype=jnp.int32) < length
    new_valid = (new_start + jnp.arange(piece_rows, dtype=jnp.int32))[None, :] <= jnp.arange(
        query_count, dtype=jnp.int32
    )[:, None]
    valid = jnp.concatenate(
        [jnp.broadcast_to(cache_valid[None, :], (query_count, cache_rows)), new_valid], 1
    )[None]
    masked = jnp.where(valid, scores, NEG_FILL)
    score_peak = jnp.max(masked, -1)
    weights = jnp.where(valid, jnp.exp(masked - score_peak[..., None]), 0.0)
    weight_sum = jnp.sum(weights, -1)
    mixed = jnp.einsum(
        "hqk,khd->qhd",
        weights.astype(jnp.bfloat16),
        value_heads,
        preferred_element_type=jnp.float32,
    )
    return (mixed, score_peak.T, weight_sum.T)


def expert_half(rows, gate_part, up_part, down_part):
    gate_val = jnp.dot(rows, gate_part, preferred_element_type=jnp.float32)
    up_val = jnp.dot(rows, up_part, preferred_element_type=jnp.float32)
    activation = (jax.nn.silu(gate_val) * up_val).astype(jnp.bfloat16)
    return jnp.dot(activation, down_part, preferred_element_type=jnp.float32).astype(jnp.bfloat16)


def deliver(rows):
    return lax.all_to_all(rows, ("req", "ep"), split_axis=0, concat_axis=0, tiled=True)


def collect(rows):
    return lax.all_to_all(rows, ("req", "ep"), split_axis=0, concat_axis=0, tiled=True)


def head_attention(keys, values, query, length, half_index, piece_rows, cache_rows):
    pieces, query_rows = query.shape[0], query.shape[1]
    block_rows = cache_rows + piece_rows
    query = query.reshape(pieces * query_rows, HD)
    scores = jnp.einsum(
        "qd,bkd->bqk", query, keys, preferred_element_type=jnp.float32
    ) * HD ** (-0.5)
    block = jnp.arange(pieces, dtype=jnp.int32)[:, None, None]
    key_pos = jnp.arange(block_rows, dtype=jnp.int32)[None, None, :]
    query_row = jnp.arange(pieces * query_rows, dtype=jnp.int32)
    query_index = (
        (query_row // query_rows) * piece_rows + half_index * query_rows + query_row % query_rows
    )[None, :, None]
    cache_valid = block * cache_rows + key_pos < length
    new_valid = block * piece_rows + (key_pos - cache_rows) <= query_index
    valid = jnp.where(key_pos < cache_rows, cache_valid, new_valid)
    masked = jnp.where(valid, scores, NEG_FILL)
    score_peak = jnp.max(masked, -1)
    weights = jnp.where(valid, jnp.exp(masked - score_peak[..., None]), 0.0)
    weight_sum = jnp.sum(weights, -1)
    mixed = jnp.einsum(
        "bqk,bkd->bqd",
        weights.astype(jnp.bfloat16),
        values,
        preferred_element_type=jnp.float32,
    )
    peak = jnp.max(score_peak, 0, keepdims=True)
    factor = jnp.exp(score_peak - peak)
    summed = jnp.sum(factor[..., None] * mixed, 0)
    denominator = jnp.sum(factor * weight_sum, 0)
    return (summed / denominator[:, None]).astype(jnp.bfloat16)


def attention_kernel(scalars, kc_ref, vc_ref, kn_ref, vn_ref, q_ref, o_ref, m_scr, acc_scr, den_scr, *, cache_rows, piece_rows, query_rows):
    step = pl.program_id(0)
    length = scalars[0]
    half = scalars[1]
    per_step = kc_ref.shape[0]
    root = HD ** (-0.5)

    @pl.when(step == 0)
    def _():
        m_scr[...] = jnp.full(m_scr.shape, NEG_FILL, jnp.float32)
        acc_scr[...] = jnp.zeros(acc_scr.shape, jnp.float32)
        den_scr[...] = jnp.zeros(den_scr.shape, jnp.float32)

    query = q_ref[...].reshape(-1, HD)
    count = query.shape[0]
    dims = (((1,), (1,)), ((), ()))
    row = lax.broadcasted_iota(jnp.int32, (count, 1), 0)
    query_index = (row // query_rows) * piece_rows + half * query_rows + row % query_rows
    cache_pos = lax.broadcasted_iota(jnp.int32, (1, cache_rows), 1)
    new_pos = lax.broadcasted_iota(jnp.int32, (1, piece_rows), 1)
    for sub in range(per_step):
        block = step * per_step + sub
        s_cache = lax.dot_general(query, kc_ref[sub], dims, preferred_element_type=jnp.float32)
        s_new = lax.dot_general(query, kn_ref[sub], dims, preferred_element_type=jnp.float32)
        cache_bias = jnp.where(block * cache_rows + cache_pos < length, 0.0, NEG_FILL)
        masked_cache = s_cache + cache_bias
        masked_new = jnp.where(block * piece_rows + new_pos <= query_index, s_new, NEG_FILL)
        peak = jnp.maximum(
            jnp.max(masked_cache, axis=1, keepdims=True), jnp.max(masked_new, axis=1, keepdims=True)
        )
        p_cache = jnp.exp((masked_cache - peak) * root)
        p_new = jnp.exp((masked_new - peak) * root)
        total = jnp.sum(p_cache, axis=1, keepdims=True) + jnp.sum(p_new, axis=1, keepdims=True)
        mixed = jnp.dot(
            p_cache.astype(jnp.bfloat16), vc_ref[sub], preferred_element_type=jnp.float32
        ) + jnp.dot(p_new.astype(jnp.bfloat16), vn_ref[sub], preferred_element_type=jnp.float32)
        peak = jnp.where(peak > 0.5 * NEG_FILL, peak * root, NEG_FILL)
        old = m_scr[...]
        top = jnp.maximum(old, peak)
        keep = jnp.exp(old - top)
        scale = jnp.exp(peak - top)
        acc_scr[...] = acc_scr[...] * keep + scale * mixed
        den_scr[...] = den_scr[...] * keep + scale * total
        m_scr[...] = top

    @pl.when(step == pl.num_programs(0) - 1)
    def _():
        o_ref[...] = (acc_scr[...] / den_scr[...]).astype(o_ref.dtype)


def head_attention_kernel(cache_got, new_got, length, half_index, piece_rows, cache_rows):
    pieces = cache_got.shape[0]
    per_step = 2
    query_rows = new_got.shape[1] - 2 * piece_rows
    count = pieces * query_rows
    scalars = jnp.stack([length, half_index]).astype(jnp.int32)
    kernel = functools.partial(attention_kernel, cache_rows=cache_rows, piece_rows=piece_rows, query_rows=query_rows)
    grid_spec = pltpu.PrefetchScalarGridSpec(
        num_scalar_prefetch=1,
        grid=(pieces // per_step,),
        in_specs=[
            pl.BlockSpec((per_step, cache_rows, HD), lambda b, s: (b, 0, 0)),
            pl.BlockSpec((per_step, cache_rows, HD), lambda b, s: (b, 1, 0)),
            pl.BlockSpec((per_step, piece_rows, HD), lambda b, s: (b, 0, 0)),
            pl.BlockSpec((per_step, piece_rows, HD), lambda b, s: (b, 1, 0)),
            pl.BlockSpec((pieces, query_rows, HD), lambda b, s: (0, 2 * piece_rows // query_rows, 0)),
        ],
        out_specs=pl.BlockSpec((count, HD), lambda b, s: (0, 0)),
        scratch_shapes=[
            pltpu.VMEM((count, 1), jnp.float32),
            pltpu.VMEM((count, HD), jnp.float32),
            pltpu.VMEM((count, 1), jnp.float32),
        ],
    )
    return pl.pallas_call(
        kernel,
        grid_spec=grid_spec,
        out_shape=jax.ShapeDtypeStruct((count, HD), jnp.bfloat16),
        compiler_params=pltpu.CompilerParams(dimension_semantics=("arbitrary",)),
    )(scalars, cache_got, cache_got, new_got, new_got, new_got)


def shards(
    residual_in,
    queries,
    new_keys,
    new_values,
    cache_keys,
    cache_values,
    cached_len,
    rope_offset,
    out_weight,
    gate_weight,
    up_weight,
    down_weight,
    expert_ids,
    gate_share,
):
    req_count = lax.axis_size("req")
    piece_count = lax.axis_size("ep")
    devices = req_count * piece_count
    experts = devices // 2
    groups, piece_rows, _ = queries.shape
    cache_rows = cache_keys.shape[1]
    top_count = expert_ids.shape[2]
    capacity = (piece_rows * top_count + experts - 1) // experts + 1
    piece_index = lax.axis_index("ep")
    new_index = piece_index * piece_rows + jnp.arange(piece_rows, dtype=jnp.int32)
    positions = rope_offset[:, None] + cached_len[:, None] + new_index[None, :]
    query_turned = rotate_rows(queries, positions, HEADS)[0]
    key_turned = rotate_rows(new_keys, positions, HEADS)[0]
    splits = piece_count // HEADS
    query_rows = piece_rows // splits

    def by_head(rows):
        return jnp.transpose(rows.reshape(rows.shape[0], HEADS, HD), (1, 0, 2))

    def both_halves(parts):
        joined = jnp.concatenate(parts, 1)
        return jnp.broadcast_to(joined[:, None], (HEADS, splits) + joined.shape[1:]).reshape(
            (piece_count,) + joined.shape[1:]
        )

    cache_sent = both_halves([by_head(cache_keys[0]), by_head(cache_values[0])])
    cache_got = lax.all_to_all(cache_sent, "ep", split_axis=0, concat_axis=0, tiled=True)
    q_parts = jnp.transpose(
        query_turned.reshape(splits, query_rows, HEADS, HD), (2, 0, 1, 3)
    ).reshape(piece_count, query_rows, HD)
    new_sent = jnp.concatenate(
        [both_halves([by_head(key_turned), by_head(new_values[0])]), q_parts], 1
    )
    new_sent, cache_got = lax.optimization_barrier((new_sent, cache_got))
    new_got = lax.all_to_all(new_sent, "ep", split_axis=0, concat_axis=0, tiled=True)
    head_out = head_attention_kernel(
        cache_got, new_got, cached_len[0], piece_index % splits, piece_rows, cache_rows
    ).reshape(piece_count, query_rows, HD)
    returned = lax.all_to_all(head_out, "ep", split_axis=0, concat_axis=0, tiled=True)
    attended = jnp.transpose(
        returned.reshape(HEADS, splits, query_rows, HD), (1, 2, 0, 3)
    ).reshape(groups, piece_rows, HEADS * HD)
    hidden = residual_in.astype(jnp.float32) + jnp.einsum(
        "gtc,cd->gtd", attended, out_weight, preferred_element_type=jnp.float32
    )
    inv_root = lax.rsqrt(jnp.mean(hidden * hidden, -1, keepdims=True) + EPS)
    normed = (hidden * inv_root).astype(jnp.bfloat16)
    width = normed.shape[-1]
    rows = normed[0]
    slots = capacity
    ids = expert_ids[0]
    matches = (ids[..., None] == jnp.arange(experts, dtype=jnp.int32)).astype(jnp.int32)
    flat_matches = matches.reshape(piece_rows * top_count, experts)
    earlier = jnp.cumsum(flat_matches, 0) - flat_matches
    slot_index = jnp.sum(earlier * flat_matches, -1).reshape(piece_rows, top_count)
    target = ids * slots + slot_index
    chosen = target[..., None] == jnp.arange(experts * slots, dtype=jnp.int32)
    picked = jnp.any(chosen, 1).reshape(piece_rows, experts, 1, slots)
    weight = jnp.sum(jnp.where(chosen, gate_share[0][..., None], 0.0), 1)
    weight = weight.reshape(piece_rows, experts, slots)
    routed = jnp.zeros((piece_rows, width), jnp.float32)
    lane = 128
    previous = None
    for low, high in ((0, 8), (8, slots)):
        chunk = high - low
        travel = (chunk, width) if chunk % 8 == 0 else (chunk * width // lane, lane)
        chunk_select = picked[..., low:high].astype(jnp.bfloat16)
        chunk_select = jnp.broadcast_to(chunk_select, (piece_rows, experts, 2, chunk))
        once = jnp.einsum(
            "teks,tw->eksw", chunk_select, rows, preferred_element_type=jnp.float32
        ).astype(jnp.bfloat16)
        sending = jnp.broadcast_to(
            once.reshape((experts, -1) + travel), (experts, 2) + travel
        ).reshape((devices,) + travel)
        if previous is not None:
            sending, previous = lax.optimization_barrier((sending, previous))
        arrived = deliver(sending)
        previous = arrived
        produced = expert_half(
            arrived.reshape(-1, width), gate_weight[0], up_weight[0], down_weight[0]
        ).reshape((devices,) + travel)
        came_back = collect(produced).reshape(experts, 2, chunk, width)
        joined = (
            came_back[:, 0].astype(jnp.float32) + came_back[:, 1].astype(jnp.float32)
        ).astype(jnp.bfloat16)
        routed = routed + jnp.dot(
            weight[..., low:high].reshape(piece_rows, experts * chunk),
            joined.reshape(experts * chunk, width).astype(jnp.float32),
            precision=lax.Precision.HIGHEST,
        )
    return (hidden + routed[None]).astype(jnp.bfloat16)


def solution(mesh):
    in_specs = (
        P("req", "ep", None),
        P("req", "ep", None),
        P("req", "ep", None),
        P("req", "ep", None),
        P("req", "ep", None),
        P("req", "ep", None),
        P("req"),
        P("req"),
        P(),
        P(("req", "ep"), None, None),
        P(("req", "ep"), None, None),
        P(("req", "ep"), None, None),
        P("req", "ep", None),
        P("req", "ep", None),
    )
    out_specs = P("req", "ep", None)
    return jax.shard_map(shards, mesh=mesh, in_specs=in_specs, out_specs=out_specs, check_vma=False)
```

```python
import functools

import jax
import jax.numpy as jnp
from jax import lax
from jax.experimental import pallas as pl
from jax.experimental.pallas import tpu as pltpu
from jax.sharding import PartitionSpec as P

HEADS = 8
HD = 128


NEG_FILL = -1e30
EPS = 1e-06
ROPE_BASE = 10000.0


def rotate_rows(values, positions, head_count):
    width_each = values.shape[-1] // head_count
    half_size = width_each // 2
    frequency = ROPE_BASE ** (
        -jnp.arange(half_size, dtype=jnp.int32).astype(jnp.float32) / half_size
    )
    angles = positions.astype(jnp.float32)[..., None] * frequency
    cosine = jnp.cos(angles)[..., None, :]
    sine = jnp.sin(angles)[..., None, :]
    shaped = values.astype(jnp.float32).reshape(values.shape[:-1] + (head_count, width_each))
    lower = shaped[..., :half_size]
    upper = shaped[..., half_size:]
    turned = jnp.concatenate(
        [lower * cosine - upper * sine, lower * sine + upper * cosine], axis=-1
    )
    return turned.reshape(values.shape).astype(jnp.bfloat16)


def block_terms(query_all, cache_k, cache_v, keys_new, values_new, length, cache_start, new_start):
    query_count = query_all.shape[0]
    cache_rows = cache_k.shape[0]
    piece_rows = keys_new.shape[0]
    query_heads = query_all.reshape(query_count, HEADS, HD)
    key_heads = jnp.concatenate([cache_k, keys_new], 0).reshape(-1, HEADS, HD)
    value_heads = jnp.concatenate([cache_v, values_new], 0).reshape(-1, HEADS, HD)
    scores = jnp.einsum(
        "qhd,khd->hqk", query_heads, key_heads, preferred_element_type=jnp.float32
    ) * HD ** (-0.5)
    cache_valid = cache_start + jnp.arange(cache_rows, dtype=jnp.int32) < length
    new_valid = (new_start + jnp.arange(piece_rows, dtype=jnp.int32))[None, :] <= jnp.arange(
        query_count, dtype=jnp.int32
    )[:, None]
    valid = jnp.concatenate(
        [jnp.broadcast_to(cache_valid[None, :], (query_count, cache_rows)), new_valid], 1
    )[None]
    masked = jnp.where(valid, scores, NEG_FILL)
    score_peak = jnp.max(masked, -1)
    weights = jnp.where(valid, jnp.exp(masked - score_peak[..., None]), 0.0)
    weight_sum = jnp.sum(weights, -1)
    mixed = jnp.einsum(
        "hqk,khd->qhd",
        weights.astype(jnp.bfloat16),
        value_heads,
        preferred_element_type=jnp.float32,
    )
    return (mixed, score_peak.T, weight_sum.T)


def expert_half(rows, gate_part, up_part, down_part):
    gate_val = jnp.dot(rows, gate_part, preferred_element_type=jnp.float32)
    up_val = jnp.dot(rows, up_part, preferred_element_type=jnp.float32)
    activation = (jax.nn.silu(gate_val) * up_val).astype(jnp.bfloat16)
    return jnp.dot(activation, down_part, preferred_element_type=jnp.float32).astype(jnp.bfloat16)


def deliver(rows):
    return lax.all_to_all(rows, ("req", "ep"), split_axis=0, concat_axis=0, tiled=True)


def collect(rows):
    return lax.all_to_all(rows, ("req", "ep"), split_axis=0, concat_axis=0, tiled=True)


def head_attention(keys, values, query, length, half_index, piece_rows, cache_rows):
    pieces, query_rows = query.shape[0], query.shape[1]
    block_rows = cache_rows + piece_rows
    query = query.reshape(pieces * query_rows, HD)
    scores = jnp.einsum(
        "qd,bkd->bqk", query, keys, preferred_element_type=jnp.float32
    ) * HD ** (-0.5)
    block = jnp.arange(pieces, dtype=jnp.int32)[:, None, None]
    key_pos = jnp.arange(block_rows, dtype=jnp.int32)[None, None, :]
    query_row = jnp.arange(pieces * query_rows, dtype=jnp.int32)
    query_index = (
        (query_row // query_rows) * piece_rows + half_index * query_rows + query_row % query_rows
    )[None, :, None]
    cache_valid = block * cache_rows + key_pos < length
    new_valid = block * piece_rows + (key_pos - cache_rows) <= query_index
    valid = jnp.where(key_pos < cache_rows, cache_valid, new_valid)
    masked = jnp.where(valid, scores, NEG_FILL)
    score_peak = jnp.max(masked, -1)
    weights = jnp.where(valid, jnp.exp(masked - score_peak[..., None]), 0.0)
    weight_sum = jnp.sum(weights, -1)
    mixed = jnp.einsum(
        "bqk,bkd->bqd",
        weights.astype(jnp.bfloat16),
        values,
        preferred_element_type=jnp.float32,
    )
    peak = jnp.max(score_peak, 0, keepdims=True)
    factor = jnp.exp(score_peak - peak)
    summed = jnp.sum(factor[..., None] * mixed, 0)
    denominator = jnp.sum(factor * weight_sum, 0)
    return (summed / denominator[:, None]).astype(jnp.bfloat16)


def attention_kernel(scalars, kc_ref, vc_ref, kn_ref, vn_ref, q_ref, o_ref, m_scr, acc_scr, den_scr, *, cache_rows, piece_rows, query_rows):
    step = pl.program_id(0)
    length = scalars[0]
    half = scalars[1]
    per_step = kc_ref.shape[0]
    root = HD ** (-0.5)

    @pl.when(step == 0)
    def _():
        m_scr[...] = jnp.full(m_scr.shape, NEG_FILL, jnp.float32)
        acc_scr[...] = jnp.zeros(acc_scr.shape, jnp.float32)
        den_scr[...] = jnp.zeros(den_scr.shape, jnp.float32)

    query = q_ref[...].reshape(-1, HD)
    count = query.shape[0]
    dims = (((1,), (1,)), ((), ()))
    row = lax.broadcasted_iota(jnp.int32, (count, 1), 0)
    query_index = (row // query_rows) * piece_rows + half * query_rows + row % query_rows
    cache_pos = lax.broadcasted_iota(jnp.int32, (1, cache_rows), 1)
    new_pos = lax.broadcasted_iota(jnp.int32, (1, piece_rows), 1)
    old, acc, den = m_scr[...], acc_scr[...], den_scr[...]
    for sub in range(per_step):
        block = step * per_step + sub
        s_cache = lax.dot_general(query, kc_ref[sub], dims, preferred_element_type=jnp.float32)
        s_new = lax.dot_general(query, kn_ref[sub], dims, preferred_element_type=jnp.float32)
        cache_bias = jnp.where(block * cache_rows + cache_pos < length, 0.0, NEG_FILL)
        masked_cache = s_cache + cache_bias
        masked_new = jnp.where(block * piece_rows + new_pos <= query_index, s_new, NEG_FILL)
        peak = jnp.maximum(
            jnp.max(masked_cache, axis=1, keepdims=True), jnp.max(masked_new, axis=1, keepdims=True)
        )
        p_cache = jnp.exp((masked_cache - peak) * root)
        p_new = jnp.exp((masked_new - peak) * root)
        total = jnp.sum(p_cache, axis=1, keepdims=True) + jnp.sum(p_new, axis=1, keepdims=True)
        mixed = jnp.dot(
            p_cache.astype(jnp.bfloat16), vc_ref[sub], preferred_element_type=jnp.float32
        ) + jnp.dot(p_new.astype(jnp.bfloat16), vn_ref[sub], preferred_element_type=jnp.float32)
        peak = jnp.where(peak > 0.5 * NEG_FILL, peak * root, NEG_FILL)
        top = jnp.maximum(old, peak)
        keep = jnp.exp(old - top)
        scale = jnp.exp(peak - top)
        acc = acc * keep + scale * mixed
        den = den * keep + scale * total
        old = top
    acc_scr[...] = acc
    den_scr[...] = den
    m_scr[...] = old

    @pl.when(step == pl.num_programs(0) - 1)
    def _():
        o_ref[...] = (acc_scr[...] / den_scr[...]).astype(o_ref.dtype)


def head_attention_kernel(cache_got, new_got, length, half_index, piece_rows, cache_rows):
    pieces = cache_got.shape[0]
    per_step = 2
    query_rows = new_got.shape[1] - 2 * piece_rows
    count = pieces * query_rows
    scalars = jnp.stack([length, half_index]).astype(jnp.int32)
    kernel = functools.partial(attention_kernel, cache_rows=cache_rows, piece_rows=piece_rows, query_rows=query_rows)
    grid_spec = pltpu.PrefetchScalarGridSpec(
        num_scalar_prefetch=1,
        grid=(pieces // per_step,),
        in_specs=[
            pl.BlockSpec((per_step, cache_rows, HD), lambda b, s: (b, 0, 0)),
            pl.BlockSpec((per_step, cache_rows, HD), lambda b, s: (b, 1, 0)),
            pl.BlockSpec((per_step, piece_rows, HD), lambda b, s: (b, 0, 0)),
            pl.BlockSpec((per_step, piece_rows, HD), lambda b, s: (b, 1, 0)),
            pl.BlockSpec((pieces, query_rows, HD), lambda b, s: (0, 2 * piece_rows // query_rows, 0)),
        ],
        out_specs=pl.BlockSpec((count, HD), lambda b, s: (0, 0)),
        scratch_shapes=[
            pltpu.VMEM((count, 1), jnp.float32),
            pltpu.VMEM((count, HD), jnp.float32),
            pltpu.VMEM((count, 1), jnp.float32),
        ],
    )
    return pl.pallas_call(
        kernel,
        grid_spec=grid_spec,
        out_shape=jax.ShapeDtypeStruct((count, HD), jnp.bfloat16),
        compiler_params=pltpu.CompilerParams(dimension_semantics=("arbitrary",)),
    )(scalars, cache_got, cache_got, new_got, new_got, new_got)


def shards(
    residual_in,
    queries,
    new_keys,
    new_values,
    cache_keys,
    cache_values,
    cached_len,
    rope_offset,
    out_weight,
    gate_weight,
    up_weight,
    down_weight,
    expert_ids,
    gate_share,
):
    req_count = lax.axis_size("req")
    piece_count = lax.axis_size("ep")
    devices = req_count * piece_count
    experts = devices // 2
    groups, piece_rows, _ = queries.shape
    cache_rows = cache_keys.shape[1]
    top_count = expert_ids.shape[2]
    capacity = (piece_rows * top_count + experts - 1) // experts + 1
    piece_index = lax.axis_index("ep")
    new_index = piece_index * piece_rows + jnp.arange(piece_rows, dtype=jnp.int32)
    positions = rope_offset[:, None] + cached_len[:, None] + new_index[None, :]
    query_turned = rotate_rows(queries, positions, HEADS)[0]
    key_turned = rotate_rows(new_keys, positions, HEADS)[0]
    splits = piece_count // HEADS
    query_rows = piece_rows // splits

    def by_head(rows):
        return jnp.transpose(rows.reshape(rows.shape[0], HEADS, HD), (1, 0, 2))

    def both_halves(parts):
        joined = jnp.concatenate(parts, 1)
        return jnp.broadcast_to(joined[:, None], (HEADS, splits) + joined.shape[1:]).reshape(
            (piece_count,) + joined.shape[1:]
        )

    cache_sent = both_halves([by_head(cache_keys[0]), by_head(cache_values[0])])
    cache_got = lax.all_to_all(cache_sent, "ep", split_axis=0, concat_axis=0, tiled=True)
    q_parts = jnp.transpose(
        query_turned.reshape(splits, query_rows, HEADS, HD), (2, 0, 1, 3)
    ).reshape(piece_count, query_rows, HD)
    new_sent = jnp.concatenate(
        [both_halves([by_head(key_turned), by_head(new_values[0])]), q_parts], 1
    )
    new_sent, cache_got = lax.optimization_barrier((new_sent, cache_got))
    new_got = lax.all_to_all(new_sent, "ep", split_axis=0, concat_axis=0, tiled=True)
    head_out = head_attention_kernel(
        cache_got, new_got, cached_len[0], piece_index % splits, piece_rows, cache_rows
    ).reshape(piece_count, query_rows, HD)
    returned = lax.all_to_all(head_out, "ep", split_axis=0, concat_axis=0, tiled=True)
    attended = jnp.transpose(
        returned.reshape(HEADS, splits, query_rows, HD), (1, 2, 0, 3)
    ).reshape(groups, piece_rows, HEADS * HD)
    hidden = residual_in.astype(jnp.float32) + jnp.einsum(
        "gtc,cd->gtd", attended, out_weight, preferred_element_type=jnp.float32
    )
    inv_root = lax.rsqrt(jnp.mean(hidden * hidden, -1, keepdims=True) + EPS)
    normed = (hidden * inv_root).astype(jnp.bfloat16)
    width = normed.shape[-1]
    rows = normed[0]
    slots = capacity
    ids = expert_ids[0]
    matches = (ids[..., None] == jnp.arange(experts, dtype=jnp.int32)).astype(jnp.int32)
    flat_matches = matches.reshape(piece_rows * top_count, experts)
    earlier = jnp.cumsum(flat_matches, 0) - flat_matches
    slot_index = jnp.sum(earlier * flat_matches, -1).reshape(piece_rows, top_count)
    target = ids * slots + slot_index
    chosen = target[..., None] == jnp.arange(experts * slots, dtype=jnp.int32)
    picked = jnp.any(chosen, 1).reshape(piece_rows, experts, 1, slots)
    weight = jnp.sum(jnp.where(chosen, gate_share[0][..., None], 0.0), 1)
    weight = weight.reshape(piece_rows, experts, slots)
    routed = jnp.zeros((piece_rows, width), jnp.float32)
    lane = 128
    previous = None
    for low, high in ((0, 8), (8, slots)):
        chunk = high - low
        travel = (chunk, width) if chunk % 8 == 0 else (chunk * width // lane, lane)
        chunk_select = picked[..., low:high].astype(jnp.bfloat16)
        chunk_select = jnp.broadcast_to(chunk_select, (piece_rows, experts, 2, chunk))
        once = jnp.einsum(
            "teks,tw->eksw", chunk_select, rows, preferred_element_type=jnp.float32
        ).astype(jnp.bfloat16)
        sending = jnp.broadcast_to(
            once.reshape((experts, -1) + travel), (experts, 2) + travel
        ).reshape((devices,) + travel)
        if previous is not None:
            sending, previous = lax.optimization_barrier((sending, previous))
        arrived = deliver(sending)
        previous = arrived
        produced = expert_half(
            arrived.reshape(-1, width), gate_weight[0], up_weight[0], down_weight[0]
        ).reshape((devices,) + travel)
        came_back = collect(produced).reshape((experts, 2) + travel)
        joined = (
            came_back[:, 0].astype(jnp.float32) + came_back[:, 1].astype(jnp.float32)
        ).astype(jnp.bfloat16)
        routed = routed + jnp.dot(
            weight[..., low:high].reshape(piece_rows, experts * chunk),
            joined.reshape(experts * chunk, width).astype(jnp.float32),
            precision=lax.Precision.HIGHEST,
        )
    return (hidden + routed[None]).astype(jnp.bfloat16)


def solution(mesh):
    in_specs = (
        P("req", "ep", None),
        P("req", "ep", None),
        P("req", "ep", None),
        P("req", "ep", None),
        P("req", "ep", None),
        P("req", "ep", None),
        P("req"),
        P("req"),
        P(),
        P(("req", "ep"), None, None),
        P(("req", "ep"), None, None),
        P(("req", "ep"), None, None),
        P("req", "ep", None),
        P("req", "ep", None),
    )
    out_specs = P("req", "ep", None)
    return jax.shard_map(shards, mesh=mesh, in_specs=in_specs, out_specs=out_specs, check_vma=False)
```

```python
import functools

import jax
import jax.numpy as jnp
from jax import lax
from jax.experimental import pallas as pl
from jax.experimental.pallas import tpu as pltpu
from jax.sharding import PartitionSpec as P

HEADS = 8
HD = 128


NEG_FILL = -1e30
EPS = 1e-06
ROPE_BASE = 10000.0


def rotate_rows(values, positions, head_count):
    width_each = values.shape[-1] // head_count
    half_size = width_each // 2
    frequency = ROPE_BASE ** (
        -jnp.arange(half_size, dtype=jnp.int32).astype(jnp.float32) / half_size
    )
    angles = positions.astype(jnp.float32)[..., None] * frequency
    cosine = jnp.cos(angles)[..., None, :]
    sine = jnp.sin(angles)[..., None, :]
    shaped = values.astype(jnp.float32).reshape(values.shape[:-1] + (head_count, width_each))
    lower = shaped[..., :half_size]
    upper = shaped[..., half_size:]
    turned = jnp.concatenate(
        [lower * cosine - upper * sine, lower * sine + upper * cosine], axis=-1
    )
    return turned.reshape(values.shape).astype(jnp.bfloat16)


def block_terms(query_all, cache_k, cache_v, keys_new, values_new, length, cache_start, new_start):
    query_count = query_all.shape[0]
    cache_rows = cache_k.shape[0]
    piece_rows = keys_new.shape[0]
    query_heads = query_all.reshape(query_count, HEADS, HD)
    key_heads = jnp.concatenate([cache_k, keys_new], 0).reshape(-1, HEADS, HD)
    value_heads = jnp.concatenate([cache_v, values_new], 0).reshape(-1, HEADS, HD)
    scores = jnp.einsum(
        "qhd,khd->hqk", query_heads, key_heads, preferred_element_type=jnp.float32
    ) * HD ** (-0.5)
    cache_valid = cache_start + jnp.arange(cache_rows, dtype=jnp.int32) < length
    new_valid = (new_start + jnp.arange(piece_rows, dtype=jnp.int32))[None, :] <= jnp.arange(
        query_count, dtype=jnp.int32
    )[:, None]
    valid = jnp.concatenate(
        [jnp.broadcast_to(cache_valid[None, :], (query_count, cache_rows)), new_valid], 1
    )[None]
    masked = jnp.where(valid, scores, NEG_FILL)
    score_peak = jnp.max(masked, -1)
    weights = jnp.where(valid, jnp.exp(masked - score_peak[..., None]), 0.0)
    weight_sum = jnp.sum(weights, -1)
    mixed = jnp.einsum(
        "hqk,khd->qhd",
        weights.astype(jnp.bfloat16),
        value_heads,
        preferred_element_type=jnp.float32,
    )
    return (mixed, score_peak.T, weight_sum.T)


def expert_half(rows, gate_part, up_part, down_part):
    gate_val = jnp.dot(rows, gate_part, preferred_element_type=jnp.float32)
    up_val = jnp.dot(rows, up_part, preferred_element_type=jnp.float32)
    activation = (jax.nn.silu(gate_val) * up_val).astype(jnp.bfloat16)
    return jnp.dot(activation, down_part, preferred_element_type=jnp.float32).astype(jnp.bfloat16)


def deliver(rows):
    return lax.all_to_all(rows, ("req", "ep"), split_axis=0, concat_axis=0, tiled=True)


def collect(rows):
    return lax.all_to_all(rows, ("req", "ep"), split_axis=0, concat_axis=0, tiled=True)


def head_attention(keys, values, query, length, half_index, piece_rows, cache_rows):
    pieces, query_rows = query.shape[0], query.shape[1]
    block_rows = cache_rows + piece_rows
    query = query.reshape(pieces * query_rows, HD)
    scores = jnp.einsum(
        "qd,bkd->bqk", query, keys, preferred_element_type=jnp.float32
    ) * HD ** (-0.5)
    block = jnp.arange(pieces, dtype=jnp.int32)[:, None, None]
    key_pos = jnp.arange(block_rows, dtype=jnp.int32)[None, None, :]
    query_row = jnp.arange(pieces * query_rows, dtype=jnp.int32)
    query_index = (
        (query_row // query_rows) * piece_rows + half_index * query_rows + query_row % query_rows
    )[None, :, None]
    cache_valid = block * cache_rows + key_pos < length
    new_valid = block * piece_rows + (key_pos - cache_rows) <= query_index
    valid = jnp.where(key_pos < cache_rows, cache_valid, new_valid)
    masked = jnp.where(valid, scores, NEG_FILL)
    score_peak = jnp.max(masked, -1)
    weights = jnp.where(valid, jnp.exp(masked - score_peak[..., None]), 0.0)
    weight_sum = jnp.sum(weights, -1)
    mixed = jnp.einsum(
        "bqk,bkd->bqd",
        weights.astype(jnp.bfloat16),
        values,
        preferred_element_type=jnp.float32,
    )
    peak = jnp.max(score_peak, 0, keepdims=True)
    factor = jnp.exp(score_peak - peak)
    summed = jnp.sum(factor[..., None] * mixed, 0)
    denominator = jnp.sum(factor * weight_sum, 0)
    return (summed / denominator[:, None]).astype(jnp.bfloat16)


def attention_kernel(scalars, kc_ref, vc_ref, kn_ref, vn_ref, q_ref, o_ref, m_scr, acc_scr, den_scr, *, cache_rows, piece_rows, query_rows):
    step = pl.program_id(0)
    length = scalars[0]
    half = scalars[1]
    per_step = kc_ref.shape[0]
    root = HD ** (-0.5)

    @pl.when(step == 0)
    def _():
        m_scr[...] = jnp.full(m_scr.shape, NEG_FILL, jnp.float32)
        acc_scr[...] = jnp.zeros(acc_scr.shape, jnp.float32)
        den_scr[...] = jnp.zeros(den_scr.shape, jnp.float32)

    query = q_ref[...].reshape(-1, HD)
    count = query.shape[0]
    dims = (((1,), (1,)), ((), ()))
    row = lax.broadcasted_iota(jnp.int32, (count, 1), 0)
    query_index = (row // query_rows) * piece_rows + half * query_rows + row % query_rows
    cache_pos = lax.broadcasted_iota(jnp.int32, (1, cache_rows), 1)
    new_pos = lax.broadcasted_iota(jnp.int32, (1, piece_rows), 1)
    for sub in range(per_step):
        block = step * per_step + sub
        s_cache = lax.dot_general(query, kc_ref[sub], dims, preferred_element_type=jnp.float32)
        s_new = lax.dot_general(query, kn_ref[sub], dims, preferred_element_type=jnp.float32)
        cache_bias = jnp.where(block * cache_rows + cache_pos < length, 0.0, NEG_FILL)
        masked_cache = s_cache + cache_bias
        masked_new = jnp.where(block * piece_rows + new_pos <= query_index, s_new, NEG_FILL)
        peak = jnp.maximum(
            jnp.max(masked_cache, axis=1, keepdims=True), jnp.max(masked_new, axis=1, keepdims=True)
        )
        p_cache = jnp.exp((masked_cache - peak) * root)
        p_new = jnp.exp((masked_new - peak) * root)
        total = jnp.sum(p_cache, axis=1, keepdims=True) + jnp.sum(p_new, axis=1, keepdims=True)
        mixed = jnp.dot(
            p_cache.astype(jnp.bfloat16), vc_ref[sub], preferred_element_type=jnp.float32
        ) + jnp.dot(p_new.astype(jnp.bfloat16), vn_ref[sub], preferred_element_type=jnp.float32)
        peak = jnp.where(peak > 0.5 * NEG_FILL, peak * root, NEG_FILL)
        old = m_scr[...]
        top = jnp.maximum(old, peak)
        keep = jnp.exp(old - top)
        scale = jnp.exp(peak - top)
        acc_scr[...] = acc_scr[...] * keep + scale * mixed
        den_scr[...] = den_scr[...] * keep + scale * total
        m_scr[...] = top

    @pl.when(step == pl.num_programs(0) - 1)
    def _():
        o_ref[...] = (acc_scr[...] / den_scr[...]).astype(o_ref.dtype)


def head_attention_kernel(cache_got, new_got, length, half_index, piece_rows, cache_rows):
    pieces = cache_got.shape[0]
    per_step = 2
    query_rows = new_got.shape[1] - 2 * piece_rows
    count = pieces * query_rows
    scalars = jnp.stack([length, half_index]).astype(jnp.int32)
    kernel = functools.partial(attention_kernel, cache_rows=cache_rows, piece_rows=piece_rows, query_rows=query_rows)
    grid_spec = pltpu.PrefetchScalarGridSpec(
        num_scalar_prefetch=1,
        grid=(pieces // per_step,),
        in_specs=[
            pl.BlockSpec((per_step, cache_rows, HD), lambda b, s: (b, 0, 0)),
            pl.BlockSpec((per_step, cache_rows, HD), lambda b, s: (b, 1, 0)),
            pl.BlockSpec((per_step, piece_rows, HD), lambda b, s: (b, 0, 0)),
            pl.BlockSpec((per_step, piece_rows, HD), lambda b, s: (b, 1, 0)),
            pl.BlockSpec((pieces, query_rows, HD), lambda b, s: (0, 2 * piece_rows // query_rows, 0)),
        ],
        out_specs=pl.BlockSpec((count, HD), lambda b, s: (0, 0)),
        scratch_shapes=[
            pltpu.VMEM((count, 1), jnp.float32),
            pltpu.VMEM((count, HD), jnp.float32),
            pltpu.VMEM((count, 1), jnp.float32),
        ],
    )
    return pl.pallas_call(
        kernel,
        grid_spec=grid_spec,
        out_shape=jax.ShapeDtypeStruct((count, HD), jnp.bfloat16),
        compiler_params=pltpu.CompilerParams(dimension_semantics=("arbitrary",)),
    )(scalars, cache_got, cache_got, new_got, new_got, new_got)


def shards(
    residual_in,
    queries,
    new_keys,
    new_values,
    cache_keys,
    cache_values,
    cached_len,
    rope_offset,
    out_weight,
    gate_weight,
    up_weight,
    down_weight,
    expert_ids,
    gate_share,
):
    req_count = lax.axis_size("req")
    piece_count = lax.axis_size("ep")
    devices = req_count * piece_count
    experts = devices // 2
    groups, piece_rows, _ = queries.shape
    cache_rows = cache_keys.shape[1]
    top_count = expert_ids.shape[2]
    capacity = (piece_rows * top_count + experts - 1) // experts + 1
    piece_index = lax.axis_index("ep")
    new_index = piece_index * piece_rows + jnp.arange(piece_rows, dtype=jnp.int32)
    positions = rope_offset[:, None] + cached_len[:, None] + new_index[None, :]
    query_turned = rotate_rows(queries, positions, HEADS)[0]
    key_turned = rotate_rows(new_keys, positions, HEADS)[0]
    splits = piece_count // HEADS
    query_rows = piece_rows // splits

    def by_head(rows):
        return jnp.transpose(rows.reshape(rows.shape[0], HEADS, HD), (1, 0, 2))

    def both_halves(parts):
        joined = jnp.concatenate(parts, 1)
        return jnp.broadcast_to(joined[:, None], (HEADS, splits) + joined.shape[1:]).reshape(
            (piece_count,) + joined.shape[1:]
        )

    cache_sent = both_halves([by_head(cache_keys[0]), by_head(cache_values[0])])
    cache_got = lax.all_to_all(cache_sent, "ep", split_axis=0, concat_axis=0, tiled=True)
    q_parts = jnp.transpose(
        query_turned.reshape(splits, query_rows, HEADS, HD), (2, 0, 1, 3)
    ).reshape(piece_count, query_rows, HD)
    new_sent = jnp.concatenate(
        [both_halves([by_head(key_turned), by_head(new_values[0])]), q_parts], 1
    )
    new_sent, cache_got = lax.optimization_barrier((new_sent, cache_got))
    new_got = lax.all_to_all(new_sent, "ep", split_axis=0, concat_axis=0, tiled=True)
    head_out = head_attention_kernel(
        cache_got, new_got, cached_len[0], piece_index % splits, piece_rows, cache_rows
    ).reshape(piece_count, query_rows, HD)
    returned = lax.all_to_all(head_out, "ep", split_axis=0, concat_axis=0, tiled=True)
    attended = jnp.transpose(
        returned.reshape(HEADS, splits, query_rows, HD), (1, 2, 0, 3)
    ).reshape(groups, piece_rows, HEADS * HD)
    hidden = residual_in.astype(jnp.float32) + jnp.einsum(
        "gtc,cd->gtd", attended, out_weight, preferred_element_type=jnp.float32
    )
    inv_root = lax.rsqrt(jnp.mean(hidden * hidden, -1, keepdims=True) + EPS)
    normed = (hidden * inv_root).astype(jnp.bfloat16)
    width = normed.shape[-1]
    rows = normed[0]
    slots = capacity
    ids = expert_ids[0]
    matches = (ids[..., None] == jnp.arange(experts, dtype=jnp.int32)).astype(jnp.int32)
    flat_matches = matches.reshape(piece_rows * top_count, experts)
    earlier = jnp.cumsum(flat_matches, 0) - flat_matches
    slot_index = jnp.sum(earlier * flat_matches, -1).reshape(piece_rows, top_count)
    target = ids * slots + slot_index
    chosen = target[..., None] == jnp.arange(experts * slots, dtype=jnp.int32)
    picked = jnp.any(chosen, 1).reshape(piece_rows, experts, 1, slots)
    weight = jnp.sum(jnp.where(chosen, gate_share[0][..., None], 0.0), 1)
    weight = weight.reshape(piece_rows, experts, slots)
    routed = jnp.zeros((piece_rows, width), jnp.float32)
    lane = 128
    previous = None
    for low, high in ((0, 8), (8, slots)):
        chunk = high - low
        travel = (chunk, width) if chunk % 8 == 0 else (chunk * width // lane, lane)
        chunk_select = picked[..., low:high].astype(jnp.bfloat16)
        chunk_select = jnp.broadcast_to(chunk_select, (piece_rows, experts, 2, chunk))
        once = jnp.einsum(
            "teks,tw->eksw", chunk_select, rows, preferred_element_type=jnp.float32
        ).astype(jnp.bfloat16)
        sending = jnp.broadcast_to(
            once.reshape((experts, -1) + travel), (experts, 2) + travel
        ).reshape((devices,) + travel)
        if previous is not None:
            sending, previous = lax.optimization_barrier((sending, previous))
        arrived = deliver(sending)
        previous = arrived
        produced = expert_half(
            arrived.reshape(-1, width), gate_weight[0], up_weight[0], down_weight[0]
        ).reshape((devices,) + travel)
        came_back = collect(produced).reshape((experts, 2) + travel)
        joined = (
            came_back[:, 0].astype(jnp.float32) + came_back[:, 1].astype(jnp.float32)
        ).astype(jnp.bfloat16)
        share = weight[..., low:high].reshape(piece_rows, experts * chunk)
        flat = joined.reshape(experts * chunk, width)
        if chunk % 8 == 0:
            routed = routed + jnp.dot(
                share, flat.astype(jnp.float32), precision=lax.Precision.HIGHEST
            )
        else:
            high_part = share.astype(jnp.bfloat16)
            low_part = (share - high_part.astype(jnp.float32)).astype(jnp.bfloat16)
            routed = (
                routed
                + jnp.dot(high_part, flat, preferred_element_type=jnp.float32)
                + jnp.dot(low_part, flat, preferred_element_type=jnp.float32)
            )
    return (hidden + routed[None]).astype(jnp.bfloat16)


def solution(mesh):
    in_specs = (
        P("req", "ep", None),
        P("req", "ep", None),
        P("req", "ep", None),
        P("req", "ep", None),
        P("req", "ep", None),
        P("req", "ep", None),
        P("req"),
        P("req"),
        P(),
        P(("req", "ep"), None, None),
        P(("req", "ep"), None, None),
        P(("req", "ep"), None, None),
        P("req", "ep", None),
        P("req", "ep", None),
    )
    out_specs = P("req", "ep", None)
    return jax.shard_map(shards, mesh=mesh, in_specs=in_specs, out_specs=out_specs, check_vma=False)
```
